128 devices in a mesh: dp: 4 (over z), tensor: 32 (over x, y, core).
Axes of the slice: x: 4, y: 4, z: 4, core: 2. Of those that a mesh axis runs over, the one named last changes fastest.
Arguments:
- tokens: bfloat16 [4, 1536, 4096], P('dp', 'tensor'), may hold values from -6 to 6
- ln_gain: float32 [4096], replicated, may hold values from 0.1 to 1.9
- ln_bias: float32 [4096], replicated, may hold values from -3 to 3
- w_qkv: bfloat16 [4096, 3, 4096], P(None, None, 'tensor'), may hold values from -0.375 to 0.375
- w_out: bfloat16 [4096, 4096], P(None, 'tensor'), may hold values from -0.09375 to 0.09375
- layer_scale: float32 [4096], P('tensor'), may hold values from 0.5 to 4
- w_merge: bfloat16 [4, 4096, 4096], P(None, 'tensor'), may hold values from -0.046875 to 0.046875
- segment_ids: int32 [4, 1536], P('dp'), may hold values from 0 to 3, as said below
- grid_sizes: int32 [4, 3, 2], P('dp'), may hold values from 14 to 28, as said below
- owners: int32 [4, 384, 1], P('dp'), may hold values from 0 to 127; in each aligned block of 384 rows (0 to 383, 384 to 767, ..., all dimensions but the last counted through in order) at most 4 rows name the same one
Outputs:
- received: bfloat16 [4, 512, 4096], P('dp', 'tensor')
The draws below stay inside these ranges and needn't reach their ends.
Inputs may be any that keep to these rules, and one draw needn't show every extreme that they name: `grid_sizes`: both sides of every grid are even; in every batch one image has sides 28 x 28 and the others have sides of at most 18. `segment_ids`: the images of a batch lie end to end from slot 0 in order; the 5 + h w slots of image i hold i, and the padding after the last image holds 3. `owners`: within one batch no owner is named by more than 4 rows, a bound that some block reaches.
All inputs are finite; a program needn't handle non-finite values.
Results may differ from the reference program's by a relative error of at most 0.01.
Values may be sent and summed in bfloat16 or wider, within the bound.
No kernel may reach another device: no remote copies, remote signals or barrier semaphores. Data moves between devices by JAX's collectives and lax.ppermute only.
A program may use at most 128 MiB of HBM per device.

```python
import math
import jax
import jax.numpy as jnp
import numpy as np
from jax import lax

D = 4096
HEADS = 32
HEAD_DIM = 128
D_OUT = 4096
SEQ = 1536
IMGS = 3
REG = 5
GRID_MIN = 14
GRID_MAX = 28
BATCHES = 4
MERGED = 384
OWN_CAP = 4
N_DP = 4
N_TENSOR = 32
DEVICES = 128


def image_grids(key):
    folded = jax.random.fold_in(key, 11)
    big_key, side_key = jax.random.split(folded)
    big_index = jax.random.randint(big_key, (BATCHES,), 0, IMGS)
    half_sides = jax.random.randint(side_key, (BATCHES, IMGS, 2), GRID_MIN // 2, (GRID_MIN + 4) // 2 + 1)
    is_big = (jnp.arange(IMGS)[None, :] == big_index[:, None])[:, :, None]
    return jnp.where(is_big, GRID_MAX, 2 * half_sides).astype(jnp.int32)


def draw_grid_sizes(key, part):
    return image_grids(key)


def draw_segment_ids(key, part):
    grids = image_grids(key)
    lengths = REG + grids[:, :, 0] * grids[:, :, 1]
    ends = jnp.cumsum(lengths, axis=1)
    position = jnp.arange(SEQ, dtype=jnp.int32)
    return jnp.sum((position[None, :, None] >= ends[:, None, :]).astype(jnp.int32), axis=2).astype(jnp.int32)


def draw_w_qkv(key, part):
    folded = jax.random.fold_in(key, 23)
    base_key = jax.random.fold_in(folded, 0)
    base = jax.random.truncated_normal(base_key, -4.0, 4.0, (D, 3, D), jnp.float32) * D ** (-0.5)
    return base.astype(jnp.bfloat16)


def steps_of(key, dims, pieces, smallest, largest):
    gain = 1.0
    for dim, parts in pieces:
        steps = jax.random.uniform(jax.random.fold_in(jax.random.fold_in(key, 6), dim), (parts,), jnp.float32, smallest / len(pieces), largest / len(pieces))
        gain = gain * jnp.repeat(jnp.exp(steps), dims[dim] // parts).reshape((-1,) + (1,) * (len(dims) - 1 - dim))
    return gain


def routed_block(rng, own, number, rows, number_of, top, bound, skew):
    order = jax.random.permutation(rng, number_of)
    packed, ordinary = load_shares(number_of, rows * top, bound, skew, True), load_shares(number_of, rows * top, bound, skew, False)
    places = jnp.arange(number_of)

    def named(sizes, rotation):
        used = int((sizes > 0).sum())
        fixed = max(1, used // 4)
        passed = fixed + (places - fixed + rotation * (used - fixed)) % max(1, number_of - fixed)
        return jnp.zeros((number_of,), jnp.int32).at[order[jnp.where(places < fixed, places, passed)]].set(jnp.asarray(sizes, jnp.int32))

    sizes = jnp.where(number % 4 == 0, named(packed, number // 4), named(ordinary, number - number // 4 - 1))
    mixed = jax.random.permutation(jax.random.fold_in(own, 3), number_of)
    donor, taker = mixed[0:number_of // 2 * 2:2], mixed[1:number_of // 2 * 2:2]
    slack = jnp.minimum(sizes[donor] - 1, bound - sizes[taker]) // 2
    slack = jnp.where((donor == order[0]) | (taker == order[0]) | (sizes[taker] == 0), 0, jnp.maximum(slack, 0))
    passed = jax.random.randint(jax.random.fold_in(own, 4), (number_of // 2,), 0, 1 << 20) % (slack + 1)
    sizes = sizes.at[donor].add(-passed).at[taker].add(passed)
    members = jnp.searchsorted(jnp.cumsum(sizes), jnp.arange(rows * top), side="right").astype(jnp.int32)
    listing = members.reshape(top, rows).T
    listing = listing[jax.random.permutation(jax.random.fold_in(own, 1), rows)]
    rotation = jax.random.randint(jax.random.fold_in(own, 2), (rows, 1), 0, top)
    return jnp.take_along_axis(listing, (jnp.arange(top)[None, :] + rotation) % top, axis=1)


def load_shares(number_of, total, most, slope, full):
    loads = [(1 << 20) // math.isqrt(rank ** slope) + 1 for rank in range(1, number_of + 1)]
    largest = most if full else min(most, max(-(-total // number_of), total * loads[0] // sum(loads)))
    least = 1 if total - largest >= number_of - 1 else 0
    given, rest = [largest] + [least] * (number_of - 1), total - largest - least * (number_of - 1)
    while rest > 0:
        candidates = [i for i in range(1, number_of) if given[i] < largest] or [i for i in range(1, number_of) if given[i] < most]
        whole, remaining = sum([loads[i] for i in candidates]), rest
        for i in candidates:
            extra = min(most - given[i], max(1, remaining * loads[i] // whole), rest)
            given[i] = given[i] + extra
            rest = rest - extra
    return np.array(given)


def normal_values(own_key, shape, scale, reach, cuts=(), held_as=jnp.bfloat16):
    factor_of = steps_of(own_key, shape, cuts, -0.22, 0.18) if cuts else 1.0
    values = jax.random.normal(own_key, shape, jnp.float32) * scale * factor_of
    return jnp.minimum(jnp.maximum(values, -reach), reach).astype(held_as)


def setup_inputs(seed: int = 0) -> dict:
    key_of = jax.random.split(jax.random.key(seed), 11)
    tokens = normal_values(key_of[0], (BATCHES, SEQ, D), 1.0, 6.0, ((0, 4), (1, 32)))
    ln_gain = jnp.clip(1.0 + 0.18 * jax.random.normal(key_of[1], (D,), jnp.float32), 0.1, 1.9)
    ln_bias = normal_values(key_of[2], (D,), 0.5, 3.0, (), jnp.float32)
    w_qkv = draw_w_qkv(jax.random.fold_in(key_of[10], 71), 0)
    w_out = normal_values(key_of[4], (D, D), D ** -0.5, 0.09375, ((1, 32),))
    layer_scale = jnp.clip(jnp.exp(math.log(4.0) - 2.0794415 * jax.random.uniform(key_of[5], (D,), jnp.float32) ** steps_of(key_of[5], (D,), ((0, 32),), -0.2, 0.2)), 0.5, 4.0)
    w_merge = normal_values(key_of[6], (4, D, D_OUT), (4 * D) ** -0.5, 0.046875, ((1, 32),))
    segment_ids = draw_segment_ids(jax.random.fold_in(key_of[10], 71), 0)
    grid_sizes = draw_grid_sizes(jax.random.fold_in(key_of[10], 71), 0)
    owners_keys = jax.random.split(jax.random.fold_in(key_of[9], 1), BATCHES * MERGED // MERGED)
    owners_turns = jax.random.permutation(jax.random.fold_in(key_of[9], 3), BATCHES * MERGED // MERGED)
    owners = jax.vmap(lambda own, number: routed_block(jax.random.fold_in(key_of[9], 2), own, number, MERGED, DEVICES, 1, OWN_CAP, 2))(owners_keys, owners_turns).reshape((BATCHES, MERGED, 1))
    return {"tokens": tokens, "ln_gain": ln_gain, "ln_bias": ln_bias, "w_qkv": w_qkv, "w_out": w_out, "layer_scale": layer_scale, "w_merge": w_merge, "segment_ids": segment_ids, "grid_sizes": grid_sizes, "owners": owners}


norm_eps = 1e-06

def layer_norm(row_data, gain_vec, shift_vec):
    values = row_data.astype(jnp.float32)
    center = values - lax.optimization_barrier(jnp.mean(values, axis=-1, keepdims=True))
    spread = lax.optimization_barrier(jnp.mean(center * center, axis=-1, keepdims=True))
    return (center * lax.rsqrt(spread + norm_eps) * gain_vec + shift_vec).astype(jnp.bfloat16)

def image_layout(grid_row):
    heights = grid_row[:, 0]
    widths = grid_row[:, 1]
    lengths = REG + heights * widths
    starts = jnp.cumsum(lengths) - lengths
    counts = heights // 2 * (widths // 2)
    merged_end = jnp.cumsum(counts)
    return (heights, widths, starts, merged_end - counts, merged_end)

def pick_rows(onehot, lookup):
    return lax.optimization_barrier(jnp.sum(onehot * lookup[None, :], axis=1))

def rope_tables(seg_row, grid_row, seq_len):
    heights, widths, starts, first_merged, last_merged = image_layout(grid_row)
    position = jnp.arange(seq_len, dtype=jnp.int32)
    image_ids = jnp.arange(IMGS, dtype=jnp.int32)
    onehot = (seg_row[:, None] == image_ids[None, :]).astype(jnp.int32)
    is_image = lax.optimization_barrier(jnp.sum(onehot, axis=1)) > 0
    in_image = position - pick_rows(onehot, starts) - REG
    is_patch = is_image & (in_image >= 0)
    row_width = jnp.maximum(pick_rows(onehot, widths), 1)
    col_height = jnp.maximum(pick_rows(onehot, heights), 1)
    clipped = jnp.maximum(in_image, 0)
    coord_y = 2.0 * ((clipped // row_width).astype(jnp.float32) + 0.5) / col_height.astype(jnp.float32) - 1.0
    coord_x = 2.0 * ((clipped % row_width).astype(jnp.float32) + 0.5) / row_width.astype(jnp.float32) - 1.0
    quarter = HEAD_DIM // 4
    pair_ids = jnp.arange(HEAD_DIM // 2, dtype=jnp.int32)
    omegas = 100.0 ** ((pair_ids % quarter).astype(jnp.float32) / quarter)
    coord_all = jnp.where(pair_ids[None, :] < quarter, coord_y[:, None], coord_x[:, None])
    angles = jnp.where(is_patch[:, None], jnp.pi * omegas[None, :] * coord_all, 0.0)
    return (jnp.cos(angles), jnp.sin(angles))

def rotate(values, cos_rows, sin_rows):
    half_dim = values.shape[-1] // 2
    first_half = values[..., :half_dim]
    second_half = values[..., half_dim:]
    return jnp.concatenate([first_half * cos_rows - second_half * sin_rows, second_half * cos_rows + first_half * sin_rows], axis=-1)

def merge_sources(grid_row, merged_rows):
    heights, widths, starts, first_merged, last_merged = image_layout(grid_row)
    row_ids = jnp.arange(merged_rows, dtype=jnp.int32)
    onehot = ((row_ids[:, None] >= first_merged[None, :]) & (row_ids[:, None] < last_merged[None, :])).astype(jnp.int32)
    is_valid = lax.optimization_barrier(jnp.sum(onehot, axis=1)) > 0
    row_width = pick_rows(onehot, widths)
    half_width = jnp.maximum(row_width // 2, 1)
    in_image = row_ids - pick_rows(onehot, first_merged)
    corner = pick_rows(onehot, starts) + REG + 2 * (in_image // half_width) * row_width + 2 * (in_image % half_width)
    offsets = jnp.stack([jnp.zeros_like(row_width), jnp.ones_like(row_width), row_width, row_width + 1], axis=1)
    sources = jnp.where(is_valid[:, None], corner[:, None] + offsets, 0)
    return (sources.astype(jnp.int32), is_valid)

def attend(query_rows, query_seg, key_rows, value_rows, key_seg):
    scores = lax.dot_general(query_rows, key_rows, (((1,), (1,)), ((), ())), preferred_element_type=jnp.float32) * HEAD_DIM ** (-0.5)
    scores = jnp.where(query_seg[:, None] == key_seg[None, :], scores, -jnp.inf)
    shifted = jnp.exp(scores - lax.optimization_barrier(jnp.max(scores, axis=1, keepdims=True)))
    weights = (shifted / lax.optimization_barrier(jnp.sum(shifted, axis=1, keepdims=True))).astype(jnp.bfloat16)
    return jnp.dot(weights, value_rows, preferred_element_type=jnp.float32).astype(jnp.bfloat16)

def owner_ranks(owner_row, device_count):
    onehot = (owner_row[:, None] == jnp.arange(device_count, dtype=jnp.int32)[None, :]).astype(jnp.int32)
    before = jnp.cumsum(onehot, axis=0) - onehot
    return lax.optimization_barrier(jnp.sum(before * onehot, axis=1))

def batch_forward(x_rows, seg_row, grid_row, ln_gain, ln_bias, w_qkv, w_out, layer_scale, w_merge):
    seq_len = x_rows.shape[0]
    normed = layer_norm(x_rows, ln_gain, ln_bias)
    qkv_rows = jnp.dot(normed, w_qkv.reshape(D, 3 * D), preferred_element_type=jnp.float32)
    cos_table, sin_table = rope_tables(seg_row, grid_row, seq_len)
    cos_rows = cos_table[:, None, :]
    sin_rows = sin_table[:, None, :]
    query_all = rotate(qkv_rows[:, :D].reshape(seq_len, HEADS, HEAD_DIM), cos_rows, sin_rows).astype(jnp.bfloat16)
    key_all = rotate(qkv_rows[:, D:2 * D].reshape(seq_len, HEADS, HEAD_DIM), cos_rows, sin_rows).astype(jnp.bfloat16)
    value_all = qkv_rows[:, 2 * D:].reshape(seq_len, HEADS, HEAD_DIM).astype(jnp.bfloat16)

    def per_head(inputs):
        return attend(inputs[0], seg_row, inputs[1], inputs[2], seg_row)
    per_heads = lax.map(per_head, (query_all.transpose(1, 0, 2), key_all.transpose(1, 0, 2), value_all.transpose(1, 0, 2)))
    context = per_heads.transpose(1, 0, 2).reshape(seq_len, D)
    mixed = jnp.dot(context, w_out, preferred_element_type=jnp.float32)
    hidden = (x_rows.astype(jnp.float32) + layer_scale * mixed).astype(jnp.bfloat16)
    merged_rows = seq_len // 4
    sources, is_valid = merge_sources(grid_row, merged_rows)
    merged = jnp.where(is_valid[:, None, None], hidden[sources], jnp.zeros((), jnp.bfloat16))
    col_width = D // N_TENSOR

    def add_group(running, group_index):
        offset = (group_index * col_width).astype(jnp.int32)
        columns = lax.dynamic_slice_in_dim(merged, offset, col_width, 2).reshape(merged_rows, 4 * col_width)
        weight_rows = lax.dynamic_slice_in_dim(w_merge, offset, col_width, 1).reshape(4 * col_width, D_OUT)
        term_part = jnp.dot(columns, weight_rows, preferred_element_type=jnp.float32)
        return (running + lax.optimization_barrier(term_part.astype(jnp.bfloat16)).astype(jnp.float32), None)
    total, unused = lax.scan(add_group, jnp.zeros((merged_rows, D_OUT), jnp.float32), jnp.arange(N_TENSOR, dtype=jnp.int32))
    return total.astype(jnp.bfloat16)

def reference(tokens, ln_gain, ln_bias, w_qkv, w_out, layer_scale, w_merge, segment_ids, grid_sizes, owners):
    outputs = []
    slot_lists = []
    for batch_index in range(BATCHES):
        outputs.append(batch_forward(tokens[batch_index], segment_ids[batch_index], grid_sizes[batch_index], ln_gain, ln_bias, w_qkv, w_out, layer_scale, w_merge))
        owner_row = owners[batch_index, :, 0]
        ranks = owner_ranks(owner_row, DEVICES)
        slot_lists.append(owner_row * (N_DP * OWN_CAP) + batch_index * OWN_CAP + ranks)
    rows_all = jnp.concatenate(outputs, axis=0)
    slots = jnp.concatenate(slot_lists, axis=0).astype(jnp.int32)
    placed = jnp.zeros((DEVICES * N_DP * OWN_CAP, D_OUT), jnp.bfloat16).at[slots].set(rows_all)
    return placed.reshape(BATCHES, N_TENSOR * N_DP * OWN_CAP, D_OUT)
```

```python
import jax
import jax.numpy as jnp
from jax import lax
from jax.sharding import Mesh
from jax.sharding import PartitionSpec as P

HEAD_DIM = 128
IMGS = 3
REG = 5


norm_eps = 1e-06


def layer_norm(row_data, gain_vec, shift_vec):
    values = row_data.astype(jnp.float32)
    center = values - jnp.mean(values, axis=-1, keepdims=True)
    spread = jnp.mean(center * center, axis=-1, keepdims=True)
    return (center * lax.rsqrt(spread + norm_eps) * gain_vec + shift_vec).astype(jnp.bfloat16)


def image_layout(grid_row):
    heights = grid_row[:, 0]
    widths = grid_row[:, 1]
    lengths = REG + heights * widths
    starts = jnp.cumsum(lengths) - lengths
    counts = heights // 2 * (widths // 2)
    merged_end = jnp.cumsum(counts)
    return (heights, widths, starts, merged_end - counts, merged_end)


def pick_rows(onehot, lookup):
    return jnp.sum(onehot * lookup[None, :], axis=1)


def rope_tables(seg_at, position, grid_row):
    heights, widths, starts, first_merged, last_merged = image_layout(grid_row)
    image_ids = jnp.arange(IMGS, dtype=jnp.int32)
    onehot = (seg_at[:, None] == image_ids[None, :]).astype(jnp.int32)
    is_image = jnp.sum(onehot, axis=1) > 0
    in_image = position - pick_rows(onehot, starts) - REG
    is_patch = is_image & (in_image >= 0)
    row_width = jnp.maximum(pick_rows(onehot, widths), 1)
    col_height = jnp.maximum(pick_rows(onehot, heights), 1)
    clipped = jnp.maximum(in_image, 0)
    coord_y = (
        2.0 * ((clipped // row_width).astype(jnp.float32) + 0.5) / col_height.astype(jnp.float32)
        - 1.0
    )
    coord_x = (
        2.0 * ((clipped % row_width).astype(jnp.float32) + 0.5) / row_width.astype(jnp.float32)
        - 1.0
    )
    quarter = HEAD_DIM // 4
    pair_ids = jnp.arange(HEAD_DIM // 2, dtype=jnp.int32)
    omegas = 100.0 ** ((pair_ids % quarter).astype(jnp.float32) / quarter)
    coord_all = jnp.where(pair_ids[None, :] < quarter, coord_y[:, None], coord_x[:, None])
    angles = jnp.where(is_patch[:, None], jnp.pi * omegas[None, :] * coord_all, 0.0)
    return (jnp.cos(angles), jnp.sin(angles))


def rotate(values, cos_rows, sin_rows):
    half_dim = values.shape[-1] // 2
    first_half = values[..., :half_dim]
    second_half = values[..., half_dim:]
    return jnp.concatenate(
        [
            first_half * cos_rows - second_half * sin_rows,
            second_half * cos_rows + first_half * sin_rows,
        ],
        axis=-1,
    )


def merge_sources(grid_row, merged_rows):
    heights, widths, starts, first_merged, last_merged = image_layout(grid_row)
    row_ids = jnp.arange(merged_rows, dtype=jnp.int32)
    onehot = (
        (row_ids[:, None] >= first_merged[None, :]) & (row_ids[:, None] < last_merged[None, :])
    ).astype(jnp.int32)
    is_valid = jnp.sum(onehot, axis=1) > 0
    row_width = pick_rows(onehot, widths)
    half_width = jnp.maximum(row_width // 2, 1)
    in_image = row_ids - pick_rows(onehot, first_merged)
    corner = (
        pick_rows(onehot, starts)
        + REG
        + 2 * (in_image // half_width) * row_width
        + 2 * (in_image % half_width)
    )
    offsets = jnp.stack(
        [jnp.zeros_like(row_width), jnp.ones_like(row_width), row_width, row_width + 1], axis=1
    )
    sources = jnp.where(is_valid[:, None], corner[:, None] + offsets, 0)
    return (sources, is_valid)


def attend(query_rows, query_seg, key_rows, value_rows, key_seg):
    scores = lax.dot_general(
        query_rows, key_rows, (((1,), (1,)), ((), ())), preferred_element_type=jnp.float32
    ) * HEAD_DIM ** (-0.5)
    scores = jnp.where(query_seg[:, None] == key_seg[None, :], scores, -jnp.inf)
    shifted = jnp.exp(scores - jnp.max(scores, axis=1, keepdims=True))
    weights = (shifted / jnp.sum(shifted, axis=1, keepdims=True)).astype(jnp.bfloat16)
    return jnp.dot(weights, value_rows, preferred_element_type=jnp.float32).astype(jnp.bfloat16)


def owner_ranks(owner_row):
    rows = owner_row.shape[0]
    same = owner_row[:, None] == owner_row[None, :]
    earlier = jnp.arange(rows)[None, :] < jnp.arange(rows)[:, None]
    return jnp.sum((same & earlier).astype(jnp.int32), axis=1)


def local(
    tokens, ln_gain, ln_bias, w_qkv, w_out, layer_scale, w_merge, segment_ids, grid_sizes, owners
):
    chips = lax.axis_size("xy")
    batch_count = lax.axis_size("dp")
    chip = lax.axis_index("xy")
    core = lax.axis_index("core")
    seg_row = segment_ids[0]
    grid_row = grid_sizes[0]
    owner_row = owners[0, :, 0]
    seq_len = seg_row.shape[0]
    block = tokens.shape[1]
    model_width = tokens.shape[2]
    col_width = layer_scale.shape[0]
    half_rows = chips * block
    merged_rows = seq_len // 4
    tensor_count = 2 * chips
    own_cap = 4
    out_width = w_merge.shape[2]

    x_rows = lax.all_gather(tokens[0], "xy", axis=0, tiled=True)
    w_pair = lax.all_gather(w_qkv, "core", axis=0, tiled=False)
    wo_pair = lax.all_gather(w_out, "core", axis=0, tiled=False)
    ls_pair = lax.all_gather(layer_scale, "core", axis=0, tiled=True)

    position = (
        (2 * jnp.arange(chips, dtype=jnp.int32) + core)[:, None] * block
        + jnp.arange(block, dtype=jnp.int32)[None, :]
    ).reshape(half_rows)
    seg_mine = seg_row.reshape(chips, 2, block)
    seg_both = jnp.transpose(seg_mine, (1, 0, 2)).reshape(2, half_rows)
    seg_here = seg_both[core]
    cos_t, sin_t = rope_tables(seg_here, position, grid_row)

    normed = layer_norm(x_rows, ln_gain, ln_bias)
    qkv_weight = jnp.transpose(w_pair, (1, 2, 0, 3)).reshape(model_width, 3 * 2 * HEAD_DIM)
    product = jnp.dot(normed, qkv_weight, preferred_element_type=jnp.float32).reshape(
        half_rows, 3, 2, HEAD_DIM
    )
    cos_rows = cos_t[:, None, :]
    sin_rows = sin_t[:, None, :]
    q_here = rotate(product[:, 0], cos_rows, sin_rows).astype(jnp.bfloat16)
    k_here = rotate(product[:, 1], cos_rows, sin_rows).astype(jnp.bfloat16)
    v_here = product[:, 2].astype(jnp.bfloat16)
    kv_here = jnp.stack([k_here, v_here], axis=1)
    kv_all = lax.all_gather(kv_here, "core", axis=0, tiled=True)
    key_all = kv_all[:, 0]
    value_all = kv_all[:, 1]
    seg_keys = seg_both.reshape(2 * half_rows)

    def one_head(h):
        return attend(q_here[:, h], seg_here, key_all[:, h], value_all[:, h], seg_keys)

    context_here = jnp.stack([one_head(0), one_head(1)], axis=1).reshape(
        half_rows, 2 * HEAD_DIM
    )
    context_g = lax.all_gather(context_here, "xy", axis=0, tiled=False)
    context = jnp.transpose(context_g, (1, 0, 2)).reshape(half_rows, model_width)
    wo_cols = jnp.transpose(wo_pair, (1, 0, 2)).reshape(model_width, 2 * col_width)
    mixed = jnp.dot(context, wo_cols, preferred_element_type=jnp.float32)
    x_cols = lax.dynamic_slice_in_dim(x_rows, chip * 2 * col_width, 2 * col_width, 1)
    hidden_here = (x_cols.astype(jnp.float32) + ls_pair * mixed).astype(jnp.bfloat16)
    hidden_sw = lax.all_to_all(
        hidden_here.reshape(half_rows, 2, col_width), "core", split_axis=1, concat_axis=1
    )
    hidden = jnp.transpose(
        hidden_sw.reshape(chips, block, 2, col_width), (0, 2, 1, 3)
    ).reshape(seq_len, col_width)

    sources, is_valid = merge_sources(grid_row, merged_rows)
    merged = jnp.where(
        is_valid[:, None, None], hidden[sources], jnp.zeros((), jnp.bfloat16)
    ).reshape(merged_rows, 4 * col_width)
    merge_weight = w_merge.reshape(4 * col_width, out_width)
    ranks = owner_ranks(owner_row)
    owner_dp = owner_row // tensor_count
    owner_t = owner_row % tensor_count
    slot_block = (owner_t % 2) * chips + owner_t // 2
    slot_keys = slot_block * (batch_count * own_cap) + owner_dp * own_cap + ranks
    slot_ids = jnp.arange(tensor_count * batch_count * own_cap, dtype=jnp.int32)
    placing = (slot_ids[:, None] == slot_keys[None, :]).astype(jnp.bfloat16)
    by_owner = jnp.dot(placing, merged, preferred_element_type=jnp.float32).astype(jnp.bfloat16)
    group_part = jnp.dot(by_owner, merge_weight, preferred_element_type=jnp.float32).astype(
        jnp.bfloat16
    )
    part32 = group_part.astype(jnp.float32)
    half = lax.psum_scatter(part32, "core", scatter_dimension=0, tiled=True)
    mine = lax.psum_scatter(half, "xy", scatter_dimension=0, tiled=True)
    outgoing = mine.astype(jnp.bfloat16).reshape(batch_count, own_cap, out_width)
    incoming = lax.all_to_all(outgoing, "dp", split_axis=0, concat_axis=0, tiled=True)
    return incoming.reshape(1, batch_count * own_cap, out_width)


def solution(mesh):
    devices = mesh.devices.reshape(mesh.shape["dp"], -1, 2)
    mesh3 = Mesh(devices, ("dp", "xy", "core"))
    tp = ("xy", "core")
    in_specs = (
        P("dp", tp, None),
        P(),
        P(),
        P(None, None, tp),
        P(None, tp),
        P(tp),
        P(None, tp, None),
        P("dp", None),
        P("dp", None, None),
        P("dp", None, None),
    )
    out_specs = P("dp", tp, None)
    return jax.shard_map(local, mesh=mesh3, in_specs=in_specs, out_specs=out_specs, check_vma=False)
```

```python
import jax
import jax.numpy as jnp
from jax import lax
from jax.sharding import Mesh
from jax.sharding import PartitionSpec as P

HEAD_DIM = 128
IMGS = 3
REG = 5


norm_eps = 1e-06


def layer_norm(row_data, gain_vec, shift_vec):
    values = row_data.astype(jnp.float32)
    center = values - jnp.mean(values, axis=-1, keepdims=True)
    spread = jnp.mean(center * center, axis=-1, keepdims=True)
    return (center * lax.rsqrt(spread + norm_eps) * gain_vec + shift_vec).astype(jnp.bfloat16)


def image_layout(grid_row):
    heights = grid_row[:, 0]
    widths = grid_row[:, 1]
    lengths = REG + heights * widths
    starts = jnp.cumsum(lengths) - lengths
    counts = heights // 2 * (widths // 2)
    merged_end = jnp.cumsum(counts)
    return (heights, widths, starts, merged_end - counts, merged_end)


def pick_rows(onehot, lookup):
    return jnp.sum(onehot * lookup[None, :], axis=1)


def rope_tables(seg_at, position, grid_row):
    heights, widths, starts, first_merged, last_merged = image_layout(grid_row)
    image_ids = jnp.arange(IMGS, dtype=jnp.int32)
    onehot = (seg_at[:, None] == image_ids[None, :]).astype(jnp.int32)
    is_image = jnp.sum(onehot, axis=1) > 0
    in_image = position - pick_rows(onehot, starts) - REG
    is_patch = is_image & (in_image >= 0)
    row_width = jnp.maximum(pick_rows(onehot, widths), 1)
    col_height = jnp.maximum(pick_rows(onehot, heights), 1)
    clipped = jnp.maximum(in_image, 0)
    coord_y = (
        2.0 * ((clipped // row_width).astype(jnp.float32) + 0.5) / col_height.astype(jnp.float32)
        - 1.0
    )
    coord_x = (
        2.0 * ((clipped % row_width).astype(jnp.float32) + 0.5) / row_width.astype(jnp.float32)
        - 1.0
    )
    quarter = HEAD_DIM // 4
    pair_ids = jnp.arange(HEAD_DIM // 2, dtype=jnp.int32)
    omegas = 100.0 ** ((pair_ids % quarter).astype(jnp.float32) / quarter)
    coord_all = jnp.where(pair_ids[None, :] < quarter, coord_y[:, None], coord_x[:, None])
    angles = jnp.where(is_patch[:, None], jnp.pi * omegas[None, :] * coord_all, 0.0)
    return (jnp.cos(angles), jnp.sin(angles))


def rotate(values, cos_rows, sin_rows):
    half_dim = values.shape[-1] // 2
    first_half = values[..., :half_dim]
    second_half = values[..., half_dim:]
    return jnp.concatenate(
        [
            first_half * cos_rows - second_half * sin_rows,
            second_half * cos_rows + first_half * sin_rows,
        ],
        axis=-1,
    )


def merge_sources(grid_row, merged_rows):
    heights, widths, starts, first_merged, last_merged = image_layout(grid_row)
    row_ids = jnp.arange(merged_rows, dtype=jnp.int32)
    onehot = (
        (row_ids[:, None] >= first_merged[None, :]) & (row_ids[:, None] < last_merged[None, :])
    ).astype(jnp.int32)
    is_valid = jnp.sum(onehot, axis=1) > 0
    row_width = pick_rows(onehot, widths)
    half_width = jnp.maximum(row_width // 2, 1)
    in_image = row_ids - pick_rows(onehot, first_merged)
    corner = (
        pick_rows(onehot, starts)
        + REG
        + 2 * (in_image // half_width) * row_width
        + 2 * (in_image % half_width)
    )
    offsets = jnp.stack(
        [jnp.zeros_like(row_width), jnp.ones_like(row_width), row_width, row_width + 1], axis=1
    )
    sources = jnp.where(is_valid[:, None], corner[:, None] + offsets, 0)
    return (sources, is_valid)


def attend(query_rows, query_seg, key_rows, value_rows, key_seg):
    scores = lax.dot_general(
        query_rows, key_rows, (((1,), (1,)), ((), ())), preferred_element_type=jnp.float32
    ) * HEAD_DIM ** (-0.5)
    scores = jnp.where(query_seg[:, None] == key_seg[None, :], scores, -jnp.inf)
    shifted = jnp.exp(scores - jnp.max(scores, axis=1, keepdims=True))
    weights = (shifted / jnp.sum(shifted, axis=1, keepdims=True)).astype(jnp.bfloat16)
    return jnp.dot(weights, value_rows, preferred_element_type=jnp.float32).astype(jnp.bfloat16)


def owner_ranks(owner_row):
    rows = owner_row.shape[0]
    same = owner_row[:, None] == owner_row[None, :]
    earlier = jnp.arange(rows)[None, :] < jnp.arange(rows)[:, None]
    return jnp.sum((same & earlier).astype(jnp.int32), axis=1)


def chip_shift(v, along, step, side):
    perm = []
    for src in range(side * side):
        x, y = src // side, src % side
        if along == 0:
            dst = ((x + step) % side) * side + y
        else:
            dst = x * side + (y + step) % side
        perm.append((src, dst))
    return lax.ppermute(v, "xy", perm)


def ring4(piece, along, side, cut):
    from_left = chip_shift(piece, along, 1, side)
    from_right = chip_shift(piece, along, -1, side)
    size = piece.shape[cut] // 2
    far_a = chip_shift(lax.slice_in_dim(from_left, 0, size, axis=cut), along, 1, side)
    far_b = chip_shift(lax.slice_in_dim(from_right, size, 2 * size, axis=cut), along, -1, side)
    far = jnp.concatenate([far_a, far_b], axis=cut)
    return jnp.stack([piece, from_right, far, from_left], axis=0)


def gather_torus(v, side, cut):
    size = v.shape[cut] // 2
    first = lax.slice_in_dim(v, 0, size, axis=cut)
    second = lax.slice_in_dim(v, size, 2 * size, axis=cut)
    row_x = ring4(first, 0, side, cut)
    col_y = ring4(second, 1, side, cut)
    first_all = ring4(row_x, 1, side, 0)
    second_all = ring4(col_y, 0, side, 0)
    first_all = jnp.swapaxes(first_all, 0, 1)
    return jnp.concatenate([first_all, second_all], axis=cut + 2)


def swap_core(v):
    return lax.ppermute(v, "core", [(0, 1), (1, 0)])


def to_absolute(v, cx, cy):
    return jnp.roll(jnp.roll(v, cx, axis=0), cy, axis=1)


def local(
    tokens, ln_gain, ln_bias, w_qkv, w_out, layer_scale, w_merge, segment_ids, grid_sizes, owners
):
    chips = lax.axis_size("xy")
    side = 4
    batch_count = lax.axis_size("dp")
    chip = lax.axis_index("xy")
    core = lax.axis_index("core")
    cx = chip // side
    cy = chip % side
    seg_row = segment_ids[0]
    grid_row = grid_sizes[0]
    owner_row = owners[0, :, 0]
    seq_len = seg_row.shape[0]
    block = tokens.shape[1]
    model_width = tokens.shape[2]
    col_width = layer_scale.shape[0]
    half_rows = chips * block
    merged_rows = seq_len // 4
    tensor_count = 2 * chips
    own_cap = 4
    out_width = w_merge.shape[2]

    x_rel = gather_torus(tokens[0], side, 1)
    w_partner = swap_core(w_qkv)
    wo_partner = swap_core(w_out)
    ls_partner = swap_core(layer_scale)

    offs = jnp.arange(side, dtype=jnp.int32)
    chip_of = ((cx + offs)[:, None] % side) * side + (cy + offs)[None, :] % side
    within = jnp.arange(block, dtype=jnp.int32)
    pos_mine = ((2 * chip_of + core)[:, :, None] * block + within).reshape(half_rows)
    pos_other = ((2 * chip_of + 1 - core)[:, :, None] * block + within).reshape(half_rows)
    seg_mine = seg_row[pos_mine]
    seg_other = seg_row[pos_other]
    cos_t, sin_t = rope_tables(seg_mine, pos_mine, grid_row)

    x_rows = x_rel.reshape(half_rows, model_width)
    normed = layer_norm(x_rows, ln_gain, ln_bias)
    w_both = jnp.stack([w_qkv, w_partner], axis=2)
    qkv_weight = w_both.reshape(model_width, 3 * 2 * HEAD_DIM)
    product = jnp.dot(normed, qkv_weight, preferred_element_type=jnp.float32).reshape(
        half_rows, 3, 2, HEAD_DIM
    )
    cos_rows = cos_t[:, None, :]
    sin_rows = sin_t[:, None, :]
    q_here = rotate(product[:, 0], cos_rows, sin_rows).astype(jnp.bfloat16)
    k_here = rotate(product[:, 1], cos_rows, sin_rows).astype(jnp.bfloat16)
    v_here = product[:, 2].astype(jnp.bfloat16)
    kv_here = jnp.stack([k_here, v_here], axis=1)
    kv_other = swap_core(kv_here)[:, :, ::-1]
    kv_all = jnp.concatenate([kv_here, kv_other], axis=0)
    key_all = kv_all[:, 0]
    value_all = kv_all[:, 1]
    seg_keys = jnp.concatenate([seg_mine, seg_other], axis=0)

    def one_head(h):
        return attend(q_here[:, h], seg_mine, key_all[:, h], value_all[:, h], seg_keys)

    context_rel = jnp.stack([one_head(0), one_head(1)], axis=1).reshape(
        side, side, block, 2 * HEAD_DIM
    )
    context_abs = to_absolute(context_rel, cx, cy).reshape(half_rows, 2 * HEAD_DIM)
    context_g = gather_torus(context_abs, side, 0)
    context = jnp.transpose(context_g, (2, 0, 1, 3)).reshape(half_rows, model_width)
    head_of = jnp.stack([2 * chip_of + core, 2 * chip_of + 1 - core], axis=2)
    feature_rows = (head_of[..., None] * HEAD_DIM + jnp.arange(HEAD_DIM, dtype=jnp.int32)).reshape(
        model_width
    )
    wo_both = jnp.concatenate([w_out, wo_partner], axis=1)
    wo_rows = jnp.take(wo_both, feature_rows, axis=0)
    mixed = jnp.dot(context, wo_rows, preferred_element_type=jnp.float32)
    group_mine = 2 * chip + core
    group_other = 2 * chip + 1 - core
    x_mine = lax.dynamic_slice_in_dim(x_rel, group_mine * col_width, col_width, 3)
    x_other = lax.dynamic_slice_in_dim(x_rel, group_other * col_width, col_width, 3)
    x_cols = to_absolute(jnp.concatenate([x_mine, x_other], axis=3), cx, cy).reshape(
        half_rows, 2 * col_width
    )
    ls_both = jnp.concatenate([layer_scale, ls_partner], axis=0)
    hidden_here = (x_cols.astype(jnp.float32) + ls_both * mixed).astype(jnp.bfloat16)
    hidden_recv = swap_core(hidden_here[:, col_width:])
    hidden = jnp.concatenate([hidden_here[:, :col_width], hidden_recv], axis=0)

    sources, is_valid = merge_sources(grid_row, merged_rows)
    src_block = sources // block
    src_index = (
        (src_block % 2 != core).astype(jnp.int32) * half_rows
        + (src_block // 2) * block
        + sources % block
    )
    merged = jnp.where(
        is_valid[:, None, None], hidden[src_index], jnp.zeros((), jnp.bfloat16)
    ).reshape(merged_rows, 4 * col_width)
    merge_weight = w_merge.reshape(4 * col_width, out_width)
    ranks = owner_ranks(owner_row)
    owner_dp = owner_row // tensor_count
    owner_t = owner_row % tensor_count
    slot_keys = owner_t * (batch_count * own_cap) + owner_dp * own_cap + ranks
    slot_ids = jnp.arange(tensor_count * batch_count * own_cap, dtype=jnp.int32)
    placing = (slot_ids[:, None] == slot_keys[None, :]).astype(jnp.bfloat16)
    by_owner = jnp.dot(placing, merged, preferred_element_type=jnp.float32).astype(jnp.bfloat16)
    group_part = jnp.dot(by_owner, merge_weight, preferred_element_type=jnp.float32).astype(
        jnp.bfloat16
    )
    part32 = group_part.astype(jnp.float32)
    mine = lax.psum_scatter(part32, ("xy", "core"), scatter_dimension=0, tiled=True)
    outgoing = mine.astype(jnp.bfloat16).reshape(batch_count, own_cap, out_width)
    incoming = lax.all_to_all(outgoing, "dp", split_axis=0, concat_axis=0, tiled=True)
    return incoming.reshape(1, batch_count * own_cap, out_width)


def solution(mesh):
    devices = mesh.devices.reshape(mesh.shape["dp"], -1, 2)
    mesh3 = Mesh(devices, ("dp", "xy", "core"))
    tp = ("xy", "core")
    in_specs = (
        P("dp", tp, None),
        P(),
        P(),
        P(None, None, tp),
        P(None, tp),
        P(tp),
        P(None, tp, None),
        P("dp", None),
        P("dp", None, None),
        P("dp", None, None),
    )
    out_specs = P("dp", tp, None)
    return jax.shard_map(local, mesh=mesh3, in_specs=in_specs, out_specs=out_specs, check_vma=False)
```

```python
import jax
import jax.numpy as jnp
from jax import lax
from jax.sharding import Mesh
from jax.sharding import PartitionSpec as P

HEAD_DIM = 128
IMGS = 3
REG = 5


norm_eps = 1e-06


def layer_norm(row_data, gain_vec, shift_vec):
    values = row_data.astype(jnp.float32)
    center = values - jnp.mean(values, axis=-1, keepdims=True)
    spread = jnp.mean(center * center, axis=-1, keepdims=True)
    return (center * lax.rsqrt(spread + norm_eps) * gain_vec + shift_vec).astype(jnp.bfloat16)


def image_layout(grid_row):
    heights = grid_row[:, 0]
    widths = grid_row[:, 1]
    lengths = REG + heights * widths
    starts = jnp.cumsum(lengths) - lengths
    counts = heights // 2 * (widths // 2)
    merged_end = jnp.cumsum(counts)
    return (heights, widths, starts, merged_end - counts, merged_end)


def pick_rows(onehot, lookup):
    return jnp.sum(onehot * lookup[None, :], axis=1)


def rope_tables(seg_at, position, grid_row):
    heights, widths, starts, first_merged, last_merged = image_layout(grid_row)
    image_ids = jnp.arange(IMGS, dtype=jnp.int32)
    onehot = (seg_at[:, None] == image_ids[None, :]).astype(jnp.int32)
    is_image = jnp.sum(onehot, axis=1) > 0
    in_image = position - pick_rows(onehot, starts) - REG
    is_patch = is_image & (in_image >= 0)
    row_width = jnp.maximum(pick_rows(onehot, widths), 1)
    col_height = jnp.maximum(pick_rows(onehot, heights), 1)
    clipped = jnp.maximum(in_image, 0)
    coord_y = (
        2.0 * ((clipped // row_width).astype(jnp.float32) + 0.5) / col_height.astype(jnp.float32)
        - 1.0
    )
    coord_x = (
        2.0 * ((clipped % row_width).astype(jnp.float32) + 0.5) / row_width.astype(jnp.float32)
        - 1.0
    )
    quarter = HEAD_DIM // 4
    pair_ids = jnp.arange(HEAD_DIM // 2, dtype=jnp.int32)
    omegas = 100.0 ** ((pair_ids % quarter).astype(jnp.float32) / quarter)
    coord_all = jnp.where(pair_ids[None, :] < quarter, coord_y[:, None], coord_x[:, None])
    angles = jnp.where(is_patch[:, None], jnp.pi * omegas[None, :] * coord_all, 0.0)
    return (jnp.cos(angles), jnp.sin(angles))


def rotate(values, cos_rows, sin_rows):
    half_dim = values.shape[-1] // 2
    first_half = values[..., :half_dim]
    second_half = values[..., half_dim:]
    return jnp.concatenate(
        [
            first_half * cos_rows - second_half * sin_rows,
            second_half * cos_rows + first_half * sin_rows,
        ],
        axis=-1,
    )


def merge_sources(grid_row, merged_rows):
    heights, widths, starts, first_merged, last_merged = image_layout(grid_row)
    row_ids = jnp.arange(merged_rows, dtype=jnp.int32)
    onehot = (
        (row_ids[:, None] >= first_merged[None, :]) & (row_ids[:, None] < last_merged[None, :])
    ).astype(jnp.int32)
    is_valid = jnp.sum(onehot, axis=1) > 0
    row_width = pick_rows(onehot, widths)
    half_width = jnp.maximum(row_width // 2, 1)
    in_image = row_ids - pick_rows(onehot, first_merged)
    corner = (
        pick_rows(onehot, starts)
        + REG
        + 2 * (in_image // half_width) * row_width
        + 2 * (in_image % half_width)
    )
    offsets = jnp.stack(
        [jnp.zeros_like(row_width), jnp.ones_like(row_width), row_width, row_width + 1], axis=1
    )
    sources = jnp.where(is_valid[:, None], corner[:, None] + offsets, 0)
    return (sources, is_valid)


def attend(query_rows, query_seg, key_rows, value_rows, key_seg):
    scores = lax.dot_general(
        query_rows, key_rows, (((1,), (1,)), ((), ())), preferred_element_type=jnp.float32
    ) * HEAD_DIM ** (-0.5)
    scores = jnp.where(query_seg[:, None] == key_seg[None, :], scores, -jnp.inf)
    shifted = jnp.exp(scores - jnp.max(scores, axis=1, keepdims=True))
    weights = (shifted / jnp.sum(shifted, axis=1, keepdims=True)).astype(jnp.bfloat16)
    return jnp.dot(weights, value_rows, preferred_element_type=jnp.float32).astype(jnp.bfloat16)


def owner_ranks(owner_row):
    rows = owner_row.shape[0]
    same = owner_row[:, None] == owner_row[None, :]
    earlier = jnp.arange(rows)[None, :] < jnp.arange(rows)[:, None]
    return jnp.sum((same & earlier).astype(jnp.int32), axis=1)


def chip_shift(v, along, step, side):
    perm = []
    for src in range(side * side):
        x, y = src // side, src % side
        if along == 0:
            dst = ((x + step) % side) * side + y
        else:
            dst = x * side + (y + step) % side
        perm.append((src, dst))
    return lax.ppermute(v, "xy", perm)


def ring4(piece, along, side, cut):
    from_left = chip_shift(piece, along, 1, side)
    from_right = chip_shift(piece, along, -1, side)
    size = piece.shape[cut] // 2
    far_a = chip_shift(lax.slice_in_dim(from_left, 0, size, axis=cut), along, 1, side)
    far_b = chip_shift(lax.slice_in_dim(from_right, size, 2 * size, axis=cut), along, -1, side)
    far = jnp.concatenate([far_a, far_b], axis=cut)
    return jnp.stack([piece, from_right, far, from_left], axis=0)


def gather_torus(v, side, cut):
    size = v.shape[cut] // 2
    first = lax.slice_in_dim(v, 0, size, axis=cut)
    second = lax.slice_in_dim(v, size, 2 * size, axis=cut)
    row_x = ring4(first, 0, side, cut)
    col_y = ring4(second, 1, side, cut)
    first_all = ring4(row_x, 1, side, 0)
    second_all = ring4(col_y, 0, side, 0)
    first_all = jnp.swapaxes(first_all, 0, 1)
    return jnp.concatenate([first_all, second_all], axis=cut + 2)


def ring_reduce(q, along, side):
    size = q.shape[-1] // 2
    from_left = chip_shift(q[2][..., :size], along, 1, side)
    from_right = chip_shift(q[2][..., size:], along, -1, side)
    to_right = jnp.concatenate([q[1][..., :size] + from_left, q[1][..., size:]], axis=-1)
    to_left = jnp.concatenate([q[3][..., :size], q[3][..., size:] + from_right], axis=-1)
    return q[0] + chip_shift(to_right, along, 1, side) + chip_shift(to_left, along, -1, side)


def reduce_torus(s_rel, side):
    size = s_rel.shape[-1] // 2
    first = jnp.swapaxes(s_rel[..., :size], 0, 1)
    second = s_rel[..., size:]
    first_sum = ring_reduce(ring_reduce(first, 1, side), 0, side)
    second_sum = ring_reduce(ring_reduce(second, 0, side), 1, side)
    return jnp.concatenate([first_sum, second_sum], axis=-1)


def swap_core(v):
    return lax.ppermute(v, "core", [(0, 1), (1, 0)])


def to_absolute(v, cx, cy):
    return jnp.roll(jnp.roll(v, cx, axis=0), cy, axis=1)


def to_relative(v, cx, cy):
    return jnp.roll(jnp.roll(v, -cx, axis=0), -cy, axis=1)


def local(
    tokens, ln_gain, ln_bias, w_qkv, w_out, layer_scale, w_merge, segment_ids, grid_sizes, owners
):
    chips = lax.axis_size("xy")
    side = 4
    batch_count = lax.axis_size("dp")
    chip = lax.axis_index("xy")
    core = lax.axis_index("core")
    cx = chip // side
    cy = chip % side
    seg_row = segment_ids[0]
    grid_row = grid_sizes[0]
    owner_row = owners[0, :, 0]
    seq_len = seg_row.shape[0]
    block = tokens.shape[1]
    model_width = tokens.shape[2]
    col_width = layer_scale.shape[0]
    half_rows = chips * block
    merged_rows = seq_len // 4
    tensor_count = 2 * chips
    own_cap = 4
    out_width = w_merge.shape[2]

    x_rel = gather_torus(tokens[0], side, 1)
    w_partner = swap_core(w_qkv)
    wo_partner = swap_core(w_out)
    ls_partner = swap_core(layer_scale)

    offs = jnp.arange(side, dtype=jnp.int32)
    chip_of = ((cx + offs)[:, None] % side) * side + (cy + offs)[None, :] % side
    within = jnp.arange(block, dtype=jnp.int32)
    pos_mine = ((2 * chip_of + core)[:, :, None] * block + within).reshape(half_rows)
    pos_other = ((2 * chip_of + 1 - core)[:, :, None] * block + within).reshape(half_rows)
    seg_cores = seg_row.reshape(side, side, 2, block)
    seg_mine = to_relative(seg_cores[:, :, core], cx, cy).reshape(half_rows)
    seg_other = to_relative(seg_cores[:, :, 1 - core], cx, cy).reshape(half_rows)
    cos_t, sin_t = rope_tables(seg_mine, pos_mine, grid_row)

    x_rows = x_rel.reshape(half_rows, model_width)
    normed = layer_norm(x_rows, ln_gain, ln_bias)
    w_both = jnp.stack([w_qkv, w_partner], axis=2)
    qkv_weight = w_both.reshape(model_width, 3 * 2 * HEAD_DIM)
    product = jnp.dot(normed, qkv_weight, preferred_element_type=jnp.float32).reshape(
        half_rows, 3, 2, HEAD_DIM
    )
    cos_rows = cos_t[:, None, :]
    sin_rows = sin_t[:, None, :]
    q_here = rotate(product[:, 0], cos_rows, sin_rows).astype(jnp.bfloat16)
    k_here = rotate(product[:, 1], cos_rows, sin_rows).astype(jnp.bfloat16)
    v_here = product[:, 2].astype(jnp.bfloat16)
    kv_here = jnp.stack([k_here, v_here], axis=1)
    kv_other = swap_core(kv_here)[:, :, ::-1]
    kv_all = jnp.concatenate([kv_here, kv_other], axis=0)
    key_all = kv_all[:, 0]
    value_all = kv_all[:, 1]
    seg_keys = jnp.concatenate([seg_mine, seg_other], axis=0)

    def one_head(h):
        return attend(q_here[:, h], seg_mine, key_all[:, h], value_all[:, h], seg_keys)

    context_rel = jnp.stack([one_head(0), one_head(1)], axis=1).reshape(
        side, side, block, 2 * HEAD_DIM
    )
    context_abs = to_absolute(context_rel, cx, cy).reshape(half_rows, 2 * HEAD_DIM)
    context_g = gather_torus(context_abs, side, 0)
    context = jnp.transpose(context_g, (2, 0, 1, 3)).reshape(half_rows, model_width)
    wo_both = jnp.concatenate([w_out, wo_partner], axis=1).reshape(
        side, side, 2, HEAD_DIM, 2 * col_width
    )
    wo_rel = to_relative(wo_both, cx, cy)
    wo_rel = jnp.where(core == 0, wo_rel, wo_rel[:, :, ::-1])
    wo_rows = wo_rel.reshape(model_width, 2 * col_width)
    mixed = jnp.dot(context, wo_rows, preferred_element_type=jnp.float32)
    group_mine = 2 * chip + core
    group_other = 2 * chip + 1 - core
    x_mine = lax.dynamic_slice_in_dim(x_rel, group_mine * col_width, col_width, 3)
    x_other = lax.dynamic_slice_in_dim(x_rel, group_other * col_width, col_width, 3)
    x_cols = to_absolute(jnp.concatenate([x_mine, x_other], axis=3), cx, cy).reshape(
        half_rows, 2 * col_width
    )
    ls_both = jnp.concatenate([layer_scale, ls_partner], axis=0)
    hidden_here = (x_cols.astype(jnp.float32) + ls_both * mixed).astype(jnp.bfloat16)
    hidden_recv = swap_core(hidden_here[:, col_width:])
    hidden = jnp.concatenate([hidden_here[:, :col_width], hidden_recv], axis=0)

    sources, is_valid = merge_sources(grid_row, merged_rows)
    src_block = sources // block
    src_index = (
        (src_block % 2 != core).astype(jnp.int32) * half_rows
        + (src_block // 2) * block
        + sources % block
    )
    merged = jnp.where(
        is_valid[:, None, None], hidden[src_index], jnp.zeros((), jnp.bfloat16)
    ).reshape(merged_rows, 4 * col_width)
    merge_weight = w_merge.reshape(4 * col_width, out_width)
    ranks = owner_ranks(owner_row)
    owner_dp = owner_row // tensor_count
    owner_t = owner_row % tensor_count
    slot_keys = owner_t * (batch_count * own_cap) + owner_dp * own_cap + ranks
    slot_ids = jnp.arange(tensor_count * batch_count * own_cap, dtype=jnp.int32)
    placing = (slot_ids[:, None] == slot_keys[None, :]).astype(jnp.bfloat16)
    by_owner = jnp.dot(placing, merged, preferred_element_type=jnp.float32).astype(jnp.bfloat16)
    group_part = jnp.dot(by_owner, merge_weight, preferred_element_type=jnp.float32).astype(
        jnp.bfloat16
    )
    part32 = group_part.astype(jnp.float32).reshape(chips, 2, batch_count * own_cap, out_width)
    part_keep = jnp.where(core == 0, part32[:, 0], part32[:, 1])
    part_send = jnp.where(core == 0, part32[:, 1], part32[:, 0])
    part_chip = part_keep + swap_core(part_send)
    s_rel = to_relative(
        part_chip.reshape(side, side, batch_count * own_cap, out_width), cx, cy
    )
    mine = reduce_torus(s_rel, side)
    outgoing = mine.astype(jnp.bfloat16).reshape(batch_count, own_cap, out_width)
    incoming = lax.all_to_all(outgoing, "dp", split_axis=0, concat_axis=0, tiled=True)
    return incoming.reshape(1, batch_count * own_cap, out_width)


def solution(mesh):
    devices = mesh.devices.reshape(mesh.shape["dp"], -1, 2)
    mesh3 = Mesh(devices, ("dp", "xy", "core"))
    tp = ("xy", "core")
    in_specs = (
        P("dp", tp, None),
        P(),
        P(),
        P(None, None, tp),
        P(None, tp),
        P(tp),
        P(None, tp, None),
        P("dp", None),
        P("dp", None, None),
        P("dp", None, None),
    )
    out_specs = P("dp", tp, None)
    return jax.shard_map(local, mesh=mesh3, in_specs=in_specs, out_specs=out_specs, check_vma=False)
```

```python
import jax
import jax.numpy as jnp
from jax import lax
from jax.sharding import Mesh
from jax.sharding import PartitionSpec as P

HEAD_DIM = 128
IMGS = 3
REG = 5


norm_eps = 1e-06


def layer_norm(row_data, gain_vec, shift_vec):
    values = row_data.astype(jnp.float32)
    center = values - jnp.mean(values, axis=-1, keepdims=True)
    spread = jnp.mean(center * center, axis=-1, keepdims=True)
    return (center * lax.rsqrt(spread + norm_eps) * gain_vec + shift_vec).astype(jnp.bfloat16)


def image_layout(grid_row):
    heights = grid_row[:, 0]
    widths = grid_row[:, 1]
    lengths = REG + heights * widths
    starts = jnp.cumsum(lengths) - lengths
    counts = heights // 2 * (widths // 2)
    merged_end = jnp.cumsum(counts)
    return (heights, widths, starts, merged_end - counts, merged_end)


def pick_rows(onehot, lookup):
    return jnp.sum(onehot * lookup[None, :], axis=1)


def rope_tables(seg_at, position, grid_row):
    heights, widths, starts, first_merged, last_merged = image_layout(grid_row)
    image_ids = jnp.arange(IMGS, dtype=jnp.int32)
    onehot = (seg_at[:, None] == image_ids[None, :]).astype(jnp.int32)
    is_image = jnp.sum(onehot, axis=1) > 0
    in_image = position - pick_rows(onehot, starts) - REG
    is_patch = is_image & (in_image >= 0)
    row_width = jnp.maximum(pick_rows(onehot, widths), 1)
    col_height = jnp.maximum(pick_rows(onehot, heights), 1)
    clipped = jnp.maximum(in_image, 0)
    coord_y = (
        2.0 * ((clipped // row_width).astype(jnp.float32) + 0.5) / col_height.astype(jnp.float32)
        - 1.0
    )
    coord_x = (
        2.0 * ((clipped % row_width).astype(jnp.float32) + 0.5) / row_width.astype(jnp.float32)
        - 1.0
    )
    quarter = HEAD_DIM // 4
    pair_ids = jnp.arange(HEAD_DIM // 2, dtype=jnp.int32)
    omegas = 100.0 ** ((pair_ids % quarter).astype(jnp.float32) / quarter)
    coord_all = jnp.where(pair_ids[None, :] < quarter, coord_y[:, None], coord_x[:, None])
    angles = jnp.where(is_patch[:, None], jnp.pi * omegas[None, :] * coord_all, 0.0)
    return (jnp.cos(angles), jnp.sin(angles))


def rotate(values, cos_rows, sin_rows):
    half_dim = values.shape[-1] // 2
    first_half = values[..., :half_dim]
    second_half = values[..., half_dim:]
    return jnp.concatenate(
        [
            first_half * cos_rows - second_half * sin_rows,
            second_half * cos_rows + first_half * sin_rows,
        ],
        axis=-1,
    )


def merge_sources(grid_row, merged_rows):
    heights, widths, starts, first_merged, last_merged = image_layout(grid_row)
    row_ids = jnp.arange(merged_rows, dtype=jnp.int32)
    onehot = (
        (row_ids[:, None] >= first_merged[None, :]) & (row_ids[:, None] < last_merged[None, :])
    ).astype(jnp.int32)
    is_valid = jnp.sum(onehot, axis=1) > 0
    row_width = pick_rows(onehot, widths)
    half_width = jnp.maximum(row_width // 2, 1)
    in_image = row_ids - pick_rows(onehot, first_merged)
    corner = (
        pick_rows(onehot, starts)
        + REG
        + 2 * (in_image // half_width) * row_width
        + 2 * (in_image % half_width)
    )
    offsets = jnp.stack(
        [jnp.zeros_like(row_width), jnp.ones_like(row_width), row_width, row_width + 1], axis=1
    )
    sources = jnp.where(is_valid[:, None], corner[:, None] + offsets, 0)
    return (sources, is_valid)


def attend(query_rows, query_seg, key_rows, value_rows, key_seg):
    scores = lax.dot_general(
        query_rows, key_rows, (((1,), (1,)), ((), ())), preferred_element_type=jnp.float32
    ) * HEAD_DIM ** (-0.5)
    scores = jnp.where(query_seg[:, None] == key_seg[None, :], scores, -jnp.inf)
    shifted = jnp.exp(scores - jnp.max(scores, axis=1, keepdims=True))
    weights = (shifted / jnp.sum(shifted, axis=1, keepdims=True)).astype(jnp.bfloat16)
    return jnp.dot(weights, value_rows, preferred_element_type=jnp.float32).astype(jnp.bfloat16)


def owner_ranks(owner_row):
    rows = owner_row.shape[0]
    same = owner_row[:, None] == owner_row[None, :]
    earlier = jnp.arange(rows)[None, :] < jnp.arange(rows)[:, None]
    return jnp.sum((same & earlier).astype(jnp.int32), axis=1)


def chip_shift(v, along, step, side):
    perm = []
    for src in range(side * side):
        x, y = src // side, src % side
        if along == 0:
            dst = ((x + step) % side) * side + y
        else:
            dst = x * side + (y + step) % side
        perm.append((src, dst))
    return lax.ppermute(v, "xy", perm)


def ring4(piece, along, side, cut):
    from_left = chip_shift(piece, along, 1, side)
    from_right = chip_shift(piece, along, -1, side)
    size = piece.shape[cut] // 2
    far_a = chip_shift(lax.slice_in_dim(from_left, 0, size, axis=cut), along, 1, side)
    far_b = chip_shift(lax.slice_in_dim(from_right, size, 2 * size, axis=cut), along, -1, side)
    far = jnp.concatenate([far_a, far_b], axis=cut)
    return jnp.stack([piece, from_right, far, from_left], axis=0)


def gather_torus(v, side, cut):
    size = v.shape[cut] // 2
    a = lax.slice_in_dim(v, 0, size, axis=cut)
    b = lax.slice_in_dim(v, size, 2 * size, axis=cut)
    a_l, a_r = chip_shift(a, 0, 1, side), chip_shift(a, 0, -1, side)
    b_l, b_r = chip_shift(b, 1, 1, side), chip_shift(b, 1, -1, side)
    a_l, a_r, b_l, b_r = lax.optimization_barrier((a_l, a_r, b_l, b_r))
    quarter = size // 2
    a_f = jnp.concatenate(
        [
            chip_shift(lax.slice_in_dim(a_l, 0, quarter, axis=cut), 0, 1, side),
            chip_shift(lax.slice_in_dim(a_r, quarter, size, axis=cut), 0, -1, side),
        ],
        axis=cut,
    )
    b_f = jnp.concatenate(
        [
            chip_shift(lax.slice_in_dim(b_l, 0, quarter, axis=cut), 1, 1, side),
            chip_shift(lax.slice_in_dim(b_r, quarter, size, axis=cut), 1, -1, side),
        ],
        axis=cut,
    )
    a_f, b_f = lax.optimization_barrier((a_f, b_f))
    row_x = jnp.stack([a, a_r, a_f, a_l], axis=0)
    col_y = jnp.stack([b, b_r, b_f, b_l], axis=0)
    ra_l, ra_r = chip_shift(row_x, 1, 1, side), chip_shift(row_x, 1, -1, side)
    cb_l, cb_r = chip_shift(col_y, 0, 1, side), chip_shift(col_y, 0, -1, side)
    ra_l, ra_r, cb_l, cb_r = lax.optimization_barrier((ra_l, ra_r, cb_l, cb_r))
    ra_f = jnp.concatenate(
        [chip_shift(ra_l[:2], 1, 1, side), chip_shift(ra_r[2:], 1, -1, side)], axis=0
    )
    cb_f = jnp.concatenate(
        [chip_shift(cb_l[:2], 0, 1, side), chip_shift(cb_r[2:], 0, -1, side)], axis=0
    )
    ra_f, cb_f = lax.optimization_barrier((ra_f, cb_f))
    first_all = jnp.swapaxes(jnp.stack([row_x, ra_r, ra_f, ra_l], axis=0), 0, 1)
    second_all = jnp.stack([col_y, cb_r, cb_f, cb_l], axis=0)
    return jnp.concatenate([first_all, second_all], axis=cut + 2)


def ring_reduce(q, along, side):
    size = q.shape[-1] // 2
    from_left = chip_shift(q[2][..., :size], along, 1, side)
    from_right = chip_shift(q[2][..., size:], along, -1, side)
    to_right = jnp.concatenate([q[1][..., :size] + from_left, q[1][..., size:]], axis=-1)
    to_left = jnp.concatenate([q[3][..., :size], q[3][..., size:] + from_right], axis=-1)
    return q[0] + chip_shift(to_right, along, 1, side) + chip_shift(to_left, along, -1, side)


def reduce_torus(s_rel, side):
    size = s_rel.shape[-1] // 2
    first = jnp.swapaxes(s_rel[..., :size], 0, 1)
    second = s_rel[..., size:]
    first_sum = ring_reduce(ring_reduce(first, 1, side), 0, side)
    second_sum = ring_reduce(ring_reduce(second, 0, side), 1, side)
    return jnp.concatenate([first_sum, second_sum], axis=-1)


def swap_core(v):
    return lax.ppermute(v, "core", [(0, 1), (1, 0)])


def to_absolute(v, cx, cy):
    return jnp.roll(jnp.roll(v, cx, axis=0), cy, axis=1)


def to_relative(v, cx, cy):
    return jnp.roll(jnp.roll(v, -cx, axis=0), -cy, axis=1)


def local(
    tokens, ln_gain, ln_bias, w_qkv, w_out, layer_scale, w_merge, segment_ids, grid_sizes, owners
):
    chips = lax.axis_size("xy")
    side = 4
    batch_count = lax.axis_size("dp")
    chip = lax.axis_index("xy")
    core = lax.axis_index("core")
    cx = chip // side
    cy = chip % side
    seg_row = segment_ids[0]
    grid_row = grid_sizes[0]
    owner_row = owners[0, :, 0]
    seq_len = seg_row.shape[0]
    block = tokens.shape[1]
    model_width = tokens.shape[2]
    col_width = layer_scale.shape[0]
    half_rows = chips * block
    merged_rows = seq_len // 4
    tensor_count = 2 * chips
    own_cap = 4
    out_width = w_merge.shape[2]

    x_rel = gather_torus(tokens[0], side, 1)
    w_partner = swap_core(w_qkv)
    wo_partner = swap_core(w_out)
    ls_partner = swap_core(layer_scale)

    offs = jnp.arange(side, dtype=jnp.int32)
    chip_of = ((cx + offs)[:, None] % side) * side + (cy + offs)[None, :] % side
    within = jnp.arange(block, dtype=jnp.int32)
    pos_mine = ((2 * chip_of + core)[:, :, None] * block + within).reshape(half_rows)
    pos_other = ((2 * chip_of + 1 - core)[:, :, None] * block + within).reshape(half_rows)
    seg_cores = seg_row.reshape(side, side, 2, block)
    seg_mine = to_relative(seg_cores[:, :, core], cx, cy).reshape(half_rows)
    seg_other = to_relative(seg_cores[:, :, 1 - core], cx, cy).reshape(half_rows)
    cos_t, sin_t = rope_tables(seg_mine, pos_mine, grid_row)

    x_rows = x_rel.reshape(half_rows, model_width)
    normed = layer_norm(x_rows, ln_gain, ln_bias)
    w_both = jnp.stack([w_qkv, w_partner], axis=2)
    qkv_weight = w_both.reshape(model_width, 3 * 2 * HEAD_DIM)
    product = jnp.dot(normed, qkv_weight, preferred_element_type=jnp.float32).reshape(
        half_rows, 3, 2, HEAD_DIM
    )
    cos_rows = cos_t[:, None, :]
    sin_rows = sin_t[:, None, :]
    q_here = rotate(product[:, 0], cos_rows, sin_rows).astype(jnp.bfloat16)
    k_here = rotate(product[:, 1], cos_rows, sin_rows).astype(jnp.bfloat16)
    v_here = product[:, 2].astype(jnp.bfloat16)
    kv_here = jnp.stack([k_here, v_here], axis=1)
    kv_other = swap_core(kv_here)[:, :, ::-1]
    kv_all = jnp.concatenate([kv_here, kv_other], axis=0)
    key_all = kv_all[:, 0]
    value_all = kv_all[:, 1]
    seg_keys = jnp.concatenate([seg_mine, seg_other], axis=0)

    def one_head(h):
        return attend(q_here[:, h], seg_mine, key_all[:, h], value_all[:, h], seg_keys)

    context_rel = jnp.stack([one_head(0), one_head(1)], axis=1).reshape(
        side, side, block, 2 * HEAD_DIM
    )
    context_abs = to_absolute(context_rel, cx, cy).reshape(half_rows, 2 * HEAD_DIM)
    context_g = gather_torus(context_abs, side, 0)
    context = jnp.transpose(context_g, (2, 0, 1, 3)).reshape(half_rows, model_width)
    wo_both = jnp.concatenate([w_out, wo_partner], axis=1).reshape(
        side, side, 2, HEAD_DIM, 2 * col_width
    )
    wo_rel = to_relative(wo_both, cx, cy)
    wo_rel = jnp.where(core == 0, wo_rel, wo_rel[:, :, ::-1])
    wo_rows = wo_rel.reshape(model_width, 2 * col_width)
    mixed = jnp.dot(context, wo_rows, preferred_element_type=jnp.float32)
    group_mine = 2 * chip + core
    group_other = 2 * chip + 1 - core
    x_mine = lax.dynamic_slice_in_dim(x_rel, group_mine * col_width, col_width, 3)
    x_other = lax.dynamic_slice_in_dim(x_rel, group_other * col_width, col_width, 3)
    x_cols = to_absolute(jnp.concatenate([x_mine, x_other], axis=3), cx, cy).reshape(
        half_rows, 2 * col_width
    )
    ls_both = jnp.concatenate([layer_scale, ls_partner], axis=0)
    hidden_here = (x_cols.astype(jnp.float32) + ls_both * mixed).astype(jnp.bfloat16)
    hidden_recv = swap_core(hidden_here[:, col_width:])
    hidden = jnp.concatenate([hidden_here[:, :col_width], hidden_recv], axis=0)

    sources, is_valid = merge_sources(grid_row, merged_rows)
    src_block = sources // block
    src_index = (
        (src_block % 2 != core).astype(jnp.int32) * half_rows
        + (src_block // 2) * block
        + sources % block
    )
    merged = jnp.where(
        is_valid[:, None, None], hidden[src_index], jnp.zeros((), jnp.bfloat16)
    ).reshape(merged_rows, 4 * col_width)
    merge_weight = w_merge.reshape(4 * col_width, out_width)
    ranks = owner_ranks(owner_row)
    owner_dp = owner_row // tensor_count
    owner_t = owner_row % tensor_count
    slot_keys = owner_t * (batch_count * own_cap) + owner_dp * own_cap + ranks
    slot_ids = jnp.arange(tensor_count * batch_count * own_cap, dtype=jnp.int32)
    placing = (slot_ids[:, None] == slot_keys[None, :]).astype(jnp.bfloat16)
    by_owner = jnp.dot(placing, merged, preferred_element_type=jnp.float32).astype(jnp.bfloat16)
    group_part = jnp.dot(by_owner, merge_weight, preferred_element_type=jnp.float32).astype(
        jnp.bfloat16
    )
    part32 = group_part.astype(jnp.float32).reshape(chips, 2, batch_count * own_cap, out_width)
    part_keep = jnp.where(core == 0, part32[:, 0], part32[:, 1])
    part_send = jnp.where(core == 0, part32[:, 1], part32[:, 0])
    part_chip = part_keep + swap_core(part_send)
    s_rel = to_relative(
        part_chip.reshape(side, side, batch_count * own_cap, out_width), cx, cy
    )
    mine = reduce_torus(s_rel, side)
    outgoing = mine.astype(jnp.bfloat16).reshape(batch_count, own_cap, out_width)
    plane = lax.axis_index("dp")
    out_rel = jnp.roll(outgoing, -plane, axis=0)
    recv = [out_rel[0]]
    for step in range(1, batch_count):
        perm = [(d, (d + step) % batch_count) for d in range(batch_count)]
        recv.append(lax.ppermute(out_rel[step], "dp", perm))
    incoming = jnp.roll(jnp.stack(recv, axis=0)[::-1], plane + 1, axis=0)
    return incoming.reshape(1, batch_count * own_cap, out_width)


def solution(mesh):
    devices = mesh.devices.reshape(mesh.shape["dp"], -1, 2)
    mesh3 = Mesh(devices, ("dp", "xy", "core"))
    tp = ("xy", "core")
    in_specs = (
        P("dp", tp, None),
        P(),
        P(),
        P(None, None, tp),
        P(None, tp),
        P(tp),
        P(None, tp, None),
        P("dp", None),
        P("dp", None, None),
        P("dp", None, None),
    )
    out_specs = P("dp", tp, None)
    return jax.shard_map(local, mesh=mesh3, in_specs=in_specs, out_specs=out_specs, check_vma=False)
```

```python
import jax
import jax.numpy as jnp
from jax import lax
from jax.sharding import Mesh
from jax.sharding import PartitionSpec as P

HEAD_DIM = 128
IMGS = 3
REG = 5


norm_eps = 1e-06


def layer_norm(row_data, gain_vec, shift_vec):
    values = row_data.astype(jnp.float32)
    center = values - jnp.mean(values, axis=-1, keepdims=True)
    spread = jnp.mean(center * center, axis=-1, keepdims=True)
    return (center * lax.rsqrt(spread + norm_eps) * gain_vec + shift_vec).astype(jnp.bfloat16)


def image_layout(grid_row):
    heights = grid_row[:, 0]
    widths = grid_row[:, 1]
    lengths = REG + heights * widths
    starts = jnp.cumsum(lengths) - lengths
    counts = heights // 2 * (widths // 2)
    merged_end = jnp.cumsum(counts)
    return (heights, widths, starts, merged_end - counts, merged_end)


def pick_rows(onehot, lookup):
    return jnp.sum(onehot * lookup[None, :], axis=1)


def rope_tables(seg_at, position, grid_row):
    heights, widths, starts, first_merged, last_merged = image_layout(grid_row)
    image_ids = jnp.arange(IMGS, dtype=jnp.int32)
    onehot = (seg_at[:, None] == image_ids[None, :]).astype(jnp.int32)
    is_image = jnp.sum(onehot, axis=1) > 0
    in_image = position - pick_rows(onehot, starts) - REG
    is_patch = is_image & (in_image >= 0)
    row_width = jnp.maximum(pick_rows(onehot, widths), 1)
    col_height = jnp.maximum(pick_rows(onehot, heights), 1)
    clipped = jnp.maximum(in_image, 0)
    coord_y = (
        2.0 * ((clipped // row_width).astype(jnp.float32) + 0.5) / col_height.astype(jnp.float32)
        - 1.0
    )
    coord_x = (
        2.0 * ((clipped % row_width).astype(jnp.float32) + 0.5) / row_width.astype(jnp.float32)
        - 1.0
    )
    quarter = HEAD_DIM // 4
    pair_ids = jnp.arange(HEAD_DIM // 2, dtype=jnp.int32)
    omegas = 100.0 ** ((pair_ids % quarter).astype(jnp.float32) / quarter)
    coord_all = jnp.where(pair_ids[None, :] < quarter, coord_y[:, None], coord_x[:, None])
    angles = jnp.where(is_patch[:, None], jnp.pi * omegas[None, :] * coord_all, 0.0)
    return (jnp.cos(angles), jnp.sin(angles))


def rotate(values, cos_rows, sin_rows):
    half_dim = values.shape[-1] // 2
    first_half = values[..., :half_dim]
    second_half = values[..., half_dim:]
    return jnp.concatenate(
        [
            first_half * cos_rows - second_half * sin_rows,
            second_half * cos_rows + first_half * sin_rows,
        ],
        axis=-1,
    )


def merge_sources(grid_row, merged_rows):
    heights, widths, starts, first_merged, last_merged = image_layout(grid_row)
    row_ids = jnp.arange(merged_rows, dtype=jnp.int32)
    onehot = (
        (row_ids[:, None] >= first_merged[None, :]) & (row_ids[:, None] < last_merged[None, :])
    ).astype(jnp.int32)
    is_valid = jnp.sum(onehot, axis=1) > 0
    row_width = pick_rows(onehot, widths)
    half_width = jnp.maximum(row_width // 2, 1)
    in_image = row_ids - pick_rows(onehot, first_merged)
    corner = (
        pick_rows(onehot, starts)
        + REG
        + 2 * (in_image // half_width) * row_width
        + 2 * (in_image % half_width)
    )
    offsets = jnp.stack(
        [jnp.zeros_like(row_width), jnp.ones_like(row_width), row_width, row_width + 1], axis=1
    )
    sources = jnp.where(is_valid[:, None], corner[:, None] + offsets, 0)
    return (sources, is_valid)


def attend(query_rows, query_seg, key_rows, value_rows, key_seg):
    scores = lax.dot_general(
        query_rows, key_rows, (((1,), (1,)), ((), ())), preferred_element_type=jnp.float32
    ) * HEAD_DIM ** (-0.5)
    scores = jnp.where(query_seg[:, None] == key_seg[None, :], scores, -jnp.inf)
    shifted = jnp.exp(scores - jnp.max(scores, axis=1, keepdims=True))
    weights = (shifted / jnp.sum(shifted, axis=1, keepdims=True)).astype(jnp.bfloat16)
    return jnp.dot(weights, value_rows, preferred_element_type=jnp.float32).astype(jnp.bfloat16)


def owner_ranks(owner_row):
    rows = owner_row.shape[0]
    same = owner_row[:, None] == owner_row[None, :]
    earlier = jnp.arange(rows)[None, :] < jnp.arange(rows)[:, None]
    return jnp.sum((same & earlier).astype(jnp.int32), axis=1)


def chip_shift(v, along, step, side):
    perm = []
    for src in range(side * side):
        x, y = src // side, src % side
        if along == 0:
            dst = ((x + step) % side) * side + y
        else:
            dst = x * side + (y + step) % side
        perm.append((src, dst))
    return lax.ppermute(v, "xy", perm)


def ring4(piece, along, side, cut):
    from_left = chip_shift(piece, along, 1, side)
    from_right = chip_shift(piece, along, -1, side)
    size = piece.shape[cut] // 2
    far_a = chip_shift(lax.slice_in_dim(from_left, 0, size, axis=cut), along, 1, side)
    far_b = chip_shift(lax.slice_in_dim(from_right, size, 2 * size, axis=cut), along, -1, side)
    far = jnp.concatenate([far_a, far_b], axis=cut)
    return jnp.stack([piece, from_right, far, from_left], axis=0)


def gather_torus(v, side, cut):
    size = v.shape[cut] // 2
    a = lax.slice_in_dim(v, 0, size, axis=cut)
    b = lax.slice_in_dim(v, size, 2 * size, axis=cut)
    a_l, a_r, a_f = (chip_shift(a, 0, k, side) for k in (1, -1, 2))
    b_l, b_r, b_f = (chip_shift(b, 1, k, side) for k in (1, -1, 2))
    a_l, a_r, a_f, b_l, b_r, b_f = lax.optimization_barrier((a_l, a_r, a_f, b_l, b_r, b_f))
    row_x = jnp.stack([a, a_r, a_f, a_l], axis=0)
    col_y = jnp.stack([b, b_r, b_f, b_l], axis=0)
    ra_l, ra_r = chip_shift(row_x, 1, 1, side), chip_shift(row_x, 1, -1, side)
    cb_l, cb_r = chip_shift(col_y, 0, 1, side), chip_shift(col_y, 0, -1, side)
    ra_l, ra_r, cb_l, cb_r = lax.optimization_barrier((ra_l, ra_r, cb_l, cb_r))
    ra_f = jnp.concatenate(
        [chip_shift(ra_l[:2], 1, 1, side), chip_shift(ra_r[2:], 1, -1, side)], axis=0
    )
    cb_f = jnp.concatenate(
        [chip_shift(cb_l[:2], 0, 1, side), chip_shift(cb_r[2:], 0, -1, side)], axis=0
    )
    ra_f, cb_f = lax.optimization_barrier((ra_f, cb_f))
    first_all = jnp.swapaxes(jnp.stack([row_x, ra_r, ra_f, ra_l], axis=0), 0, 1)
    second_all = jnp.stack([col_y, cb_r, cb_f, cb_l], axis=0)
    return jnp.concatenate([first_all, second_all], axis=cut + 2)


def ring_reduce(q, along, side):
    size = q.shape[-1] // 2
    from_left = chip_shift(q[2][..., :size], along, 1, side)
    from_right = chip_shift(q[2][..., size:], along, -1, side)
    to_right = jnp.concatenate([q[1][..., :size] + from_left, q[1][..., size:]], axis=-1)
    to_left = jnp.concatenate([q[3][..., :size], q[3][..., size:] + from_right], axis=-1)
    return q[0] + chip_shift(to_right, along, 1, side) + chip_shift(to_left, along, -1, side)


def direct_reduce(q, along, side):
    return (
        q[0]
        + chip_shift(q[1], along, 1, side)
        + chip_shift(q[3], along, -1, side)
        + chip_shift(q[2], along, 2, side)
    )


def reduce_torus(s_rel, side):
    size = s_rel.shape[-1] // 2
    first = jnp.swapaxes(s_rel[..., :size], 0, 1)
    second = s_rel[..., size:]
    first_sum = direct_reduce(ring_reduce(first, 1, side), 0, side)
    second_sum = direct_reduce(ring_reduce(second, 0, side), 1, side)
    return jnp.concatenate([first_sum, second_sum], axis=-1)


def swap_core(v):
    return lax.ppermute(v, "core", [(0, 1), (1, 0)])


def to_absolute(v, cx, cy):
    return jnp.roll(jnp.roll(v, cx, axis=0), cy, axis=1)


def to_relative(v, cx, cy):
    return jnp.roll(jnp.roll(v, -cx, axis=0), -cy, axis=1)


def local(
    tokens, ln_gain, ln_bias, w_qkv, w_out, layer_scale, w_merge, segment_ids, grid_sizes, owners
):
    chips = lax.axis_size("xy")
    side = 4
    batch_count = lax.axis_size("dp")
    chip = lax.axis_index("xy")
    core = lax.axis_index("core")
    cx = chip // side
    cy = chip % side
    seg_row = segment_ids[0]
    grid_row = grid_sizes[0]
    owner_row = owners[0, :, 0]
    seq_len = seg_row.shape[0]
    block = tokens.shape[1]
    model_width = tokens.shape[2]
    col_width = layer_scale.shape[0]
    half_rows = chips * block
    merged_rows = seq_len // 4
    tensor_count = 2 * chips
    own_cap = 4
    out_width = w_merge.shape[2]

    x_rel = gather_torus(tokens[0], side, 1)
    w_partner = swap_core(w_qkv)
    wo_partner = swap_core(w_out)
    ls_partner = swap_core(layer_scale)

    offs = jnp.arange(side, dtype=jnp.int32)
    chip_of = ((cx + offs)[:, None] % side) * side + (cy + offs)[None, :] % side
    within = jnp.arange(block, dtype=jnp.int32)
    pos_mine = ((2 * chip_of + core)[:, :, None] * block + within).reshape(half_rows)
    pos_other = ((2 * chip_of + 1 - core)[:, :, None] * block + within).reshape(half_rows)
    seg_cores = seg_row.reshape(side, side, 2, block)
    seg_mine = to_relative(seg_cores[:, :, core], cx, cy).reshape(half_rows)
    seg_other = to_relative(seg_cores[:, :, 1 - core], cx, cy).reshape(half_rows)
    cos_t, sin_t = rope_tables(seg_mine, pos_mine, grid_row)

    x_rows = x_rel.reshape(half_rows, model_width)
    normed = layer_norm(x_rows, ln_gain, ln_bias)
    w_both = jnp.stack([w_qkv, w_partner], axis=2)
    qkv_weight = w_both.reshape(model_width, 3 * 2 * HEAD_DIM)
    product = jnp.dot(normed, qkv_weight, preferred_element_type=jnp.float32).reshape(
        half_rows, 3, 2, HEAD_DIM
    )
    cos_rows = cos_t[:, None, :]
    sin_rows = sin_t[:, None, :]
    q_here = rotate(product[:, 0], cos_rows, sin_rows).astype(jnp.bfloat16)
    k_here = rotate(product[:, 1], cos_rows, sin_rows).astype(jnp.bfloat16)
    v_here = product[:, 2].astype(jnp.bfloat16)
    kv_here = jnp.stack([k_here, v_here], axis=1)
    kv_other = swap_core(kv_here)[:, :, ::-1]
    kv_all = jnp.concatenate([kv_here, kv_other], axis=0)
    key_all = kv_all[:, 0]
    value_all = kv_all[:, 1]
    seg_keys = jnp.concatenate([seg_mine, seg_other], axis=0)

    def one_head(h):
        return attend(q_here[:, h], seg_mine, key_all[:, h], value_all[:, h], seg_keys)

    context_rel = jnp.stack([one_head(0), one_head(1)], axis=1).reshape(
        side, side, block, 2 * HEAD_DIM
    )
    context_abs = to_absolute(context_rel, cx, cy).reshape(half_rows, 2 * HEAD_DIM)
    context_g = gather_torus(context_abs, side, 0)
    context = jnp.transpose(context_g, (2, 0, 1, 3)).reshape(half_rows, model_width)
    wo_both = jnp.concatenate([w_out, wo_partner], axis=1).reshape(
        side, side, 2, HEAD_DIM, 2 * col_width
    )
    wo_rel = to_relative(wo_both, cx, cy)
    wo_rel = jnp.where(core == 0, wo_rel, wo_rel[:, :, ::-1])
    wo_rows = wo_rel.reshape(model_width, 2 * col_width)
    mixed = jnp.dot(context, wo_rows, preferred_element_type=jnp.float32)
    group_mine = 2 * chip + core
    group_other = 2 * chip + 1 - core
    x_mine = lax.dynamic_slice_in_dim(x_rel, group_mine * col_width, col_width, 3)
    x_other = lax.dynamic_slice_in_dim(x_rel, group_other * col_width, col_width, 3)
    x_cols = to_absolute(jnp.concatenate([x_mine, x_other], axis=3), cx, cy).reshape(
        half_rows, 2 * col_width
    )
    ls_both = jnp.concatenate([layer_scale, ls_partner], axis=0)
    hidden_here = (x_cols.astype(jnp.float32) + ls_both * mixed).astype(jnp.bfloat16)
    hidden_recv = swap_core(hidden_here[:, col_width:])
    hidden = jnp.concatenate([hidden_here[:, :col_width], hidden_recv], axis=0)

    sources, is_valid = merge_sources(grid_row, merged_rows)
    src_block = sources // block
    src_index = (
        (src_block % 2 != core).astype(jnp.int32) * half_rows
        + (src_block // 2) * block
        + sources % block
    )
    merged = jnp.where(
        is_valid[:, None, None], hidden[src_index], jnp.zeros((), jnp.bfloat16)
    ).reshape(merged_rows, 4 * col_width)
    merge_weight = w_merge.reshape(4 * col_width, out_width)
    ranks = owner_ranks(owner_row)
    owner_dp = owner_row // tensor_count
    owner_t = owner_row % tensor_count
    slot_keys = owner_t * (batch_count * own_cap) + owner_dp * own_cap + ranks
    slot_ids = jnp.arange(tensor_count * batch_count * own_cap, dtype=jnp.int32)
    placing = (slot_ids[:, None] == slot_keys[None, :]).astype(jnp.bfloat16)
    by_owner = jnp.dot(placing, merged, preferred_element_type=jnp.float32).astype(jnp.bfloat16)
    group_part = jnp.dot(by_owner, merge_weight, preferred_element_type=jnp.float32).astype(
        jnp.bfloat16
    )
    part32 = group_part.astype(jnp.float32).reshape(chips, 2, batch_count * own_cap, out_width)
    part_keep = jnp.where(core == 0, part32[:, 0], part32[:, 1])
    part_send = jnp.where(core == 0, part32[:, 1], part32[:, 0])
    part_chip = part_keep + swap_core(part_send)
    s_rel = to_relative(
        part_chip.reshape(side, side, batch_count * own_cap, out_width), cx, cy
    )
    mine = reduce_torus(s_rel, side)
    outgoing = mine.astype(jnp.bfloat16).reshape(batch_count, own_cap, out_width)
    plane = lax.axis_index("dp")
    out_rel = jnp.roll(outgoing, -plane, axis=0)
    recv = [out_rel[0]]
    for step in range(1, batch_count):
        perm = [(d, (d + step) % batch_count) for d in range(batch_count)]
        recv.append(lax.ppermute(out_rel[step], "dp", perm))
    incoming = jnp.roll(jnp.stack(recv, axis=0)[::-1], plane + 1, axis=0)
    return incoming.reshape(1, batch_count * own_cap, out_width)


def solution(mesh):
    devices = mesh.devices.reshape(mesh.shape["dp"], -1, 2)
    mesh3 = Mesh(devices, ("dp", "xy", "core"))
    tp = ("xy", "core")
    in_specs = (
        P("dp", tp, None),
        P(),
        P(),
        P(None, None, tp),
        P(None, tp),
        P(tp),
        P(None, tp, None),
        P("dp", None),
        P("dp", None, None),
        P("dp", None, None),
    )
    out_specs = P("dp", tp, None)
    return jax.shard_map(local, mesh=mesh3, in_specs=in_specs, out_specs=out_specs, check_vma=False)
```

```python
import jax
import jax.numpy as jnp
from jax import lax
from jax.sharding import Mesh
from jax.sharding import PartitionSpec as P

HEAD_DIM = 128
IMGS = 3
REG = 5


norm_eps = 1e-06


def layer_norm(row_data, gain_vec, shift_vec):
    values = row_data.astype(jnp.float32)
    center = values - jnp.mean(values, axis=-1, keepdims=True)
    spread = jnp.mean(center * center, axis=-1, keepdims=True)
    return (center * lax.rsqrt(spread + norm_eps) * gain_vec + shift_vec).astype(jnp.bfloat16)


def image_layout(grid_row):
    heights = grid_row[:, 0]
    widths = grid_row[:, 1]
    lengths = REG + heights * widths
    starts = jnp.cumsum(lengths) - lengths
    counts = heights // 2 * (widths // 2)
    merged_end = jnp.cumsum(counts)
    return (heights, widths, starts, merged_end - counts, merged_end)


def pick_rows(onehot, lookup):
    return jnp.sum(onehot * lookup[None, :], axis=1)


def rope_tables(seg_at, position, grid_row):
    heights, widths, starts, first_merged, last_merged = image_layout(grid_row)
    image_ids = jnp.arange(IMGS, dtype=jnp.int32)
    onehot = (seg_at[:, None] == image_ids[None, :]).astype(jnp.int32)
    is_image = jnp.sum(onehot, axis=1) > 0
    in_image = position - pick_rows(onehot, starts) - REG
    is_patch = is_image & (in_image >= 0)
    row_width = jnp.maximum(pick_rows(onehot, widths), 1)
    col_height = jnp.maximum(pick_rows(onehot, heights), 1)
    clipped = jnp.maximum(in_image, 0)
    coord_y = (
        2.0 * ((clipped // row_width).astype(jnp.float32) + 0.5) / col_height.astype(jnp.float32)
        - 1.0
    )
    coord_x = (
        2.0 * ((clipped % row_width).astype(jnp.float32) + 0.5) / row_width.astype(jnp.float32)
        - 1.0
    )
    quarter = HEAD_DIM // 4
    pair_ids = jnp.arange(HEAD_DIM // 2, dtype=jnp.int32)
    omegas = 100.0 ** ((pair_ids % quarter).astype(jnp.float32) / quarter)
    coord_all = jnp.where(pair_ids[None, :] < quarter, coord_y[:, None], coord_x[:, None])
    angles = jnp.where(is_patch[:, None], jnp.pi * omegas[None, :] * coord_all, 0.0)
    return (jnp.cos(angles), jnp.sin(angles))


def rotate(values, cos_rows, sin_rows):
    half_dim = values.shape[-1] // 2
    first_half = values[..., :half_dim]
    second_half = values[..., half_dim:]
    return jnp.concatenate(
        [
            first_half * cos_rows - second_half * sin_rows,
            second_half * cos_rows + first_half * sin_rows,
        ],
        axis=-1,
    )


def merge_sources(grid_row, merged_rows):
    heights, widths, starts, first_merged, last_merged = image_layout(grid_row)
    row_ids = jnp.arange(merged_rows, dtype=jnp.int32)
    onehot = (
        (row_ids[:, None] >= first_merged[None, :]) & (row_ids[:, None] < last_merged[None, :])
    ).astype(jnp.int32)
    is_valid = jnp.sum(onehot, axis=1) > 0
    row_width = pick_rows(onehot, widths)
    half_width = jnp.maximum(row_width // 2, 1)
    in_image = row_ids - pick_rows(onehot, first_merged)
    corner = (
        pick_rows(onehot, starts)
        + REG
        + 2 * (in_image // half_width) * row_width
        + 2 * (in_image % half_width)
    )
    offsets = jnp.stack(
        [jnp.zeros_like(row_width), jnp.ones_like(row_width), row_width, row_width + 1], axis=1
    )
    sources = jnp.where(is_valid[:, None], corner[:, None] + offsets, 0)
    return (sources, is_valid)


def attend(query_rows, query_seg, key_rows, value_rows, key_seg):
    scores = lax.dot_general(
        query_rows, key_rows, (((1,), (1,)), ((), ())), preferred_element_type=jnp.float32
    ) * HEAD_DIM ** (-0.5)
    scores = jnp.where(query_seg[:, None] == key_seg[None, :], scores, -jnp.inf)
    shifted = jnp.exp(scores - jnp.max(scores, axis=1, keepdims=True))
    weights = (shifted / jnp.sum(shifted, axis=1, keepdims=True)).astype(jnp.bfloat16)
    return jnp.dot(weights, value_rows, preferred_element_type=jnp.float32).astype(jnp.bfloat16)


def owner_ranks(owner_row):
    rows = owner_row.shape[0]
    same = owner_row[:, None] == owner_row[None, :]
    earlier = jnp.arange(rows)[None, :] < jnp.arange(rows)[:, None]
    return jnp.sum((same & earlier).astype(jnp.int32), axis=1)


def chip_shift(v, along, step, side):
    perm = []
    for src in range(side * side):
        x, y = src // side, src % side
        if along == 0:
            dst = ((x + step) % side) * side + y
        else:
            dst = x * side + (y + step) % side
        perm.append((src, dst))
    return lax.ppermute(v, "xy", perm)


def ring4(piece, along, side, cut):
    from_left = chip_shift(piece, along, 1, side)
    from_right = chip_shift(piece, along, -1, side)
    size = piece.shape[cut] // 2
    far_a = chip_shift(lax.slice_in_dim(from_left, 0, size, axis=cut), along, 1, side)
    far_b = chip_shift(lax.slice_in_dim(from_right, size, 2 * size, axis=cut), along, -1, side)
    far = jnp.concatenate([far_a, far_b], axis=cut)
    return jnp.stack([piece, from_right, far, from_left], axis=0)


def gather_torus(v, side, cut):
    size = v.shape[cut] // 2
    a = lax.slice_in_dim(v, 0, size, axis=cut)
    b = lax.slice_in_dim(v, size, 2 * size, axis=cut)
    a_l, a_r, a_f = (chip_shift(a, 0, k, side) for k in (1, -1, 2))
    b_l, b_r, b_f = (chip_shift(b, 1, k, side) for k in (1, -1, 2))
    a_l, a_r, a_f, b_l, b_r, b_f = lax.optimization_barrier((a_l, a_r, a_f, b_l, b_r, b_f))
    row_x = jnp.stack([a, a_r, a_f, a_l], axis=0)
    col_y = jnp.stack([b, b_r, b_f, b_l], axis=0)
    ra_l, ra_r = chip_shift(row_x, 1, 1, side), chip_shift(row_x, 1, -1, side)
    cb_l, cb_r = chip_shift(col_y, 0, 1, side), chip_shift(col_y, 0, -1, side)
    ra_l, ra_r, cb_l, cb_r = lax.optimization_barrier((ra_l, ra_r, cb_l, cb_r))
    ra_f = jnp.concatenate(
        [chip_shift(ra_l[:2], 1, 1, side), chip_shift(ra_r[2:], 1, -1, side)], axis=0
    )
    cb_f = jnp.concatenate(
        [chip_shift(cb_l[:2], 0, 1, side), chip_shift(cb_r[2:], 0, -1, side)], axis=0
    )
    ra_f, cb_f = lax.optimization_barrier((ra_f, cb_f))
    first_all = jnp.swapaxes(jnp.stack([row_x, ra_r, ra_f, ra_l], axis=0), 0, 1)
    second_all = jnp.stack([col_y, cb_r, cb_f, cb_l], axis=0)
    return jnp.concatenate([first_all, second_all], axis=cut + 2)


def gather_mixed(v, side, cut, cx, cy):
    width = v.shape[-1] // 2
    by_ring = lax.all_gather(v[..., :width], "xy", axis=0, tiled=False)
    by_ring = to_relative(by_ring.reshape((side, side) + by_ring.shape[1:]), cx, cy)
    by_torus = gather_torus(v[..., width:], side, cut)
    return jnp.concatenate([by_ring, by_torus], axis=-1)


def ring_reduce(q, along, side):
    size = q.shape[-1] // 2
    from_left = chip_shift(q[2][..., :size], along, 1, side)
    from_right = chip_shift(q[2][..., size:], along, -1, side)
    to_right = jnp.concatenate([q[1][..., :size] + from_left, q[1][..., size:]], axis=-1)
    to_left = jnp.concatenate([q[3][..., :size], q[3][..., size:] + from_right], axis=-1)
    return q[0] + chip_shift(to_right, along, 1, side) + chip_shift(to_left, along, -1, side)


def direct_reduce(q, along, side):
    return (
        q[0]
        + chip_shift(q[1], along, 1, side)
        + chip_shift(q[3], along, -1, side)
        + chip_shift(q[2], along, 2, side)
    )


def reduce_torus(s_rel, side):
    size = s_rel.shape[-1] // 2
    first = jnp.swapaxes(s_rel[..., :size], 0, 1)
    second = s_rel[..., size:]
    first_sum = direct_reduce(ring_reduce(first, 1, side), 0, side)
    second_sum = direct_reduce(ring_reduce(second, 0, side), 1, side)
    return jnp.concatenate([first_sum, second_sum], axis=-1)


def swap_core(v):
    return lax.ppermute(v, "core", [(0, 1), (1, 0)])


def to_absolute(v, cx, cy):
    return jnp.roll(jnp.roll(v, cx, axis=0), cy, axis=1)


def to_relative(v, cx, cy):
    return jnp.roll(jnp.roll(v, -cx, axis=0), -cy, axis=1)


def local(
    tokens, ln_gain, ln_bias, w_qkv, w_out, layer_scale, w_merge, segment_ids, grid_sizes, owners
):
    chips = lax.axis_size("xy")
    side = 4
    batch_count = lax.axis_size("dp")
    chip = lax.axis_index("xy")
    core = lax.axis_index("core")
    cx = chip // side
    cy = chip % side
    seg_row = segment_ids[0]
    grid_row = grid_sizes[0]
    owner_row = owners[0, :, 0]
    seq_len = seg_row.shape[0]
    block = tokens.shape[1]
    model_width = tokens.shape[2]
    col_width = layer_scale.shape[0]
    half_rows = chips * block
    merged_rows = seq_len // 4
    tensor_count = 2 * chips
    own_cap = 4
    out_width = w_merge.shape[2]

    x_rel = gather_mixed(tokens[0], side, 1, cx, cy)
    w_partner = swap_core(w_qkv)
    wo_partner = swap_core(w_out)
    ls_partner = swap_core(layer_scale)

    offs = jnp.arange(side, dtype=jnp.int32)
    chip_of = ((cx + offs)[:, None] % side) * side + (cy + offs)[None, :] % side
    within = jnp.arange(block, dtype=jnp.int32)
    pos_mine = ((2 * chip_of + core)[:, :, None] * block + within).reshape(half_rows)
    pos_other = ((2 * chip_of + 1 - core)[:, :, None] * block + within).reshape(half_rows)
    seg_cores = seg_row.reshape(side, side, 2, block)
    seg_mine = to_relative(seg_cores[:, :, core], cx, cy).reshape(half_rows)
    seg_other = to_relative(seg_cores[:, :, 1 - core], cx, cy).reshape(half_rows)
    cos_t, sin_t = rope_tables(seg_mine, pos_mine, grid_row)

    x_rows = x_rel.reshape(half_rows, model_width)
    normed = layer_norm(x_rows, ln_gain, ln_bias)
    w_both = jnp.stack([w_qkv, w_partner], axis=2)
    qkv_weight = w_both.reshape(model_width, 3 * 2 * HEAD_DIM)
    product = jnp.dot(normed, qkv_weight, preferred_element_type=jnp.float32).reshape(
        half_rows, 3, 2, HEAD_DIM
    )
    cos_rows = cos_t[:, None, :]
    sin_rows = sin_t[:, None, :]
    q_here = rotate(product[:, 0], cos_rows, sin_rows).astype(jnp.bfloat16)
    k_here = rotate(product[:, 1], cos_rows, sin_rows).astype(jnp.bfloat16)
    v_here = product[:, 2].astype(jnp.bfloat16)
    kv_here = jnp.stack([k_here, v_here], axis=1)
    kv_other = swap_core(kv_here)[:, :, ::-1]
    kv_all = jnp.concatenate([kv_here, kv_other], axis=0)
    key_all = kv_all[:, 0]
    value_all = kv_all[:, 1]
    seg_keys = jnp.concatenate([seg_mine, seg_other], axis=0)

    def one_head(h):
        return attend(q_here[:, h], seg_mine, key_all[:, h], value_all[:, h], seg_keys)

    context_rel = jnp.stack([one_head(0), one_head(1)], axis=1).reshape(
        side, side, block, 2 * HEAD_DIM
    )
    context_abs = to_absolute(context_rel, cx, cy).reshape(half_rows, 2 * HEAD_DIM)
    context_g = gather_mixed(context_abs, side, 0, cx, cy)
    context = jnp.transpose(context_g, (2, 0, 1, 3)).reshape(half_rows, model_width)
    wo_both = jnp.concatenate([w_out, wo_partner], axis=1).reshape(
        side, side, 2, HEAD_DIM, 2 * col_width
    )
    wo_rel = to_relative(wo_both, cx, cy)
    wo_rel = jnp.where(core == 0, wo_rel, wo_rel[:, :, ::-1])
    wo_rows = wo_rel.reshape(model_width, 2 * col_width)
    mixed = jnp.dot(context, wo_rows, preferred_element_type=jnp.float32)
    group_mine = 2 * chip + core
    group_other = 2 * chip + 1 - core
    x_mine = lax.dynamic_slice_in_dim(x_rel, group_mine * col_width, col_width, 3)
    x_other = lax.dynamic_slice_in_dim(x_rel, group_other * col_width, col_width, 3)
    x_cols = to_absolute(jnp.concatenate([x_mine, x_other], axis=3), cx, cy).reshape(
        half_rows, 2 * col_width
    )
    ls_both = jnp.concatenate([layer_scale, ls_partner], axis=0)
    hidden_here = (x_cols.astype(jnp.float32) + ls_both * mixed).astype(jnp.bfloat16)
    hidden_recv = swap_core(hidden_here[:, col_width:])
    hidden = jnp.concatenate([hidden_here[:, :col_width], hidden_recv], axis=0)

    sources, is_valid = merge_sources(grid_row, merged_rows)
    src_block = sources // block
    src_index = (
        (src_block % 2 != core).astype(jnp.int32) * half_rows
        + (src_block // 2) * block
        + sources % block
    )
    merged = jnp.where(
        is_valid[:, None, None], hidden[src_index], jnp.zeros((), jnp.bfloat16)
    ).reshape(merged_rows, 4 * col_width)
    merge_weight = w_merge.reshape(4 * col_width, out_width)
    ranks = owner_ranks(owner_row)
    owner_dp = owner_row // tensor_count
    owner_t = owner_row % tensor_count
    slot_keys = owner_t * (batch_count * own_cap) + owner_dp * own_cap + ranks
    slot_ids = jnp.arange(tensor_count * batch_count * own_cap, dtype=jnp.int32)
    placing = (slot_ids[:, None] == slot_keys[None, :]).astype(jnp.bfloat16)
    by_owner = jnp.dot(placing, merged, preferred_element_type=jnp.float32).astype(jnp.bfloat16)
    group_part = jnp.dot(by_owner, merge_weight, preferred_element_type=jnp.float32).astype(
        jnp.bfloat16
    )
    part32 = group_part.astype(jnp.float32).reshape(chips, 2, batch_count * own_cap, out_width)
    part_keep = jnp.where(core == 0, part32[:, 0], part32[:, 1])
    part_send = jnp.where(core == 0, part32[:, 1], part32[:, 0])
    part_chip = part_keep + swap_core(part_send)
    s_rel = to_relative(
        part_chip.reshape(side, side, batch_count * own_cap, out_width), cx, cy
    )
    mine = reduce_torus(s_rel, side)
    outgoing = mine.astype(jnp.bfloat16).reshape(batch_count, own_cap, out_width)
    plane = lax.axis_index("dp")
    out_rel = jnp.roll(outgoing, -plane, axis=0)
    recv = [out_rel[0]]
    for step in range(1, batch_count):
        perm = [(d, (d + step) % batch_count) for d in range(batch_count)]
        recv.append(lax.ppermute(out_rel[step], "dp", perm))
    incoming = jnp.roll(jnp.stack(recv, axis=0)[::-1], plane + 1, axis=0)
    return incoming.reshape(1, batch_count * own_cap, out_width)


def solution(mesh):
    devices = mesh.devices.reshape(mesh.shape["dp"], -1, 2)
    mesh3 = Mesh(devices, ("dp", "xy", "core"))
    tp = ("xy", "core")
    in_specs = (
        P("dp", tp, None),
        P(),
        P(),
        P(None, None, tp),
        P(None, tp),
        P(tp),
        P(None, tp, None),
        P("dp", None),
        P("dp", None, None),
        P("dp", None, None),
    )
    out_specs = P("dp", tp, None)
    return jax.shard_map(local, mesh=mesh3, in_specs=in_specs, out_specs=out_specs, check_vma=False)
```

```python
import jax
import jax.numpy as jnp
from jax import lax
from jax.sharding import Mesh
from jax.sharding import PartitionSpec as P

HEAD_DIM = 128
IMGS = 3
REG = 5


norm_eps = 1e-06


def layer_norm(row_data, gain_vec, shift_vec):
    values = row_data.astype(jnp.float32)
    center = values - jnp.mean(values, axis=-1, keepdims=True)
    spread = jnp.mean(center * center, axis=-1, keepdims=True)
    return (center * lax.rsqrt(spread + norm_eps) * gain_vec + shift_vec).astype(jnp.bfloat16)


def image_layout(grid_row):
    heights = grid_row[:, 0]
    widths = grid_row[:, 1]
    lengths = REG + heights * widths
    starts = jnp.cumsum(lengths) - lengths
    counts = heights // 2 * (widths // 2)
    merged_end = jnp.cumsum(counts)
    return (heights, widths, starts, merged_end - counts, merged_end)


def pick_rows(onehot, lookup):
    return jnp.sum(onehot * lookup[None, :], axis=1)


def rope_tables(seg_at, position, grid_row):
    heights, widths, starts, first_merged, last_merged = image_layout(grid_row)
    image_ids = jnp.arange(IMGS, dtype=jnp.int32)
    onehot = (seg_at[:, None] == image_ids[None, :]).astype(jnp.int32)
    is_image = jnp.sum(onehot, axis=1) > 0
    in_image = position - pick_rows(onehot, starts) - REG
    is_patch = is_image & (in_image >= 0)
    row_width = jnp.maximum(pick_rows(onehot, widths), 1)
    col_height = jnp.maximum(pick_rows(onehot, heights), 1)
    clipped = jnp.maximum(in_image, 0)
    coord_y = (
        2.0 * ((clipped // row_width).astype(jnp.float32) + 0.5) / col_height.astype(jnp.float32)
        - 1.0
    )
    coord_x = (
        2.0 * ((clipped % row_width).astype(jnp.float32) + 0.5) / row_width.astype(jnp.float32)
        - 1.0
    )
    quarter = HEAD_DIM // 4
    pair_ids = jnp.arange(HEAD_DIM // 2, dtype=jnp.int32)
    omegas = 100.0 ** ((pair_ids % quarter).astype(jnp.float32) / quarter)
    coord_all = jnp.where(pair_ids[None, :] < quarter, coord_y[:, None], coord_x[:, None])
    angles = jnp.where(is_patch[:, None], jnp.pi * omegas[None, :] * coord_all, 0.0)
    return (jnp.cos(angles), jnp.sin(angles))


def rotate(values, cos_rows, sin_rows):
    half_dim = values.shape[-1] // 2
    first_half = values[..., :half_dim]
    second_half = values[..., half_dim:]
    return jnp.concatenate(
        [
            first_half * cos_rows - second_half * sin_rows,
            second_half * cos_rows + first_half * sin_rows,
        ],
        axis=-1,
    )


def merge_sources(grid_row, merged_rows):
    heights, widths, starts, first_merged, last_merged = image_layout(grid_row)
    row_ids = jnp.arange(merged_rows, dtype=jnp.int32)
    onehot = (
        (row_ids[:, None] >= first_merged[None, :]) & (row_ids[:, None] < last_merged[None, :])
    ).astype(jnp.int32)
    is_valid = jnp.sum(onehot, axis=1) > 0
    row_width = pick_rows(onehot, widths)
    half_width = jnp.maximum(row_width // 2, 1)
    in_image = row_ids - pick_rows(onehot, first_merged)
    corner = (
        pick_rows(onehot, starts)
        + REG
        + 2 * (in_image // half_width) * row_width
        + 2 * (in_image % half_width)
    )
    offsets = jnp.stack(
        [jnp.zeros_like(row_width), jnp.ones_like(row_width), row_width, row_width + 1], axis=1
    )
    sources = jnp.where(is_valid[:, None], corner[:, None] + offsets, 0)
    return (sources, is_valid)


def attend(query_rows, query_seg, key_rows, value_rows, key_seg):
    scores = lax.dot_general(
        query_rows, key_rows, (((1,), (1,)), ((), ())), preferred_element_type=jnp.float32
    ) * HEAD_DIM ** (-0.5)
    scores = jnp.where(query_seg[:, None] == key_seg[None, :], scores, -jnp.inf)
    shifted = jnp.exp(scores - jnp.max(scores, axis=1, keepdims=True))
    weights = (shifted / jnp.sum(shifted, axis=1, keepdims=True)).astype(jnp.bfloat16)
    return jnp.dot(weights, value_rows, preferred_element_type=jnp.float32).astype(jnp.bfloat16)


def owner_ranks(owner_row):
    rows = owner_row.shape[0]
    same = owner_row[:, None] == owner_row[None, :]
    earlier = jnp.arange(rows)[None, :] < jnp.arange(rows)[:, None]
    return jnp.sum((same & earlier).astype(jnp.int32), axis=1)


def chip_shift(v, along, step, side):
    perm = []
    for src in range(side * side):
        x, y = src // side, src % side
        if along == 0:
            dst = ((x + step) % side) * side + y
        else:
            dst = x * side + (y + step) % side
        perm.append((src, dst))
    return lax.ppermute(v, "xy", perm)


def ring4(piece, along, side, cut):
    from_left = chip_shift(piece, along, 1, side)
    from_right = chip_shift(piece, along, -1, side)
    size = piece.shape[cut] // 2
    far_a = chip_shift(lax.slice_in_dim(from_left, 0, size, axis=cut), along, 1, side)
    far_b = chip_shift(lax.slice_in_dim(from_right, size, 2 * size, axis=cut), along, -1, side)
    far = jnp.concatenate([far_a, far_b], axis=cut)
    return jnp.stack([piece, from_right, far, from_left], axis=0)


def gather_torus(v, side, cut):
    size = v.shape[cut] // 2
    a = lax.slice_in_dim(v, 0, size, axis=cut)
    b = lax.slice_in_dim(v, size, 2 * size, axis=cut)
    a_l, a_r, a_f = (chip_shift(a, 0, k, side) for k in (1, -1, 2))
    b_l, b_r, b_f = (chip_shift(b, 1, k, side) for k in (1, -1, 2))
    a_l, a_r, a_f, b_l, b_r, b_f = lax.optimization_barrier((a_l, a_r, a_f, b_l, b_r, b_f))
    row_x = jnp.stack([a, a_r, a_f, a_l], axis=0)
    col_y = jnp.stack([b, b_r, b_f, b_l], axis=0)
    ra_l, ra_r = chip_shift(row_x, 1, 1, side), chip_shift(row_x, 1, -1, side)
    cb_l, cb_r = chip_shift(col_y, 0, 1, side), chip_shift(col_y, 0, -1, side)
    ra_l, ra_r, cb_l, cb_r = lax.optimization_barrier((ra_l, ra_r, cb_l, cb_r))
    ra_f = jnp.concatenate(
        [chip_shift(ra_l[:2], 1, 1, side), chip_shift(ra_r[2:], 1, -1, side)], axis=0
    )
    cb_f = jnp.concatenate(
        [chip_shift(cb_l[:2], 0, 1, side), chip_shift(cb_r[2:], 0, -1, side)], axis=0
    )
    ra_f, cb_f = lax.optimization_barrier((ra_f, cb_f))
    first_all = jnp.swapaxes(jnp.stack([row_x, ra_r, ra_f, ra_l], axis=0), 0, 1)
    second_all = jnp.stack([col_y, cb_r, cb_f, cb_l], axis=0)
    return jnp.concatenate([first_all, second_all], axis=cut + 2)


def gather_pieces(v, side, cut, work):
    size = v.shape[cut] // 2
    a = lax.slice_in_dim(v, 0, size, axis=cut)
    b = lax.slice_in_dim(v, size, 2 * size, axis=cut)
    a_l, a_r, a_f = (chip_shift(a, 0, k, side) for k in (1, -1, 2))
    b_l, b_r, b_f = (chip_shift(b, 1, k, side) for k in (1, -1, 2))
    a_l, a_r, a_f, b_l, b_r, b_f = lax.optimization_barrier((a_l, a_r, a_f, b_l, b_r, b_f))
    row_x = jnp.stack([a, a_r, a_f, a_l], axis=0)
    col_y = jnp.stack([b, b_r, b_f, b_l], axis=0)
    ra_l, ra_r = chip_shift(row_x, 1, 1, side), chip_shift(row_x, 1, -1, side)
    cb_l, cb_r = chip_shift(col_y, 0, 1, side), chip_shift(col_y, 0, -1, side)
    early = (work(row_x), work(col_y))
    ra_l, ra_r, cb_l, cb_r, early = lax.optimization_barrier((ra_l, ra_r, cb_l, cb_r, early))
    ra_f = jnp.concatenate(
        [chip_shift(ra_l[:2], 1, 1, side), chip_shift(ra_r[2:], 1, -1, side)], axis=0
    )
    cb_f = jnp.concatenate(
        [chip_shift(cb_l[:2], 0, 1, side), chip_shift(cb_r[2:], 0, -1, side)], axis=0
    )
    middle = (work(ra_r), work(ra_l), work(cb_r), work(cb_l))
    ra_f, cb_f, middle = lax.optimization_barrier((ra_f, cb_f, middle))
    late = (work(ra_f), work(cb_f))
    pieces = ([row_x, ra_r, ra_f, ra_l], [col_y, cb_r, cb_f, cb_l])
    works = (
        [early[0], middle[0], late[0], middle[1]],
        [early[1], middle[2], late[1], middle[3]],
    )
    return pieces, works


def assemble(a_by_dy, b_by_dx, cut):
    first_all = jnp.swapaxes(jnp.stack(a_by_dy, axis=0), 0, 1)
    second_all = jnp.stack(b_by_dx, axis=0)
    return jnp.concatenate([first_all, second_all], axis=cut + 2)


def ring_reduce(q, along, side):
    size = q.shape[-1] // 2
    from_left = chip_shift(q[2][..., :size], along, 1, side)
    from_right = chip_shift(q[2][..., size:], along, -1, side)
    to_right = jnp.concatenate([q[1][..., :size] + from_left, q[1][..., size:]], axis=-1)
    to_left = jnp.concatenate([q[3][..., :size], q[3][..., size:] + from_right], axis=-1)
    return q[0] + chip_shift(to_right, along, 1, side) + chip_shift(to_left, along, -1, side)


def direct_reduce(q, along, side):
    return (
        q[0]
        + chip_shift(q[1], along, 1, side)
        + chip_shift(q[3], along, -1, side)
        + chip_shift(q[2], along, 2, side)
    )


def reduce_torus(s_rel, side):
    size = s_rel.shape[-1] // 2
    first = jnp.swapaxes(s_rel[..., :size], 0, 1)
    second = s_rel[..., size:]
    first_sum = direct_reduce(ring_reduce(first, 1, side), 0, side)
    second_sum = direct_reduce(ring_reduce(second, 0, side), 1, side)
    return jnp.concatenate([first_sum, second_sum], axis=-1)


def swap_core(v):
    return lax.ppermute(v, "core", [(0, 1), (1, 0)])


def to_absolute(v, cx, cy):
    return jnp.roll(jnp.roll(v, cx, axis=0), cy, axis=1)


def to_relative(v, cx, cy):
    return jnp.roll(jnp.roll(v, -cx, axis=0), -cy, axis=1)


def local(
    tokens, ln_gain, ln_bias, w_qkv, w_out, layer_scale, w_merge, segment_ids, grid_sizes, owners
):
    chips = lax.axis_size("xy")
    side = 4
    batch_count = lax.axis_size("dp")
    chip = lax.axis_index("xy")
    core = lax.axis_index("core")
    cx = chip // side
    cy = chip % side
    seg_row = segment_ids[0]
    grid_row = grid_sizes[0]
    owner_row = owners[0, :, 0]
    seq_len = seg_row.shape[0]
    block = tokens.shape[1]
    model_width = tokens.shape[2]
    col_width = layer_scale.shape[0]
    half_rows = chips * block
    merged_rows = seq_len // 4
    tensor_count = 2 * chips
    own_cap = 4
    out_width = w_merge.shape[2]

    w_partner = swap_core(w_qkv)
    w_mine_flat = w_qkv.reshape(model_width, 3 * HEAD_DIM)
    w_partner_flat = w_partner.reshape(model_width, 3 * HEAD_DIM)

    def project(piece):
        lead = piece.shape[:-1]
        rows = layer_norm(piece.reshape(-1, model_width), ln_gain, ln_bias)
        mine = jnp.dot(rows, w_mine_flat, preferred_element_type=jnp.float32)
        other = jnp.dot(rows, w_partner_flat, preferred_element_type=jnp.float32)
        out = jnp.stack(
            [mine.reshape(-1, 3, HEAD_DIM), other.reshape(-1, 3, HEAD_DIM)], axis=2
        )
        return out.reshape(lead + (3 * 2 * HEAD_DIM,))

    (a_pieces, b_pieces), (qkv_a, qkv_b) = gather_pieces(tokens[0], side, 0, project)
    x_rel = assemble(a_pieces, b_pieces, 0)
    wo_partner = swap_core(w_out)
    ls_partner = swap_core(layer_scale)

    offs = jnp.arange(side, dtype=jnp.int32)
    chip_of = ((cx + offs)[:, None] % side) * side + (cy + offs)[None, :] % side
    within = jnp.arange(block, dtype=jnp.int32)
    pos_mine = ((2 * chip_of + core)[:, :, None] * block + within).reshape(half_rows)
    pos_other = ((2 * chip_of + 1 - core)[:, :, None] * block + within).reshape(half_rows)
    seg_cores = seg_row.reshape(side, side, 2, block)
    seg_mine = to_relative(seg_cores[:, :, core], cx, cy).reshape(half_rows)
    seg_other = to_relative(seg_cores[:, :, 1 - core], cx, cy).reshape(half_rows)
    cos_t, sin_t = rope_tables(seg_mine, pos_mine, grid_row)

    product = assemble(qkv_a, qkv_b, 0).reshape(half_rows, 3, 2, HEAD_DIM)
    cos_rows = cos_t[:, None, :]
    sin_rows = sin_t[:, None, :]
    q_here = rotate(product[:, 0], cos_rows, sin_rows).astype(jnp.bfloat16)
    k_here = rotate(product[:, 1], cos_rows, sin_rows).astype(jnp.bfloat16)
    v_here = product[:, 2].astype(jnp.bfloat16)
    kv_here = jnp.stack([k_here, v_here], axis=1)
    kv_other = swap_core(kv_here)[:, :, ::-1]
    kv_all = jnp.concatenate([kv_here, kv_other], axis=0)
    key_all = kv_all[:, 0]
    value_all = kv_all[:, 1]
    seg_keys = jnp.concatenate([seg_mine, seg_other], axis=0)

    def one_head(h):
        return attend(q_here[:, h], seg_mine, key_all[:, h], value_all[:, h], seg_keys)

    context_rel = jnp.stack([one_head(0), one_head(1)], axis=1).reshape(
        side, side, block, 2 * HEAD_DIM
    )
    context_abs = to_absolute(context_rel, cx, cy).reshape(half_rows, 2 * HEAD_DIM)
    context_g = gather_torus(context_abs, side, 0)
    context = jnp.transpose(context_g, (2, 0, 1, 3)).reshape(half_rows, model_width)
    wo_both = jnp.concatenate([w_out, wo_partner], axis=1).reshape(
        side, side, 2, HEAD_DIM, 2 * col_width
    )
    wo_rel = to_relative(wo_both, cx, cy)
    wo_rel = jnp.where(core == 0, wo_rel, wo_rel[:, :, ::-1])
    wo_rows = wo_rel.reshape(model_width, 2 * col_width)
    mixed = jnp.dot(context, wo_rows, preferred_element_type=jnp.float32)
    group_mine = 2 * chip + core
    group_other = 2 * chip + 1 - core
    x_mine = lax.dynamic_slice_in_dim(x_rel, group_mine * col_width, col_width, 3)
    x_other = lax.dynamic_slice_in_dim(x_rel, group_other * col_width, col_width, 3)
    x_cols = to_absolute(jnp.concatenate([x_mine, x_other], axis=3), cx, cy).reshape(
        half_rows, 2 * col_width
    )
    ls_both = jnp.concatenate([layer_scale, ls_partner], axis=0)
    hidden_here = (x_cols.astype(jnp.float32) + ls_both * mixed).astype(jnp.bfloat16)
    hidden_recv = swap_core(hidden_here[:, col_width:])
    hidden = jnp.concatenate([hidden_here[:, :col_width], hidden_recv], axis=0)

    sources, is_valid = merge_sources(grid_row, merged_rows)
    src_block = sources // block
    src_index = (
        (src_block % 2 != core).astype(jnp.int32) * half_rows
        + (src_block // 2) * block
        + sources % block
    )
    merged = jnp.where(
        is_valid[:, None, None], hidden[src_index], jnp.zeros((), jnp.bfloat16)
    ).reshape(merged_rows, 4 * col_width)
    merge_weight = w_merge.reshape(4 * col_width, out_width)
    ranks = owner_ranks(owner_row)
    owner_dp = owner_row // tensor_count
    owner_t = owner_row % tensor_count
    slot_keys = owner_t * (batch_count * own_cap) + owner_dp * own_cap + ranks
    slot_ids = jnp.arange(tensor_count * batch_count * own_cap, dtype=jnp.int32)
    placing = (slot_ids[:, None] == slot_keys[None, :]).astype(jnp.bfloat16)
    by_owner = jnp.dot(placing, merged, preferred_element_type=jnp.float32).astype(jnp.bfloat16)
    group_part = jnp.dot(by_owner, merge_weight, preferred_element_type=jnp.float32).astype(
        jnp.bfloat16
    )
    part32 = group_part.astype(jnp.float32).reshape(chips, 2, batch_count * own_cap, out_width)
    part_keep = jnp.where(core == 0, part32[:, 0], part32[:, 1])
    part_send = jnp.where(core == 0, part32[:, 1], part32[:, 0])
    part_chip = part_keep + swap_core(part_send)
    s_rel = to_relative(
        part_chip.reshape(side, side, batch_count * own_cap, out_width), cx, cy
    )
    mine = reduce_torus(s_rel, side)
    outgoing = mine.astype(jnp.bfloat16).reshape(batch_count, own_cap, out_width)
    plane = lax.axis_index("dp")
    out_rel = jnp.roll(outgoing, -plane, axis=0)
    recv = [out_rel[0]]
    for step in range(1, batch_count):
        perm = [(d, (d + step) % batch_count) for d in range(batch_count)]
        recv.append(lax.ppermute(out_rel[step], "dp", perm))
    incoming = jnp.roll(jnp.stack(recv, axis=0)[::-1], plane + 1, axis=0)
    return incoming.reshape(1, batch_count * own_cap, out_width)


def solution(mesh):
    devices = mesh.devices.reshape(mesh.shape["dp"], -1, 2)
    mesh3 = Mesh(devices, ("dp", "xy", "core"))
    tp = ("xy", "core")
    in_specs = (
        P("dp", tp, None),
        P(),
        P(),
        P(None, None, tp),
        P(None, tp),
        P(tp),
        P(None, tp, None),
        P("dp", None),
        P("dp", None, None),
        P("dp", None, None),
    )
    out_specs = P("dp", tp, None)
    return jax.shard_map(local, mesh=mesh3, in_specs=in_specs, out_specs=out_specs, check_vma=False)
```

```python
import jax
import jax.numpy as jnp
from jax import lax
from jax.sharding import Mesh
from jax.sharding import PartitionSpec as P

HEAD_DIM = 128
IMGS = 3
REG = 5


norm_eps = 1e-06


def layer_norm(row_data, gain_vec, shift_vec):
    values = row_data.astype(jnp.float32)
    center = values - jnp.mean(values, axis=-1, keepdims=True)
    spread = jnp.mean(center * center, axis=-1, keepdims=True)
    return (center * lax.rsqrt(spread + norm_eps) * gain_vec + shift_vec).astype(jnp.bfloat16)


def image_layout(grid_row):
    heights = grid_row[:, 0]
    widths = grid_row[:, 1]
    lengths = REG + heights * widths
    starts = jnp.cumsum(lengths) - lengths
    counts = heights // 2 * (widths // 2)
    merged_end = jnp.cumsum(counts)
    return (heights, widths, starts, merged_end - counts, merged_end)


def pick_rows(onehot, lookup):
    return jnp.sum(onehot * lookup[None, :], axis=1)


def rope_tables(seg_at, position, grid_row):
    heights, widths, starts, first_merged, last_merged = image_layout(grid_row)
    image_ids = jnp.arange(IMGS, dtype=jnp.int32)
    onehot = (seg_at[:, None] == image_ids[None, :]).astype(jnp.int32)
    is_image = jnp.sum(onehot, axis=1) > 0
    in_image = position - pick_rows(onehot, starts) - REG
    is_patch = is_image & (in_image >= 0)
    row_width = jnp.maximum(pick_rows(onehot, widths), 1)
    col_height = jnp.maximum(pick_rows(onehot, heights), 1)
    clipped = jnp.maximum(in_image, 0)
    coord_y = (
        2.0 * ((clipped // row_width).astype(jnp.float32) + 0.5) / col_height.astype(jnp.float32)
        - 1.0
    )
    coord_x = (
        2.0 * ((clipped % row_width).astype(jnp.float32) + 0.5) / row_width.astype(jnp.float32)
        - 1.0
    )
    quarter = HEAD_DIM // 4
    pair_ids = jnp.arange(HEAD_DIM // 2, dtype=jnp.int32)
    omegas = 100.0 ** ((pair_ids % quarter).astype(jnp.float32) / quarter)
    coord_all = jnp.where(pair_ids[None, :] < quarter, coord_y[:, None], coord_x[:, None])
    angles = jnp.where(is_patch[:, None], jnp.pi * omegas[None, :] * coord_all, 0.0)
    return (jnp.cos(angles), jnp.sin(angles))


def rotate(values, cos_rows, sin_rows):
    half_dim = values.shape[-1] // 2
    first_half = values[..., :half_dim]
    second_half = values[..., half_dim:]
    return jnp.concatenate(
        [
            first_half * cos_rows - second_half * sin_rows,
            second_half * cos_rows + first_half * sin_rows,
        ],
        axis=-1,
    )


def merge_sources(grid_row, merged_rows):
    heights, widths, starts, first_merged, last_merged = image_layout(grid_row)
    row_ids = jnp.arange(merged_rows, dtype=jnp.int32)
    onehot = (
        (row_ids[:, None] >= first_merged[None, :]) & (row_ids[:, None] < last_merged[None, :])
    ).astype(jnp.int32)
    is_valid = jnp.sum(onehot, axis=1) > 0
    row_width = pick_rows(onehot, widths)
    half_width = jnp.maximum(row_width // 2, 1)
    in_image = row_ids - pick_rows(onehot, first_merged)
    corner = (
        pick_rows(onehot, starts)
        + REG
        + 2 * (in_image // half_width) * row_width
        + 2 * (in_image % half_width)
    )
    offsets = jnp.stack(
        [jnp.zeros_like(row_width), jnp.ones_like(row_width), row_width, row_width + 1], axis=1
    )
    sources = jnp.where(is_valid[:, None], corner[:, None] + offsets, 0)
    return (sources, is_valid)


def attend(query_rows, query_seg, key_rows, value_rows, key_seg):
    scores = lax.dot_general(
        query_rows, key_rows, (((1,), (1,)), ((), ())), preferred_element_type=jnp.float32
    ) * HEAD_DIM ** (-0.5)
    scores = jnp.where(query_seg[:, None] == key_seg[None, :], scores, -jnp.inf)
    shifted = jnp.exp(scores - jnp.max(scores, axis=1, keepdims=True))
    weights = (shifted / jnp.sum(shifted, axis=1, keepdims=True)).astype(jnp.bfloat16)
    return jnp.dot(weights, value_rows, preferred_element_type=jnp.float32).astype(jnp.bfloat16)


def owner_ranks(owner_row):
    rows = owner_row.shape[0]
    same = owner_row[:, None] == owner_row[None, :]
    earlier = jnp.arange(rows)[None, :] < jnp.arange(rows)[:, None]
    return jnp.sum((same & earlier).astype(jnp.int32), axis=1)


def chip_shift(v, along, step, side):
    perm = []
    for src in range(side * side):
        x, y = src // side, src % side
        if along == 0:
            dst = ((x + step) % side) * side + y
        else:
            dst = x * side + (y + step) % side
        perm.append((src, dst))
    return lax.ppermute(v, "xy", perm)


def ring4(piece, along, side, cut):
    from_left = chip_shift(piece, along, 1, side)
    from_right = chip_shift(piece, along, -1, side)
    size = piece.shape[cut] // 2
    far_a = chip_shift(lax.slice_in_dim(from_left, 0, size, axis=cut), along, 1, side)
    far_b = chip_shift(lax.slice_in_dim(from_right, size, 2 * size, axis=cut), along, -1, side)
    far = jnp.concatenate([far_a, far_b], axis=cut)
    return jnp.stack([piece, from_right, far, from_left], axis=0)


def gather_torus(v, side, cut):
    size = v.shape[cut] // 2
    a = lax.slice_in_dim(v, 0, size, axis=cut)
    b = lax.slice_in_dim(v, size, 2 * size, axis=cut)
    a_l, a_r, a_f = (chip_shift(a, 0, k, side) for k in (1, -1, 2))
    b_l, b_r, b_f = (chip_shift(b, 1, k, side) for k in (1, -1, 2))
    a_l, a_r, a_f, b_l, b_r, b_f = lax.optimization_barrier((a_l, a_r, a_f, b_l, b_r, b_f))
    row_x = jnp.stack([a, a_r, a_f, a_l], axis=0)
    col_y = jnp.stack([b, b_r, b_f, b_l], axis=0)
    ra_l, ra_r = chip_shift(row_x, 1, 1, side), chip_shift(row_x, 1, -1, side)
    cb_l, cb_r = chip_shift(col_y, 0, 1, side), chip_shift(col_y, 0, -1, side)
    ra_l, ra_r, cb_l, cb_r = lax.optimization_barrier((ra_l, ra_r, cb_l, cb_r))
    ra_f = jnp.concatenate(
        [chip_shift(ra_l[:2], 1, 1, side), chip_shift(ra_r[2:], 1, -1, side)], axis=0
    )
    cb_f = jnp.concatenate(
        [chip_shift(cb_l[:2], 0, 1, side), chip_shift(cb_r[2:], 0, -1, side)], axis=0
    )
    ra_f, cb_f = lax.optimization_barrier((ra_f, cb_f))
    first_all = jnp.swapaxes(jnp.stack([row_x, ra_r, ra_f, ra_l], axis=0), 0, 1)
    second_all = jnp.stack([col_y, cb_r, cb_f, cb_l], axis=0)
    return jnp.concatenate([first_all, second_all], axis=cut + 2)


def send_bf16(v, along, step, side):
    return chip_shift(v.astype(jnp.bfloat16), along, step, side).astype(jnp.float32)


def ring_reduce(q, along, side):
    size = q.shape[-1] // 2
    from_left = send_bf16(q[2][..., :size], along, 1, side)
    from_right = send_bf16(q[2][..., size:], along, -1, side)
    to_right = jnp.concatenate([q[1][..., :size] + from_left, q[1][..., size:]], axis=-1)
    to_left = jnp.concatenate([q[3][..., :size], q[3][..., size:] + from_right], axis=-1)
    return q[0] + send_bf16(to_right, along, 1, side) + send_bf16(to_left, along, -1, side)


def direct_reduce(q, along, side):
    return (
        q[0]
        + send_bf16(q[1], along, 1, side)
        + send_bf16(q[3], along, -1, side)
        + send_bf16(q[2], along, 2, side)
    )


def reduce_torus(s_rel, side):
    size = s_rel.shape[-1] // 2
    first = jnp.swapaxes(s_rel[..., :size], 0, 1)
    second = s_rel[..., size:]
    first_sum = direct_reduce(ring_reduce(first, 1, side), 0, side)
    second_sum = direct_reduce(ring_reduce(second, 0, side), 1, side)
    return jnp.concatenate([first_sum, second_sum], axis=-1)


def swap_core(v):
    return lax.ppermute(v, "core", [(0, 1), (1, 0)])


def to_absolute(v, cx, cy):
    return jnp.roll(jnp.roll(v, cx, axis=0), cy, axis=1)


def to_relative(v, cx, cy):
    return jnp.roll(jnp.roll(v, -cx, axis=0), -cy, axis=1)


def local(
    tokens, ln_gain, ln_bias, w_qkv, w_out, layer_scale, w_merge, segment_ids, grid_sizes, owners
):
    chips = lax.axis_size("xy")
    side = 4
    batch_count = lax.axis_size("dp")
    chip = lax.axis_index("xy")
    core = lax.axis_index("core")
    cx = chip // side
    cy = chip % side
    seg_row = segment_ids[0]
    grid_row = grid_sizes[0]
    owner_row = owners[0, :, 0]
    seq_len = seg_row.shape[0]
    block = tokens.shape[1]
    model_width = tokens.shape[2]
    col_width = layer_scale.shape[0]
    half_rows = chips * block
    merged_rows = seq_len // 4
    tensor_count = 2 * chips
    own_cap = 4
    out_width = w_merge.shape[2]

    x_rel = gather_torus(tokens[0], side, 1)
    w_partner = swap_core(w_qkv)
    wo_partner = swap_core(w_out)
    ls_partner = swap_core(layer_scale)

    offs = jnp.arange(side, dtype=jnp.int32)
    chip_of = ((cx + offs)[:, None] % side) * side + (cy + offs)[None, :] % side
    within = jnp.arange(block, dtype=jnp.int32)
    pos_mine = ((2 * chip_of + core)[:, :, None] * block + within).reshape(half_rows)
    pos_other = ((2 * chip_of + 1 - core)[:, :, None] * block + within).reshape(half_rows)
    seg_cores = seg_row.reshape(side, side, 2, block)
    seg_mine = to_relative(seg_cores[:, :, core], cx, cy).reshape(half_rows)
    seg_other = to_relative(seg_cores[:, :, 1 - core], cx, cy).reshape(half_rows)
    cos_t, sin_t = rope_tables(seg_mine, pos_mine, grid_row)

    x_rows = x_rel.reshape(half_rows, model_width)
    normed = layer_norm(x_rows, ln_gain, ln_bias)
    w_both = jnp.stack([w_qkv, w_partner], axis=2)
    qkv_weight = w_both.reshape(model_width, 3 * 2 * HEAD_DIM)
    product = jnp.dot(normed, qkv_weight, preferred_element_type=jnp.float32).reshape(
        half_rows, 3, 2, HEAD_DIM
    )
    cos_rows = cos_t[:, None, :]
    sin_rows = sin_t[:, None, :]
    q_here = rotate(product[:, 0], cos_rows, sin_rows).astype(jnp.bfloat16)
    k_here = rotate(product[:, 1], cos_rows, sin_rows).astype(jnp.bfloat16)
    v_here = product[:, 2].astype(jnp.bfloat16)
    kv_here = jnp.stack([k_here, v_here], axis=1)
    kv_other = swap_core(kv_here)[:, :, ::-1]
    kv_all = jnp.concatenate([kv_here, kv_other], axis=0)
    key_all = kv_all[:, 0]
    value_all = kv_all[:, 1]
    seg_keys = jnp.concatenate([seg_mine, seg_other], axis=0)

    def one_head(h):
        return attend(q_here[:, h], seg_mine, key_all[:, h], value_all[:, h], seg_keys)

    context_rel = jnp.stack([one_head(0), one_head(1)], axis=1).reshape(
        side, side, block, 2 * HEAD_DIM
    )
    context_abs = to_absolute(context_rel, cx, cy).reshape(half_rows, 2 * HEAD_DIM)
    context_g = gather_torus(context_abs, side, 0)
    context = jnp.transpose(context_g, (2, 0, 1, 3)).reshape(half_rows, model_width)
    wo_both = jnp.concatenate([w_out, wo_partner], axis=1).reshape(
        side, side, 2, HEAD_DIM, 2 * col_width
    )
    wo_rel = to_relative(wo_both, cx, cy)
    wo_rel = jnp.where(core == 0, wo_rel, wo_rel[:, :, ::-1])
    wo_rows = wo_rel.reshape(model_width, 2 * col_width)
    mixed = jnp.dot(context, wo_rows, preferred_element_type=jnp.float32)
    group_mine = 2 * chip + core
    group_other = 2 * chip + 1 - core
    x_mine = lax.dynamic_slice_in_dim(x_rel, group_mine * col_width, col_width, 3)
    x_other = lax.dynamic_slice_in_dim(x_rel, group_other * col_width, col_width, 3)
    x_cols = to_absolute(jnp.concatenate([x_mine, x_other], axis=3), cx, cy).reshape(
        half_rows, 2 * col_width
    )
    ls_both = jnp.concatenate([layer_scale, ls_partner], axis=0)
    hidden_here = (x_cols.astype(jnp.float32) + ls_both * mixed).astype(jnp.bfloat16)
    hidden_recv = swap_core(hidden_here[:, col_width:])
    hidden = jnp.concatenate([hidden_here[:, :col_width], hidden_recv], axis=0)

    sources, is_valid = merge_sources(grid_row, merged_rows)
    src_block = sources // block
    src_index = (
        (src_block % 2 != core).astype(jnp.int32) * half_rows
        + (src_block // 2) * block
        + sources % block
    )
    merged = jnp.where(
        is_valid[:, None, None], hidden[src_index], jnp.zeros((), jnp.bfloat16)
    ).reshape(merged_rows, 4 * col_width)
    merge_weight = w_merge.reshape(4 * col_width, out_width)
    ranks = owner_ranks(owner_row)
    owner_dp = owner_row // tensor_count
    owner_t = owner_row % tensor_count
    slot_keys = owner_t * (batch_count * own_cap) + owner_dp * own_cap + ranks
    slot_ids = jnp.arange(tensor_count * batch_count * own_cap, dtype=jnp.int32)
    placing = (slot_ids[:, None] == slot_keys[None, :]).astype(jnp.bfloat16)
    by_owner = jnp.dot(placing, merged, preferred_element_type=jnp.float32).astype(jnp.bfloat16)
    group_part = jnp.dot(by_owner, merge_weight, preferred_element_type=jnp.float32).astype(
        jnp.bfloat16
    )
    part16 = group_part.reshape(chips, 2, batch_count * own_cap, out_width)
    part_keep = jnp.where(core == 0, part16[:, 0], part16[:, 1])
    part_send = jnp.where(core == 0, part16[:, 1], part16[:, 0])
    part_chip = part_keep.astype(jnp.float32) + swap_core(part_send).astype(jnp.float32)
    s_rel = to_relative(
        part_chip.reshape(side, side, batch_count * own_cap, out_width), cx, cy
    )
    mine = reduce_torus(s_rel, side)
    outgoing = mine.astype(jnp.bfloat16).reshape(batch_count, own_cap, out_width)
    plane = lax.axis_index("dp")
    out_rel = jnp.roll(outgoing, -plane, axis=0)
    recv = [out_rel[0]]
    for step in range(1, batch_count):
        perm = [(d, (d + step) % batch_count) for d in range(batch_count)]
        recv.append(lax.ppermute(out_rel[step], "dp", perm))
    incoming = jnp.roll(jnp.stack(recv, axis=0)[::-1], plane + 1, axis=0)
    return incoming.reshape(1, batch_count * own_cap, out_width)


def solution(mesh):
    devices = mesh.devices.reshape(mesh.shape["dp"], -1, 2)
    mesh3 = Mesh(devices, ("dp", "xy", "core"))
    tp = ("xy", "core")
    in_specs = (
        P("dp", tp, None),
        P(),
        P(),
        P(None, None, tp),
        P(None, tp),
        P(tp),
        P(None, tp, None),
        P("dp", None),
        P("dp", None, None),
        P("dp", None, None),
    )
    out_specs = P("dp", tp, None)
    return jax.shard_map(local, mesh=mesh3, in_specs=in_specs, out_specs=out_specs, check_vma=False)
```

```python
import jax
import jax.numpy as jnp
from jax import lax
from jax.sharding import Mesh
from jax.sharding import PartitionSpec as P

HEAD_DIM = 128
IMGS = 3
REG = 5


norm_eps = 1e-06


def layer_norm(row_data, gain_vec, shift_vec):
    values = row_data.astype(jnp.float32)
    center = values - jnp.mean(values, axis=-1, keepdims=True)
    spread = jnp.mean(center * center, axis=-1, keepdims=True)
    return (center * lax.rsqrt(spread + norm_eps) * gain_vec + shift_vec).astype(jnp.bfloat16)


def image_layout(grid_row):
    heights = grid_row[:, 0]
    widths = grid_row[:, 1]
    lengths = REG + heights * widths
    starts = jnp.cumsum(lengths) - lengths
    counts = heights // 2 * (widths // 2)
    merged_end = jnp.cumsum(counts)
    return (heights, widths, starts, merged_end - counts, merged_end)


def pick_rows(onehot, lookup):
    return jnp.sum(onehot * lookup[None, :], axis=1)


def rope_tables(seg_at, position, grid_row):
    heights, widths, starts, first_merged, last_merged = image_layout(grid_row)
    image_ids = jnp.arange(IMGS, dtype=jnp.int32)
    onehot = (seg_at[:, None] == image_ids[None, :]).astype(jnp.int32)
    is_image = jnp.sum(onehot, axis=1) > 0
    in_image = position - pick_rows(onehot, starts) - REG
    is_patch = is_image & (in_image >= 0)
    row_width = jnp.maximum(pick_rows(onehot, widths), 1)
    col_height = jnp.maximum(pick_rows(onehot, heights), 1)
    clipped = jnp.maximum(in_image, 0)
    coord_y = (
        2.0 * ((clipped // row_width).astype(jnp.float32) + 0.5) / col_height.astype(jnp.float32)
        - 1.0
    )
    coord_x = (
        2.0 * ((clipped % row_width).astype(jnp.float32) + 0.5) / row_width.astype(jnp.float32)
        - 1.0
    )
    quarter = HEAD_DIM // 4
    pair_ids = jnp.arange(HEAD_DIM // 2, dtype=jnp.int32)
    omegas = 100.0 ** ((pair_ids % quarter).astype(jnp.float32) / quarter)
    coord_all = jnp.where(pair_ids[None, :] < quarter, coord_y[:, None], coord_x[:, None])
    angles = jnp.where(is_patch[:, None], jnp.pi * omegas[None, :] * coord_all, 0.0)
    return (jnp.cos(angles), jnp.sin(angles))


def rotate(values, cos_rows, sin_rows):
    half_dim = values.shape[-1] // 2
    first_half = values[..., :half_dim]
    second_half = values[..., half_dim:]
    return jnp.concatenate(
        [
            first_half * cos_rows - second_half * sin_rows,
            second_half * cos_rows + first_half * sin_rows,
        ],
        axis=-1,
    )


def merge_sources(grid_row, merged_rows):
    heights, widths, starts, first_merged, last_merged = image_layout(grid_row)
    row_ids = jnp.arange(merged_rows, dtype=jnp.int32)
    onehot = (
        (row_ids[:, None] >= first_merged[None, :]) & (row_ids[:, None] < last_merged[None, :])
    ).astype(jnp.int32)
    is_valid = jnp.sum(onehot, axis=1) > 0
    row_width = pick_rows(onehot, widths)
    half_width = jnp.maximum(row_width // 2, 1)
    in_image = row_ids - pick_rows(onehot, first_merged)
    corner = (
        pick_rows(onehot, starts)
        + REG
        + 2 * (in_image // half_width) * row_width
        + 2 * (in_image % half_width)
    )
    offsets = jnp.stack(
        [jnp.zeros_like(row_width), jnp.ones_like(row_width), row_width, row_width + 1], axis=1
    )
    sources = jnp.where(is_valid[:, None], corner[:, None] + offsets, 0)
    return (sources, is_valid)


def attend(query_rows, query_seg, key_rows, value_rows, key_seg):
    scores = lax.dot_general(
        query_rows, key_rows, (((1,), (1,)), ((), ())), preferred_element_type=jnp.float32
    ) * HEAD_DIM ** (-0.5)
    scores = jnp.where(query_seg[:, None] == key_seg[None, :], scores, -jnp.inf)
    shifted = jnp.exp(scores - jnp.max(scores, axis=1, keepdims=True))
    weights = (shifted / jnp.sum(shifted, axis=1, keepdims=True)).astype(jnp.bfloat16)
    return jnp.dot(weights, value_rows, preferred_element_type=jnp.float32).astype(jnp.bfloat16)


def owner_ranks(owner_row):
    rows = owner_row.shape[0]
    same = owner_row[:, None] == owner_row[None, :]
    earlier = jnp.arange(rows)[None, :] < jnp.arange(rows)[:, None]
    return jnp.sum((same & earlier).astype(jnp.int32), axis=1)


def chip_shift(v, along, step, side):
    perm = []
    for src in range(side * side):
        x, y = src // side, src % side
        if along == 0:
            dst = ((x + step) % side) * side + y
        else:
            dst = x * side + (y + step) % side
        perm.append((src, dst))
    return lax.ppermute(v, "xy", perm)


def ring4(piece, along, side, cut):
    from_left = chip_shift(piece, along, 1, side)
    from_right = chip_shift(piece, along, -1, side)
    size = piece.shape[cut] // 2
    far_a = chip_shift(lax.slice_in_dim(from_left, 0, size, axis=cut), along, 1, side)
    far_b = chip_shift(lax.slice_in_dim(from_right, size, 2 * size, axis=cut), along, -1, side)
    far = jnp.concatenate([far_a, far_b], axis=cut)
    return jnp.stack([piece, from_right, far, from_left], axis=0)


def gather_torus(v, side, cut):
    size = v.shape[cut] // 2
    a = lax.slice_in_dim(v, 0, size, axis=cut)
    b = lax.slice_in_dim(v, size, 2 * size, axis=cut)
    a_l, a_r, a_f = (chip_shift(a, 0, k, side) for k in (1, -1, 2))
    b_l, b_r, b_f = (chip_shift(b, 1, k, side) for k in (1, -1, 2))
    a_l, a_r, a_f, b_l, b_r, b_f = lax.optimization_barrier((a_l, a_r, a_f, b_l, b_r, b_f))
    row_x = jnp.stack([a, a_r, a_f, a_l], axis=0)
    col_y = jnp.stack([b, b_r, b_f, b_l], axis=0)
    ra_l, ra_r = chip_shift(row_x, 1, 1, side), chip_shift(row_x, 1, -1, side)
    cb_l, cb_r = chip_shift(col_y, 0, 1, side), chip_shift(col_y, 0, -1, side)
    ra_l, ra_r, cb_l, cb_r = lax.optimization_barrier((ra_l, ra_r, cb_l, cb_r))
    ra_f = jnp.concatenate(
        [chip_shift(ra_l[:2], 1, 1, side), chip_shift(ra_r[2:], 1, -1, side)], axis=0
    )
    cb_f = jnp.concatenate(
        [chip_shift(cb_l[:2], 0, 1, side), chip_shift(cb_r[2:], 0, -1, side)], axis=0
    )
    ra_f, cb_f = lax.optimization_barrier((ra_f, cb_f))
    first_all = jnp.swapaxes(jnp.stack([row_x, ra_r, ra_f, ra_l], axis=0), 0, 1)
    second_all = jnp.stack([col_y, cb_r, cb_f, cb_l], axis=0)
    return jnp.concatenate([first_all, second_all], axis=cut + 2)


def send_bf16(v, along, step, side):
    return chip_shift(v.astype(jnp.bfloat16), along, step, side).astype(jnp.float32)


def ring_reduce(q, along, side):
    size = q.shape[-1] // 2
    from_left = send_bf16(q[2][..., :size], along, 1, side)
    from_right = send_bf16(q[2][..., size:], along, -1, side)
    to_right = jnp.concatenate([q[1][..., :size] + from_left, q[1][..., size:]], axis=-1)
    to_left = jnp.concatenate([q[3][..., :size], q[3][..., size:] + from_right], axis=-1)
    return q[0] + send_bf16(to_right, along, 1, side) + send_bf16(to_left, along, -1, side)


def direct_reduce(q, along, side):
    return (
        q[0]
        + send_bf16(q[1], along, 1, side)
        + send_bf16(q[3], along, -1, side)
        + send_bf16(q[2], along, 2, side)
    )


def reduce_torus(s_rel, side):
    size = s_rel.shape[-1] // 2
    first = jnp.swapaxes(s_rel[..., :size], 0, 1)
    second = s_rel[..., size:]
    first_sum = direct_reduce(ring_reduce(first, 1, side), 0, side)
    second_sum = direct_reduce(ring_reduce(second, 0, side), 1, side)
    return jnp.concatenate([first_sum, second_sum], axis=-1)


def swap_core(v):
    return lax.ppermute(v, "core", [(0, 1), (1, 0)])


def to_absolute(v, cx, cy):
    return jnp.roll(jnp.roll(v, cx, axis=0), cy, axis=1)


def to_relative(v, cx, cy):
    return jnp.roll(jnp.roll(v, -cx, axis=0), -cy, axis=1)


def local(
    tokens, ln_gain, ln_bias, w_qkv, w_out, layer_scale, w_merge, segment_ids, grid_sizes, owners
):
    chips = lax.axis_size("xy")
    side = 4
    batch_count = lax.axis_size("dp")
    chip = lax.axis_index("xy")
    core = lax.axis_index("core")
    cx = chip // side
    cy = chip % side
    seg_row = segment_ids[0]
    grid_row = grid_sizes[0]
    owner_row = owners[0, :, 0]
    seq_len = seg_row.shape[0]
    block = tokens.shape[1]
    model_width = tokens.shape[2]
    col_width = layer_scale.shape[0]
    half_rows = chips * block
    merged_rows = seq_len // 4
    tensor_count = 2 * chips
    own_cap = 4
    out_width = w_merge.shape[2]

    x_rel = gather_torus(tokens[0], side, 1)
    w_partner = swap_core(w_qkv)
    wo_partner = swap_core(w_out)
    ls_partner = swap_core(layer_scale)

    offs = jnp.arange(side, dtype=jnp.int32)
    chip_of = ((cx + offs)[:, None] % side) * side + (cy + offs)[None, :] % side
    within = jnp.arange(block, dtype=jnp.int32)
    pos_mine = ((2 * chip_of + core)[:, :, None] * block + within).reshape(half_rows)
    pos_other = ((2 * chip_of + 1 - core)[:, :, None] * block + within).reshape(half_rows)
    seg_cores = seg_row.reshape(side, side, 2, block)
    seg_mine = to_relative(seg_cores[:, :, core], cx, cy).reshape(half_rows)
    seg_other = to_relative(seg_cores[:, :, 1 - core], cx, cy).reshape(half_rows)
    cos_t, sin_t = rope_tables(seg_mine, pos_mine, grid_row)

    x_rows = x_rel.reshape(half_rows, model_width)
    normed = layer_norm(x_rows, ln_gain, ln_bias)
    w_both = jnp.stack([w_qkv, w_partner], axis=2)
    qkv_weight = w_both.reshape(model_width, 3 * 2 * HEAD_DIM)
    product = jnp.dot(normed, qkv_weight, preferred_element_type=jnp.float32).reshape(
        half_rows, 3, 2, HEAD_DIM
    )
    cos_rows = cos_t[:, None, :]
    sin_rows = sin_t[:, None, :]
    q_here = rotate(product[:, 0], cos_rows, sin_rows).astype(jnp.bfloat16)
    k_here = rotate(product[:, 1], cos_rows, sin_rows).astype(jnp.bfloat16)
    v_here = product[:, 2].astype(jnp.bfloat16)
    kv_here = jnp.stack([k_here, v_here], axis=1)
    kv_other = swap_core(kv_here)[:, :, ::-1]
    kv_all = jnp.concatenate([kv_here, kv_other], axis=0)
    key_all = kv_all[:, 0]
    value_all = kv_all[:, 1]
    seg_keys = jnp.concatenate([seg_mine, seg_other], axis=0)

    def one_head(h):
        return attend(q_here[:, h], seg_mine, key_all[:, h], value_all[:, h], seg_keys)

    context_rel = jnp.stack([one_head(0), one_head(1)], axis=1).reshape(
        side, side, block, 2 * HEAD_DIM
    )
    context_abs = to_absolute(context_rel, cx, cy).reshape(half_rows, 2 * HEAD_DIM)
    context_g = gather_torus(context_abs, side, 0)
    context = jnp.transpose(context_g, (2, 0, 1, 3)).reshape(half_rows, model_width)
    wo_both = jnp.concatenate([w_out, wo_partner], axis=1).reshape(
        side, side, 2, HEAD_DIM, 2 * col_width
    )
    wo_rel = to_relative(wo_both, cx, cy)
    wo_rel = jnp.where(core == 0, wo_rel, wo_rel[:, :, ::-1])
    wo_rows = wo_rel.reshape(model_width, 2 * col_width)
    mixed = jnp.dot(context, wo_rows, preferred_element_type=jnp.float32)
    group_mine = 2 * chip + core
    group_other = 2 * chip + 1 - core
    x_mine = lax.dynamic_slice_in_dim(x_rel, group_mine * col_width, col_width, 3)
    x_other = lax.dynamic_slice_in_dim(x_rel, group_other * col_width, col_width, 3)
    x_cols = to_absolute(jnp.concatenate([x_mine, x_other], axis=3), cx, cy).reshape(
        half_rows, 2 * col_width
    )
    ls_both = jnp.concatenate([layer_scale, ls_partner], axis=0)
    hidden_here = (x_cols.astype(jnp.float32) + ls_both * mixed).astype(jnp.bfloat16)
    hidden_recv = swap_core(hidden_here[:, col_width:])
    hidden = jnp.concatenate([hidden_here[:, :col_width], hidden_recv], axis=0)

    sources, is_valid = merge_sources(grid_row, merged_rows)
    src_block = sources // block
    src_index = (
        (src_block % 2 != core).astype(jnp.int32) * half_rows
        + (src_block // 2) * block
        + sources % block
    )
    merged = jnp.where(
        is_valid[:, None, None], hidden[src_index], jnp.zeros((), jnp.bfloat16)
    ).reshape(merged_rows, 4 * col_width)
    merge_weight = w_merge.reshape(4 * col_width, out_width)
    ranks = owner_ranks(owner_row)
    owner_dp = owner_row // tensor_count
    owner_t = owner_row % tensor_count
    slot_keys = owner_t * (batch_count * own_cap) + owner_dp * own_cap + ranks
    slot_ids = jnp.arange(tensor_count * batch_count * own_cap, dtype=jnp.int32).reshape(
        chips, 2, batch_count * own_cap
    )

    def project_slots(ids):
        placing = (ids.reshape(-1)[:, None] == slot_keys[None, :]).astype(jnp.bfloat16)
        by_owner = jnp.dot(placing, merged, preferred_element_type=jnp.float32).astype(
            jnp.bfloat16
        )
        return jnp.dot(by_owner, merge_weight, preferred_element_type=jnp.float32).astype(
            jnp.bfloat16
        )

    part_send = project_slots(jnp.where(core == 0, slot_ids[:, 1], slot_ids[:, 0]))
    part_recv = swap_core(part_send)
    part_keep = project_slots(jnp.where(core == 0, slot_ids[:, 0], slot_ids[:, 1]))
    part_chip = part_keep.astype(jnp.float32) + part_recv.astype(jnp.float32)
    s_rel = to_relative(
        part_chip.reshape(side, side, batch_count * own_cap, out_width), cx, cy
    )
    mine = reduce_torus(s_rel, side)
    outgoing = mine.astype(jnp.bfloat16).reshape(batch_count, own_cap, out_width)
    plane = lax.axis_index("dp")
    out_rel = jnp.roll(outgoing, -plane, axis=0)
    recv = [out_rel[0]]
    for step in range(1, batch_count):
        perm = [(d, (d + step) % batch_count) for d in range(batch_count)]
        recv.append(lax.ppermute(out_rel[step], "dp", perm))
    incoming = jnp.roll(jnp.stack(recv, axis=0)[::-1], plane + 1, axis=0)
    return incoming.reshape(1, batch_count * own_cap, out_width)


def solution(mesh):
    devices = mesh.devices.reshape(mesh.shape["dp"], -1, 2)
    mesh3 = Mesh(devices, ("dp", "xy", "core"))
    tp = ("xy", "core")
    in_specs = (
        P("dp", tp, None),
        P(),
        P(),
        P(None, None, tp),
        P(None, tp),
        P(tp),
        P(None, tp, None),
        P("dp", None),
        P("dp", None, None),
        P("dp", None, None),
    )
    out_specs = P("dp", tp, None)
    return jax.shard_map(local, mesh=mesh3, in_specs=in_specs, out_specs=out_specs, check_vma=False)
```

```python
import jax
import jax.numpy as jnp
from jax import lax
from jax.sharding import Mesh
from jax.sharding import PartitionSpec as P

HEAD_DIM = 128
IMGS = 3
REG = 5


norm_eps = 1e-06


def layer_norm(row_data, gain_vec, shift_vec):
    values = row_data.astype(jnp.float32)
    center = values - jnp.mean(values, axis=-1, keepdims=True)
    spread = jnp.mean(center * center, axis=-1, keepdims=True)
    return (center * lax.rsqrt(spread + norm_eps) * gain_vec + shift_vec).astype(jnp.bfloat16)


def image_layout(grid_row):
    heights = grid_row[:, 0]
    widths = grid_row[:, 1]
    lengths = REG + heights * widths
    starts = jnp.cumsum(lengths) - lengths
    counts = heights // 2 * (widths // 2)
    merged_end = jnp.cumsum(counts)
    return (heights, widths, starts, merged_end - counts, merged_end)


def pick_rows(onehot, lookup):
    return jnp.sum(onehot * lookup[None, :], axis=1)


def rope_tables(seg_at, position, grid_row):
    heights, widths, starts, first_merged, last_merged = image_layout(grid_row)
    image_ids = jnp.arange(IMGS, dtype=jnp.int32)
    onehot = (seg_at[:, None] == image_ids[None, :]).astype(jnp.int32)
    is_image = jnp.sum(onehot, axis=1) > 0
    in_image = position - pick_rows(onehot, starts) - REG
    is_patch = is_image & (in_image >= 0)
    row_width = jnp.maximum(pick_rows(onehot, widths), 1)
    col_height = jnp.maximum(pick_rows(onehot, heights), 1)
    clipped = jnp.maximum(in_image, 0)
    coord_y = (
        2.0 * ((clipped // row_width).astype(jnp.float32) + 0.5) / col_height.astype(jnp.float32)
        - 1.0
    )
    coord_x = (
        2.0 * ((clipped % row_width).astype(jnp.float32) + 0.5) / row_width.astype(jnp.float32)
        - 1.0
    )
    quarter = HEAD_DIM // 4
    pair_ids = jnp.arange(HEAD_DIM // 2, dtype=jnp.int32)
    omegas = 100.0 ** ((pair_ids % quarter).astype(jnp.float32) / quarter)
    coord_all = jnp.where(pair_ids[None, :] < quarter, coord_y[:, None], coord_x[:, None])
    angles = jnp.where(is_patch[:, None], jnp.pi * omegas[None, :] * coord_all, 0.0)
    return (jnp.cos(angles), jnp.sin(angles))


def rotate(values, cos_rows, sin_rows):
    half_dim = values.shape[-1] // 2
    first_half = values[..., :half_dim]
    second_half = values[..., half_dim:]
    return jnp.concatenate(
        [
            first_half * cos_rows - second_half * sin_rows,
            second_half * cos_rows + first_half * sin_rows,
        ],
        axis=-1,
    )


def merge_sources(grid_row, merged_rows):
    heights, widths, starts, first_merged, last_merged = image_layout(grid_row)
    row_ids = jnp.arange(merged_rows, dtype=jnp.int32)
    onehot = (
        (row_ids[:, None] >= first_merged[None, :]) & (row_ids[:, None] < last_merged[None, :])
    ).astype(jnp.int32)
    is_valid = jnp.sum(onehot, axis=1) > 0
    row_width = pick_rows(onehot, widths)
    half_width = jnp.maximum(row_width // 2, 1)
    in_image = row_ids - pick_rows(onehot, first_merged)
    corner = (
        pick_rows(onehot, starts)
        + REG
        + 2 * (in_image // half_width) * row_width
        + 2 * (in_image % half_width)
    )
    offsets = jnp.stack(
        [jnp.zeros_like(row_width), jnp.ones_like(row_width), row_width, row_width + 1], axis=1
    )
    sources = jnp.where(is_valid[:, None], corner[:, None] + offsets, 0)
    return (sources, is_valid)


def attend(query_rows, query_seg, key_rows, value_rows, key_seg):
    scores = lax.dot_general(
        query_rows, key_rows, (((1,), (1,)), ((), ())), preferred_element_type=jnp.float32
    ) * HEAD_DIM ** (-0.5)
    scores = jnp.where(query_seg[:, None] == key_seg[None, :], scores, -jnp.inf)
    shifted = jnp.exp(scores - jnp.max(scores, axis=1, keepdims=True))
    weights = (shifted / jnp.sum(shifted, axis=1, keepdims=True)).astype(jnp.bfloat16)
    return jnp.dot(weights, value_rows, preferred_element_type=jnp.float32).astype(jnp.bfloat16)


def owner_ranks(owner_row):
    rows = owner_row.shape[0]
    same = owner_row[:, None] == owner_row[None, :]
    earlier = jnp.arange(rows)[None, :] < jnp.arange(rows)[:, None]
    return jnp.sum((same & earlier).astype(jnp.int32), axis=1)


def chip_shift(v, along, step, side):
    perm = []
    for src in range(side * side):
        x, y = src // side, src % side
        if along == 0:
            dst = ((x + step) % side) * side + y
        else:
            dst = x * side + (y + step) % side
        perm.append((src, dst))
    return lax.ppermute(v, "xy", perm)


def ring4(piece, along, side, cut):
    from_left = chip_shift(piece, along, 1, side)
    from_right = chip_shift(piece, along, -1, side)
    size = piece.shape[cut] // 2
    far_a = chip_shift(lax.slice_in_dim(from_left, 0, size, axis=cut), along, 1, side)
    far_b = chip_shift(lax.slice_in_dim(from_right, size, 2 * size, axis=cut), along, -1, side)
    far = jnp.concatenate([far_a, far_b], axis=cut)
    return jnp.stack([piece, from_right, far, from_left], axis=0)


def gather_torus(v, side, cut):
    size = v.shape[cut] // 2
    a = lax.slice_in_dim(v, 0, size, axis=cut)
    b = lax.slice_in_dim(v, size, 2 * size, axis=cut)
    a_l, a_r, a_f = (chip_shift(a, 0, k, side) for k in (1, -1, 2))
    b_l, b_r, b_f = (chip_shift(b, 1, k, side) for k in (1, -1, 2))
    row_x = jnp.stack([a, a_r, a_f, a_l], axis=0)
    col_y = jnp.stack([b, b_r, b_f, b_l], axis=0)
    ra_l, ra_r = chip_shift(row_x, 1, 1, side), chip_shift(row_x, 1, -1, side)
    cb_l, cb_r = chip_shift(col_y, 0, 1, side), chip_shift(col_y, 0, -1, side)
    ra_f = jnp.concatenate(
        [chip_shift(ra_l[:2], 1, 1, side), chip_shift(ra_r[2:], 1, -1, side)], axis=0
    )
    cb_f = jnp.concatenate(
        [chip_shift(cb_l[:2], 0, 1, side), chip_shift(cb_r[2:], 0, -1, side)], axis=0
    )
    first_all = jnp.swapaxes(jnp.stack([row_x, ra_r, ra_f, ra_l], axis=0), 0, 1)
    second_all = jnp.stack([col_y, cb_r, cb_f, cb_l], axis=0)
    return jnp.concatenate([first_all, second_all], axis=cut + 2)


def send_bf16(v, along, step, side):
    return chip_shift(v.astype(jnp.bfloat16), along, step, side).astype(jnp.float32)


def ring_reduce(q, along, side):
    size = q.shape[-1] // 2
    from_left = send_bf16(q[2][..., :size], along, 1, side)
    from_right = send_bf16(q[2][..., size:], along, -1, side)
    to_right = jnp.concatenate([q[1][..., :size] + from_left, q[1][..., size:]], axis=-1)
    to_left = jnp.concatenate([q[3][..., :size], q[3][..., size:] + from_right], axis=-1)
    return q[0] + send_bf16(to_right, along, 1, side) + send_bf16(to_left, along, -1, side)


def direct_reduce(q, along, side):
    return (
        q[0]
        + send_bf16(q[1], along, 1, side)
        + send_bf16(q[3], along, -1, side)
        + send_bf16(q[2], along, 2, side)
    )


def reduce_torus(s_rel, side):
    size = s_rel.shape[-1] // 2
    first = jnp.swapaxes(s_rel[..., :size], 0, 1)
    second = s_rel[..., size:]
    first_sum = direct_reduce(ring_reduce(first, 1, side), 0, side)
    second_sum = direct_reduce(ring_reduce(second, 0, side), 1, side)
    return jnp.concatenate([first_sum, second_sum], axis=-1)


def swap_core(v):
    return lax.ppermute(v, "core", [(0, 1), (1, 0)])


def to_absolute(v, cx, cy):
    return jnp.roll(jnp.roll(v, cx, axis=0), cy, axis=1)


def to_relative(v, cx, cy):
    return jnp.roll(jnp.roll(v, -cx, axis=0), -cy, axis=1)


def local(
    tokens, ln_gain, ln_bias, w_qkv, w_out, layer_scale, w_merge, segment_ids, grid_sizes, owners
):
    chips = lax.axis_size("xy")
    side = 4
    batch_count = lax.axis_size("dp")
    chip = lax.axis_index("xy")
    core = lax.axis_index("core")
    cx = chip // side
    cy = chip % side
    seg_row = segment_ids[0]
    grid_row = grid_sizes[0]
    owner_row = owners[0, :, 0]
    seq_len = seg_row.shape[0]
    block = tokens.shape[1]
    model_width = tokens.shape[2]
    col_width = layer_scale.shape[0]
    half_rows = chips * block
    merged_rows = seq_len // 4
    tensor_count = 2 * chips
    own_cap = 4
    out_width = w_merge.shape[2]

    x_rel = gather_torus(tokens[0], side, 1)
    w_partner = swap_core(w_qkv)
    wo_partner = swap_core(w_out)
    ls_partner = swap_core(layer_scale)

    offs = jnp.arange(side, dtype=jnp.int32)
    chip_of = ((cx + offs)[:, None] % side) * side + (cy + offs)[None, :] % side
    within = jnp.arange(block, dtype=jnp.int32)
    pos_mine = ((2 * chip_of + core)[:, :, None] * block + within).reshape(half_rows)
    pos_other = ((2 * chip_of + 1 - core)[:, :, None] * block + within).reshape(half_rows)
    seg_cores = seg_row.reshape(side, side, 2, block)
    seg_mine = to_relative(seg_cores[:, :, core], cx, cy).reshape(half_rows)
    seg_other = to_relative(seg_cores[:, :, 1 - core], cx, cy).reshape(half_rows)
    cos_t, sin_t = rope_tables(seg_mine, pos_mine, grid_row)

    x_rows = x_rel.reshape(half_rows, model_width)
    normed = layer_norm(x_rows, ln_gain, ln_bias)
    w_both = jnp.stack([w_qkv, w_partner], axis=2)
    qkv_weight = w_both.reshape(model_width, 3 * 2 * HEAD_DIM)
    product = jnp.dot(normed, qkv_weight, preferred_element_type=jnp.float32).reshape(
        half_rows, 3, 2, HEAD_DIM
    )
    cos_rows = cos_t[:, None, :]
    sin_rows = sin_t[:, None, :]
    q_here = rotate(product[:, 0], cos_rows, sin_rows).astype(jnp.bfloat16)
    k_here = rotate(product[:, 1], cos_rows, sin_rows).astype(jnp.bfloat16)
    v_here = product[:, 2].astype(jnp.bfloat16)
    kv_here = jnp.stack([k_here, v_here], axis=1)
    kv_other = swap_core(kv_here)[:, :, ::-1]
    kv_all = jnp.concatenate([kv_here, kv_other], axis=0)
    key_all = kv_all[:, 0]
    value_all = kv_all[:, 1]
    seg_keys = jnp.concatenate([seg_mine, seg_other], axis=0)

    def one_head(h):
        return attend(q_here[:, h], seg_mine, key_all[:, h], value_all[:, h], seg_keys)

    context_rel = jnp.stack([one_head(0), one_head(1)], axis=1).reshape(
        side, side, block, 2 * HEAD_DIM
    )
    context_abs = to_absolute(context_rel, cx, cy).reshape(half_rows, 2 * HEAD_DIM)
    context_g = gather_torus(context_abs, side, 0)
    context = jnp.transpose(context_g, (2, 0, 1, 3)).reshape(half_rows, model_width)
    wo_both = jnp.concatenate([w_out, wo_partner], axis=1).reshape(
        side, side, 2, HEAD_DIM, 2 * col_width
    )
    wo_rel = to_relative(wo_both, cx, cy)
    wo_rel = jnp.where(core == 0, wo_rel, wo_rel[:, :, ::-1])
    wo_rows = wo_rel.reshape(model_width, 2 * col_width)
    mixed = jnp.dot(context, wo_rows, preferred_element_type=jnp.float32)
    group_mine = 2 * chip + core
    group_other = 2 * chip + 1 - core
    x_mine = lax.dynamic_slice_in_dim(x_rel, group_mine * col_width, col_width, 3)
    x_other = lax.dynamic_slice_in_dim(x_rel, group_other * col_width, col_width, 3)
    x_cols = to_absolute(jnp.concatenate([x_mine, x_other], axis=3), cx, cy).reshape(
        half_rows, 2 * col_width
    )
    ls_both = jnp.concatenate([layer_scale, ls_partner], axis=0)
    hidden_here = (x_cols.astype(jnp.float32) + ls_both * mixed).astype(jnp.bfloat16)
    hidden_recv = swap_core(hidden_here[:, col_width:])
    hidden = jnp.concatenate([hidden_here[:, :col_width], hidden_recv], axis=0)

    sources, is_valid = merge_sources(grid_row, merged_rows)
    src_block = sources // block
    src_index = (
        (src_block % 2 != core).astype(jnp.int32) * half_rows
        + (src_block // 2) * block
        + sources % block
    )
    merged = jnp.where(
        is_valid[:, None, None], hidden[src_index], jnp.zeros((), jnp.bfloat16)
    ).reshape(merged_rows, 4 * col_width)
    merge_weight = w_merge.reshape(4 * col_width, out_width)
    ranks = owner_ranks(owner_row)
    owner_dp = owner_row // tensor_count
    owner_t = owner_row % tensor_count
    slot_keys = owner_t * (batch_count * own_cap) + owner_dp * own_cap + ranks
    slot_ids = jnp.arange(tensor_count * batch_count * own_cap, dtype=jnp.int32)
    placing = (slot_ids[:, None] == slot_keys[None, :]).astype(jnp.bfloat16)
    by_owner = jnp.dot(placing, merged, preferred_element_type=jnp.float32).astype(jnp.bfloat16)
    group_part = jnp.dot(by_owner, merge_weight, preferred_element_type=jnp.float32).astype(
        jnp.bfloat16
    )
    part16 = group_part.reshape(chips, 2, batch_count * own_cap, out_width)
    part_keep = jnp.where(core == 0, part16[:, 0], part16[:, 1])
    part_send = jnp.where(core == 0, part16[:, 1], part16[:, 0])
    part_chip = part_keep.astype(jnp.float32) + swap_core(part_send).astype(jnp.float32)
    s_rel = to_relative(
        part_chip.reshape(side, side, batch_count * own_cap, out_width), cx, cy
    )
    mine = reduce_torus(s_rel, side)
    outgoing = mine.astype(jnp.bfloat16).reshape(batch_count, own_cap, out_width)
    plane = lax.axis_index("dp")
    out_rel = jnp.roll(outgoing, -plane, axis=0)
    recv = [out_rel[0]]
    for step in range(1, batch_count):
        perm = [(d, (d + step) % batch_count) for d in range(batch_count)]
        recv.append(lax.ppermute(out_rel[step], "dp", perm))
    incoming = jnp.roll(jnp.stack(recv, axis=0)[::-1], plane + 1, axis=0)
    return incoming.reshape(1, batch_count * own_cap, out_width)


def solution(mesh):
    devices = mesh.devices.reshape(mesh.shape["dp"], -1, 2)
    mesh3 = Mesh(devices, ("dp", "xy", "core"))
    tp = ("xy", "core")
    in_specs = (
        P("dp", tp, None),
        P(),
        P(),
        P(None, None, tp),
        P(None, tp),
        P(tp),
        P(None, tp, None),
        P("dp", None),
        P("dp", None, None),
        P("dp", None, None),
    )
    out_specs = P("dp", tp, None)
    return jax.shard_map(local, mesh=mesh3, in_specs=in_specs, out_specs=out_specs, check_vma=False)
```

```python
import jax
import jax.numpy as jnp
from jax import lax
from jax.sharding import Mesh
from jax.sharding import PartitionSpec as P

HEAD_DIM = 128
IMGS = 3
REG = 5


norm_eps = 1e-06


def layer_norm(row_data, gain_vec, shift_vec):
    values = row_data.astype(jnp.float32)
    center = values - jnp.mean(values, axis=-1, keepdims=True)
    spread = jnp.mean(center * center, axis=-1, keepdims=True)
    return (center * lax.rsqrt(spread + norm_eps) * gain_vec + shift_vec).astype(jnp.bfloat16)


def image_layout(grid_row):
    heights = grid_row[:, 0]
    widths = grid_row[:, 1]
    lengths = REG + heights * widths
    starts = jnp.cumsum(lengths) - lengths
    counts = heights // 2 * (widths // 2)
    merged_end = jnp.cumsum(counts)
    return (heights, widths, starts, merged_end - counts, merged_end)


def pick_rows(onehot, lookup):
    return jnp.sum(onehot * lookup[None, :], axis=1)


def rope_tables(seg_at, position, grid_row):
    heights, widths, starts, first_merged, last_merged = image_layout(grid_row)
    image_ids = jnp.arange(IMGS, dtype=jnp.int32)
    onehot = (seg_at[:, None] == image_ids[None, :]).astype(jnp.int32)
    is_image = jnp.sum(onehot, axis=1) > 0
    in_image = position - pick_rows(onehot, starts) - REG
    is_patch = is_image & (in_image >= 0)
    row_width = jnp.maximum(pick_rows(onehot, widths), 1)
    col_height = jnp.maximum(pick_rows(onehot, heights), 1)
    clipped = jnp.maximum(in_image, 0)
    coord_y = (
        2.0 * ((clipped // row_width).astype(jnp.float32) + 0.5) / col_height.astype(jnp.float32)
        - 1.0
    )
    coord_x = (
        2.0 * ((clipped % row_width).astype(jnp.float32) + 0.5) / row_width.astype(jnp.float32)
        - 1.0
    )
    quarter = HEAD_DIM // 4
    pair_ids = jnp.arange(HEAD_DIM // 2, dtype=jnp.int32)
    omegas = 100.0 ** ((pair_ids % quarter).astype(jnp.float32) / quarter)
    coord_all = jnp.where(pair_ids[None, :] < quarter, coord_y[:, None], coord_x[:, None])
    angles = jnp.where(is_patch[:, None], jnp.pi * omegas[None, :] * coord_all, 0.0)
    return (jnp.cos(angles), jnp.sin(angles))


def rotate(values, cos_rows, sin_rows):
    half_dim = values.shape[-1] // 2
    first_half = values[..., :half_dim]
    second_half = values[..., half_dim:]
    return jnp.concatenate(
        [
            first_half * cos_rows - second_half * sin_rows,
            second_half * cos_rows + first_half * sin_rows,
        ],
        axis=-1,
    )


def merge_sources(grid_row, merged_rows):
    heights, widths, starts, first_merged, last_merged = image_layout(grid_row)
    row_ids = jnp.arange(merged_rows, dtype=jnp.int32)
    onehot = (
        (row_ids[:, None] >= first_merged[None, :]) & (row_ids[:, None] < last_merged[None, :])
    ).astype(jnp.int32)
    is_valid = jnp.sum(onehot, axis=1) > 0
    row_width = pick_rows(onehot, widths)
    half_width = jnp.maximum(row_width // 2, 1)
    in_image = row_ids - pick_rows(onehot, first_merged)
    corner = (
        pick_rows(onehot, starts)
        + REG
        + 2 * (in_image // half_width) * row_width
        + 2 * (in_image % half_width)
    )
    offsets = jnp.stack(
        [jnp.zeros_like(row_width), jnp.ones_like(row_width), row_width, row_width + 1], axis=1
    )
    sources = jnp.where(is_valid[:, None], corner[:, None] + offsets, 0)
    return (sources, is_valid)


def attend(query_rows, query_seg, key_rows, value_rows, key_seg):
    scores = lax.dot_general(
        query_rows, key_rows, (((1,), (1,)), ((), ())), preferred_element_type=jnp.float32
    ) * HEAD_DIM ** (-0.5)
    scores = jnp.where(query_seg[:, None] == key_seg[None, :], scores, -jnp.inf)
    shifted = jnp.exp(scores - jnp.max(scores, axis=1, keepdims=True))
    weights = (shifted / jnp.sum(shifted, axis=1, keepdims=True)).astype(jnp.bfloat16)
    return jnp.dot(weights, value_rows, preferred_element_type=jnp.float32).astype(jnp.bfloat16)


def owner_ranks(owner_row):
    rows = owner_row.shape[0]
    same = owner_row[:, None] == owner_row[None, :]
    earlier = jnp.arange(rows)[None, :] < jnp.arange(rows)[:, None]
    return jnp.sum((same & earlier).astype(jnp.int32), axis=1)


def chip_shift(v, along, step, side):
    perm = []
    for src in range(side * side):
        x, y = src // side, src % side
        if along == 0:
            dst = ((x + step) % side) * side + y
        else:
            dst = x * side + (y + step) % side
        perm.append((src, dst))
    return lax.ppermute(v, "xy", perm)


def ring4(piece, along, side, cut):
    from_left = chip_shift(piece, along, 1, side)
    from_right = chip_shift(piece, along, -1, side)
    size = piece.shape[cut] // 2
    far_a = chip_shift(lax.slice_in_dim(from_left, 0, size, axis=cut), along, 1, side)
    far_b = chip_shift(lax.slice_in_dim(from_right, size, 2 * size, axis=cut), along, -1, side)
    far = jnp.concatenate([far_a, far_b], axis=cut)
    return jnp.stack([piece, from_right, far, from_left], axis=0)


def gather_torus(v, side, cut):
    size = v.shape[cut] // 2
    a = lax.slice_in_dim(v, 0, size, axis=cut)
    b = lax.slice_in_dim(v, size, 2 * size, axis=cut)
    a_l, a_r, a_f = (chip_shift(a, 0, k, side) for k in (1, -1, 2))
    b_l, b_r, b_f = (chip_shift(b, 1, k, side) for k in (1, -1, 2))
    row_x = jnp.stack([a, a_r, a_f, a_l], axis=0)
    col_y = jnp.stack([b, b_r, b_f, b_l], axis=0)
    ra_l, ra_r = chip_shift(row_x, 1, 1, side), chip_shift(row_x, 1, -1, side)
    cb_l, cb_r = chip_shift(col_y, 0, 1, side), chip_shift(col_y, 0, -1, side)
    ra_f = jnp.concatenate(
        [chip_shift(ra_l[:2], 1, 1, side), chip_shift(ra_r[2:], 1, -1, side)], axis=0
    )
    cb_f = jnp.concatenate(
        [chip_shift(cb_l[:2], 0, 1, side), chip_shift(cb_r[2:], 0, -1, side)], axis=0
    )
    first_all = jnp.swapaxes(jnp.stack([row_x, ra_r, ra_f, ra_l], axis=0), 0, 1)
    second_all = jnp.stack([col_y, cb_r, cb_f, cb_l], axis=0)
    return jnp.concatenate([first_all, second_all], axis=cut + 2)


def send_bf16(v, along, step, side):
    return chip_shift(v.astype(jnp.bfloat16), along, step, side).astype(jnp.float32)


def ring_reduce(q, along, side):
    size = q.shape[-1] // 2
    from_left = send_bf16(q[2][..., :size], along, 1, side)
    from_right = send_bf16(q[2][..., size:], along, -1, side)
    to_right = jnp.concatenate([q[1][..., :size] + from_left, q[1][..., size:]], axis=-1)
    to_left = jnp.concatenate([q[3][..., :size], q[3][..., size:] + from_right], axis=-1)
    return q[0] + send_bf16(to_right, along, 1, side) + send_bf16(to_left, along, -1, side)


def direct_reduce(q, along, side):
    return (
        q[0]
        + send_bf16(q[1], along, 1, side)
        + send_bf16(q[3], along, -1, side)
        + send_bf16(q[2], along, 2, side)
    )


def reduce_torus(s_rel, side):
    size = s_rel.shape[-1] // 2
    first = jnp.swapaxes(s_rel[..., :size], 0, 1)
    second = s_rel[..., size:]
    first_sum = direct_reduce(ring_reduce(first, 1, side), 0, side)
    second_sum = direct_reduce(ring_reduce(second, 0, side), 1, side)
    return jnp.concatenate([first_sum, second_sum], axis=-1)


def swap_core(v):
    return lax.ppermute(v, "core", [(0, 1), (1, 0)])


def to_absolute(v, cx, cy):
    return jnp.roll(jnp.roll(v, cx, axis=0), cy, axis=1)


def to_relative(v, cx, cy):
    return jnp.roll(jnp.roll(v, -cx, axis=0), -cy, axis=1)


def local(
    tokens, ln_gain, ln_bias, w_qkv, w_out, layer_scale, w_merge, segment_ids, grid_sizes, owners
):
    chips = lax.axis_size("xy")
    side = 4
    batch_count = lax.axis_size("dp")
    chip = lax.axis_index("xy")
    core = lax.axis_index("core")
    cx = chip // side
    cy = chip % side
    seg_row = segment_ids[0]
    grid_row = grid_sizes[0]
    owner_row = owners[0, :, 0]
    seq_len = seg_row.shape[0]
    block = tokens.shape[1]
    model_width = tokens.shape[2]
    col_width = layer_scale.shape[0]
    half_rows = chips * block
    merged_rows = seq_len // 4
    tensor_count = 2 * chips
    own_cap = 4
    out_width = w_merge.shape[2]

    x_rel = gather_torus(tokens[0], side, 1)
    w_partner = swap_core(w_qkv)
    wo_partner = swap_core(w_out)
    ls_partner = swap_core(layer_scale)

    offs = jnp.arange(side, dtype=jnp.int32)
    chip_of = ((cx + offs)[:, None] % side) * side + (cy + offs)[None, :] % side
    within = jnp.arange(block, dtype=jnp.int32)
    pos_mine = ((2 * chip_of + core)[:, :, None] * block + within).reshape(half_rows)
    pos_other = ((2 * chip_of + 1 - core)[:, :, None] * block + within).reshape(half_rows)
    seg_cores = seg_row.reshape(side, side, 2, block)
    seg_mine = to_relative(seg_cores[:, :, core], cx, cy).reshape(half_rows)
    seg_other = to_relative(seg_cores[:, :, 1 - core], cx, cy).reshape(half_rows)
    cos_t, sin_t = rope_tables(seg_mine, pos_mine, grid_row)

    x_rows = x_rel.reshape(half_rows, model_width)
    normed = layer_norm(x_rows, ln_gain, ln_bias)
    w_both = jnp.stack([w_qkv, w_partner], axis=2)
    qkv_weight = w_both.reshape(model_width, 3 * 2 * HEAD_DIM)
    product = jnp.dot(normed, qkv_weight, preferred_element_type=jnp.float32).reshape(
        half_rows, 3, 2, HEAD_DIM
    )
    cos_rows = cos_t[:, None, :]
    sin_rows = sin_t[:, None, :]
    q_here = rotate(product[:, 0], cos_rows, sin_rows).astype(jnp.bfloat16)
    k_here = rotate(product[:, 1], cos_rows, sin_rows).astype(jnp.bfloat16)
    v_here = product[:, 2].astype(jnp.bfloat16)
    kv_here = jnp.stack([k_here, v_here], axis=1)
    kv_other = swap_core(kv_here)[:, :, ::-1]
    kv_all = jnp.concatenate([kv_here, kv_other], axis=0)
    key_all = kv_all[:, 0]
    value_all = kv_all[:, 1]
    seg_keys = jnp.concatenate([seg_mine, seg_other], axis=0)

    def one_head(h):
        return attend(q_here[:, h], seg_mine, key_all[:, h], value_all[:, h], seg_keys)

    context_rel = jnp.stack([one_head(0), one_head(1)], axis=1).reshape(
        side, side, block, 2 * HEAD_DIM
    )
    context_abs = to_absolute(context_rel, cx, cy).reshape(half_rows, 2 * HEAD_DIM)
    context_g = gather_torus(context_abs, side, 0)
    context = jnp.transpose(context_g, (2, 0, 1, 3)).reshape(half_rows, model_width)
    wo_both = jnp.concatenate([w_out, wo_partner], axis=1).reshape(
        side, side, 2, HEAD_DIM, 2 * col_width
    )
    wo_rel = to_relative(wo_both, cx, cy)
    wo_rel = jnp.where(core == 0, wo_rel, wo_rel[:, :, ::-1])
    wo_rows = wo_rel.reshape(model_width, 2 * col_width)
    mixed = jnp.dot(context, wo_rows, preferred_element_type=jnp.float32)
    group_mine = 2 * chip + core
    group_other = 2 * chip + 1 - core
    x_mine = lax.dynamic_slice_in_dim(x_rel, group_mine * col_width, col_width, 3)
    x_other = lax.dynamic_slice_in_dim(x_rel, group_other * col_width, col_width, 3)
    x_cols = to_absolute(jnp.concatenate([x_mine, x_other], axis=3), cx, cy).reshape(
        half_rows, 2 * col_width
    )
    ls_both = jnp.concatenate([layer_scale, ls_partner], axis=0)
    hidden_here = (x_cols.astype(jnp.float32) + ls_both * mixed).astype(jnp.bfloat16)
    hidden_recv = swap_core(hidden_here[:, col_width:])
    hidden = jnp.concatenate([hidden_here[:, :col_width], hidden_recv], axis=0)

    sources, is_valid = merge_sources(grid_row, merged_rows)
    src_block = sources // block
    src_index = (
        (src_block % 2 != core).astype(jnp.int32) * half_rows
        + (src_block // 2) * block
        + sources % block
    )
    merged = jnp.where(
        is_valid[:, None, None], hidden[src_index], jnp.zeros((), jnp.bfloat16)
    ).reshape(merged_rows, 4 * col_width)
    merge_weight = w_merge.reshape(4 * col_width, out_width)
    ranks = owner_ranks(owner_row)
    owner_dp = owner_row // tensor_count
    owner_t = owner_row % tensor_count
    owner_chip = owner_t // 2
    owner_rel = ((owner_chip // side - cx) % side) * side + (owner_chip % side - cy) % side
    slot_keys = (owner_rel * 2 + owner_t % 2) * (batch_count * own_cap) + owner_dp * own_cap + ranks
    slot_ids = jnp.arange(tensor_count * batch_count * own_cap, dtype=jnp.int32)
    placing = (slot_ids[:, None] == slot_keys[None, :]).astype(jnp.bfloat16)
    by_owner = jnp.dot(placing, merged, preferred_element_type=jnp.float32).astype(jnp.bfloat16)
    group_part = jnp.dot(by_owner, merge_weight, preferred_element_type=jnp.float32).astype(
        jnp.bfloat16
    )
    part16 = group_part.reshape(chips, 2, batch_count * own_cap, out_width)
    part_keep = jnp.where(core == 0, part16[:, 0], part16[:, 1])
    part_send = jnp.where(core == 0, part16[:, 1], part16[:, 0])
    part_chip = part_keep.astype(jnp.float32) + swap_core(part_send).astype(jnp.float32)
    s_rel = part_chip.reshape(side, side, batch_count * own_cap, out_width)
    mine = reduce_torus(s_rel, side)
    outgoing = mine.astype(jnp.bfloat16).reshape(batch_count, own_cap, out_width)
    plane = lax.axis_index("dp")
    out_rel = jnp.roll(outgoing, -plane, axis=0)
    recv = [out_rel[0]]
    for step in range(1, batch_count):
        perm = [(d, (d + step) % batch_count) for d in range(batch_count)]
        recv.append(lax.ppermute(out_rel[step], "dp", perm))
    incoming = jnp.roll(jnp.stack(recv, axis=0)[::-1], plane + 1, axis=0)
    return incoming.reshape(1, batch_count * own_cap, out_width)


def solution(mesh):
    devices = mesh.devices.reshape(mesh.shape["dp"], -1, 2)
    mesh3 = Mesh(devices, ("dp", "xy", "core"))
    tp = ("xy", "core")
    in_specs = (
        P("dp", tp, None),
        P(),
        P(),
        P(None, None, tp),
        P(None, tp),
        P(tp),
        P(None, tp, None),
        P("dp", None),
        P("dp", None, None),
        P("dp", None, None),
    )
    out_specs = P("dp", tp, None)
    return jax.shard_map(local, mesh=mesh3, in_specs=in_specs, out_specs=out_specs, check_vma=False)
```

```python
import jax
import jax.numpy as jnp
from jax import lax
from jax.sharding import Mesh
from jax.sharding import PartitionSpec as P

HEAD_DIM = 128
IMGS = 3
REG = 5


norm_eps = 1e-06


def layer_norm(row_data, gain_vec, shift_vec):
    values = row_data.astype(jnp.float32)
    center = values - jnp.mean(values, axis=-1, keepdims=True)
    spread = jnp.mean(center * center, axis=-1, keepdims=True)
    return (center * lax.rsqrt(spread + norm_eps) * gain_vec + shift_vec).astype(jnp.bfloat16)


def image_layout(grid_row):
    heights = grid_row[:, 0]
    widths = grid_row[:, 1]
    lengths = REG + heights * widths
    starts = jnp.cumsum(lengths) - lengths
    counts = heights // 2 * (widths // 2)
    merged_end = jnp.cumsum(counts)
    return (heights, widths, starts, merged_end - counts, merged_end)


def pick_rows(onehot, lookup):
    return jnp.sum(onehot * lookup[None, :], axis=1)


def rope_tables(seg_at, position, grid_row):
    heights, widths, starts, first_merged, last_merged = image_layout(grid_row)
    image_ids = jnp.arange(IMGS, dtype=jnp.int32)
    onehot = (seg_at[:, None] == image_ids[None, :]).astype(jnp.int32)
    is_image = jnp.sum(onehot, axis=1) > 0
    in_image = position - pick_rows(onehot, starts) - REG
    is_patch = is_image & (in_image >= 0)
    row_width = jnp.maximum(pick_rows(onehot, widths), 1)
    col_height = jnp.maximum(pick_rows(onehot, heights), 1)
    clipped = jnp.maximum(in_image, 0)
    coord_y = (
        2.0 * ((clipped // row_width).astype(jnp.float32) + 0.5) / col_height.astype(jnp.float32)
        - 1.0
    )
    coord_x = (
        2.0 * ((clipped % row_width).astype(jnp.float32) + 0.5) / row_width.astype(jnp.float32)
        - 1.0
    )
    quarter = HEAD_DIM // 4
    pair_ids = jnp.arange(HEAD_DIM // 2, dtype=jnp.int32)
    omegas = 100.0 ** ((pair_ids % quarter).astype(jnp.float32) / quarter)
    coord_all = jnp.where(pair_ids[None, :] < quarter, coord_y[:, None], coord_x[:, None])
    angles = jnp.where(is_patch[:, None], jnp.pi * omegas[None, :] * coord_all, 0.0)
    return (jnp.cos(angles), jnp.sin(angles))


def rotate(values, cos_rows, sin_rows):
    half_dim = values.shape[-1] // 2
    first_half = values[..., :half_dim]
    second_half = values[..., half_dim:]
    return jnp.concatenate(
        [
            first_half * cos_rows - second_half * sin_rows,
            second_half * cos_rows + first_half * sin_rows,
        ],
        axis=-1,
    )


def merge_sources(grid_row, merged_rows):
    heights, widths, starts, first_merged, last_merged = image_layout(grid_row)
    row_ids = jnp.arange(merged_rows, dtype=jnp.int32)
    onehot = (
        (row_ids[:, None] >= first_merged[None, :]) & (row_ids[:, None] < last_merged[None, :])
    ).astype(jnp.int32)
    is_valid = jnp.sum(onehot, axis=1) > 0
    row_width = pick_rows(onehot, widths)
    half_width = jnp.maximum(row_width // 2, 1)
    in_image = row_ids - pick_rows(onehot, first_merged)
    corner = (
        pick_rows(onehot, starts)
        + REG
        + 2 * (in_image // half_width) * row_width
        + 2 * (in_image % half_width)
    )
    offsets = jnp.stack(
        [jnp.zeros_like(row_width), jnp.ones_like(row_width), row_width, row_width + 1], axis=1
    )
    sources = jnp.where(is_valid[:, None], corner[:, None] + offsets, 0)
    return (sources, is_valid)


def attend(query_rows, query_seg, key_rows, value_rows, key_seg):
    scores = lax.dot_general(
        query_rows, key_rows, (((1,), (1,)), ((), ())), preferred_element_type=jnp.float32
    ) * HEAD_DIM ** (-0.5)
    scores = jnp.where(query_seg[:, None] == key_seg[None, :], scores, -jnp.inf)
    shifted = jnp.exp(scores - jnp.max(scores, axis=1, keepdims=True))
    weights = (shifted / jnp.sum(shifted, axis=1, keepdims=True)).astype(jnp.bfloat16)
    return jnp.dot(weights, value_rows, preferred_element_type=jnp.float32).astype(jnp.bfloat16)


def owner_ranks(owner_row):
    rows = owner_row.shape[0]
    same = owner_row[:, None] == owner_row[None, :]
    earlier = jnp.arange(rows)[None, :] < jnp.arange(rows)[:, None]
    return jnp.sum((same & earlier).astype(jnp.int32), axis=1)


def chip_shift(v, along, step, side):
    perm = []
    for src in range(side * side):
        x, y = src // side, src % side
        if along == 0:
            dst = ((x + step) % side) * side + y
        else:
            dst = x * side + (y + step) % side
        perm.append((src, dst))
    return lax.ppermute(v, "xy", perm)


def ring4(piece, along, side, cut):
    from_left = chip_shift(piece, along, 1, side)
    from_right = chip_shift(piece, along, -1, side)
    size = piece.shape[cut] // 2
    far_a = chip_shift(lax.slice_in_dim(from_left, 0, size, axis=cut), along, 1, side)
    far_b = chip_shift(lax.slice_in_dim(from_right, size, 2 * size, axis=cut), along, -1, side)
    far = jnp.concatenate([far_a, far_b], axis=cut)
    return jnp.stack([piece, from_right, far, from_left], axis=0)


def gather_torus(v, side, cut):
    size = v.shape[cut] // 2
    a = lax.slice_in_dim(v, 0, size, axis=cut)
    b = lax.slice_in_dim(v, size, 2 * size, axis=cut)
    a_l, a_r, a_f = (chip_shift(a, 0, k, side) for k in (1, -1, 2))
    b_l, b_r, b_f = (chip_shift(b, 1, k, side) for k in (1, -1, 2))
    row_x = jnp.stack([a, a_r, a_f, a_l], axis=0)
    col_y = jnp.stack([b, b_r, b_f, b_l], axis=0)
    ra_l, ra_r = chip_shift(row_x, 1, 1, side), chip_shift(row_x, 1, -1, side)
    cb_l, cb_r = chip_shift(col_y, 0, 1, side), chip_shift(col_y, 0, -1, side)
    ra_f = jnp.concatenate(
        [chip_shift(ra_l[:2], 1, 1, side), chip_shift(ra_r[2:], 1, -1, side)], axis=0
    )
    cb_f = jnp.concatenate(
        [chip_shift(cb_l[:2], 0, 1, side), chip_shift(cb_r[2:], 0, -1, side)], axis=0
    )
    first_all = jnp.swapaxes(jnp.stack([row_x, ra_r, ra_f, ra_l], axis=0), 0, 1)
    second_all = jnp.stack([col_y, cb_r, cb_f, cb_l], axis=0)
    return jnp.concatenate([first_all, second_all], axis=cut + 2)


def send_bf16(v, along, step, side):
    return chip_shift(v.astype(jnp.bfloat16), along, step, side).astype(jnp.float32)


def ring_reduce(q, along, side):
    size = q.shape[-1] // 2
    from_left = send_bf16(q[2][..., :size], along, 1, side)
    from_right = send_bf16(q[2][..., size:], along, -1, side)
    to_right = jnp.concatenate([q[1][..., :size] + from_left, q[1][..., size:]], axis=-1)
    to_left = jnp.concatenate([q[3][..., :size], q[3][..., size:] + from_right], axis=-1)
    return q[0] + send_bf16(to_right, along, 1, side) + send_bf16(to_left, along, -1, side)


def direct_reduce(q, along, side):
    size = q.shape[-1] // 2
    far = jnp.concatenate(
        [send_bf16(q[2][..., :size], along, 2, side), send_bf16(q[2][..., size:], along, -2, side)],
        axis=-1,
    )
    return q[0] + send_bf16(q[1], along, 1, side) + send_bf16(q[3], along, -1, side) + far


def reduce_torus(s_rel, side):
    size = s_rel.shape[-1] // 2
    first = jnp.swapaxes(s_rel[..., :size], 0, 1)
    second = s_rel[..., size:]
    first_sum = direct_reduce(direct_reduce(first, 1, side), 0, side)
    second_sum = direct_reduce(direct_reduce(second, 0, side), 1, side)
    return jnp.concatenate([first_sum, second_sum], axis=-1)


def swap_core(v):
    return lax.ppermute(v, "core", [(0, 1), (1, 0)])


def to_absolute(v, cx, cy):
    return jnp.roll(jnp.roll(v, cx, axis=0), cy, axis=1)


def to_relative(v, cx, cy):
    return jnp.roll(jnp.roll(v, -cx, axis=0), -cy, axis=1)


def local(
    tokens, ln_gain, ln_bias, w_qkv, w_out, layer_scale, w_merge, segment_ids, grid_sizes, owners
):
    chips = lax.axis_size("xy")
    side = 4
    batch_count = lax.axis_size("dp")
    chip = lax.axis_index("xy")
    core = lax.axis_index("core")
    cx = chip // side
    cy = chip % side
    seg_row = segment_ids[0]
    grid_row = grid_sizes[0]
    owner_row = owners[0, :, 0]
    seq_len = seg_row.shape[0]
    block = tokens.shape[1]
    model_width = tokens.shape[2]
    col_width = layer_scale.shape[0]
    half_rows = chips * block
    merged_rows = seq_len // 4
    tensor_count = 2 * chips
    own_cap = 4
    out_width = w_merge.shape[2]

    x_rel = gather_torus(tokens[0], side, 1)
    w_partner = swap_core(w_qkv)
    wo_partner = swap_core(w_out)
    ls_partner = swap_core(layer_scale)

    offs = jnp.arange(side, dtype=jnp.int32)
    chip_of = ((cx + offs)[:, None] % side) * side + (cy + offs)[None, :] % side
    within = jnp.arange(block, dtype=jnp.int32)
    pos_mine = ((2 * chip_of + core)[:, :, None] * block + within).reshape(half_rows)
    pos_other = ((2 * chip_of + 1 - core)[:, :, None] * block + within).reshape(half_rows)
    seg_cores = seg_row.reshape(side, side, 2, block)
    seg_mine = to_relative(seg_cores[:, :, core], cx, cy).reshape(half_rows)
    seg_other = to_relative(seg_cores[:, :, 1 - core], cx, cy).reshape(half_rows)
    cos_t, sin_t = rope_tables(seg_mine, pos_mine, grid_row)

    x_rows = x_rel.reshape(half_rows, model_width)
    normed = layer_norm(x_rows, ln_gain, ln_bias)
    w_both = jnp.stack([w_qkv, w_partner], axis=2)
    qkv_weight = w_both.reshape(model_width, 3 * 2 * HEAD_DIM)
    product = jnp.dot(normed, qkv_weight, preferred_element_type=jnp.float32).reshape(
        half_rows, 3, 2, HEAD_DIM
    )
    cos_rows = cos_t[:, None, :]
    sin_rows = sin_t[:, None, :]
    q_here = rotate(product[:, 0], cos_rows, sin_rows).astype(jnp.bfloat16)
    k_here = rotate(product[:, 1], cos_rows, sin_rows).astype(jnp.bfloat16)
    v_here = product[:, 2].astype(jnp.bfloat16)
    kv_here = jnp.stack([k_here, v_here], axis=1)
    kv_other = swap_core(kv_here)[:, :, ::-1]
    kv_all = jnp.concatenate([kv_here, kv_other], axis=0)
    key_all = kv_all[:, 0]
    value_all = kv_all[:, 1]
    seg_keys = jnp.concatenate([seg_mine, seg_other], axis=0)

    def one_head(h):
        return attend(q_here[:, h], seg_mine, key_all[:, h], value_all[:, h], seg_keys)

    context_rel = jnp.stack([one_head(0), one_head(1)], axis=1).reshape(
        side, side, block, 2 * HEAD_DIM
    )
    context_abs = to_absolute(context_rel, cx, cy).reshape(half_rows, 2 * HEAD_DIM)
    context_g = gather_torus(context_abs, side, 0)
    context = jnp.transpose(context_g, (2, 0, 1, 3)).reshape(half_rows, model_width)
    wo_both = jnp.concatenate([w_out, wo_partner], axis=1).reshape(
        side, side, 2, HEAD_DIM, 2 * col_width
    )
    wo_rel = to_relative(wo_both, cx, cy)
    wo_rel = jnp.where(core == 0, wo_rel, wo_rel[:, :, ::-1])
    wo_rows = wo_rel.reshape(model_width, 2 * col_width)
    mixed = jnp.dot(context, wo_rows, preferred_element_type=jnp.float32)
    group_mine = 2 * chip + core
    group_other = 2 * chip + 1 - core
    x_mine = lax.dynamic_slice_in_dim(x_rel, group_mine * col_width, col_width, 3)
    x_other = lax.dynamic_slice_in_dim(x_rel, group_other * col_width, col_width, 3)
    x_cols = to_absolute(jnp.concatenate([x_mine, x_other], axis=3), cx, cy).reshape(
        half_rows, 2 * col_width
    )
    ls_both = jnp.concatenate([layer_scale, ls_partner], axis=0)
    hidden_here = (x_cols.astype(jnp.float32) + ls_both * mixed).astype(jnp.bfloat16)
    hidden_recv = swap_core(hidden_here[:, col_width:])
    hidden = jnp.concatenate([hidden_here[:, :col_width], hidden_recv], axis=0)

    sources, is_valid = merge_sources(grid_row, merged_rows)
    src_block = sources // block
    src_index = (
        (src_block % 2 != core).astype(jnp.int32) * half_rows
        + (src_block // 2) * block
        + sources % block
    )
    merged = jnp.where(
        is_valid[:, None, None], hidden[src_index], jnp.zeros((), jnp.bfloat16)
    ).reshape(merged_rows, 4 * col_width)
    merge_weight = w_merge.reshape(4 * col_width, out_width)
    ranks = owner_ranks(owner_row)
    owner_dp = owner_row // tensor_count
    owner_t = owner_row % tensor_count
    owner_chip = owner_t // 2
    owner_rel = ((owner_chip // side - cx) % side) * side + (owner_chip % side - cy) % side
    slot_keys = (owner_rel * 2 + owner_t % 2) * (batch_count * own_cap) + owner_dp * own_cap + ranks
    slot_ids = jnp.arange(tensor_count * batch_count * own_cap, dtype=jnp.int32)
    placing = (slot_ids[:, None] == slot_keys[None, :]).astype(jnp.bfloat16)
    by_owner = jnp.dot(placing, merged, preferred_element_type=jnp.float32).astype(jnp.bfloat16)
    group_part = jnp.dot(by_owner, merge_weight, preferred_element_type=jnp.float32).astype(
        jnp.bfloat16
    )
    part16 = group_part.reshape(chips, 2, batch_count * own_cap, out_width)
    part_keep = jnp.where(core == 0, part16[:, 0], part16[:, 1])
    part_send = jnp.where(core == 0, part16[:, 1], part16[:, 0])
    part_chip = part_keep.astype(jnp.float32) + swap_core(part_send).astype(jnp.float32)
    s_rel = part_chip.reshape(side, side, batch_count * own_cap, out_width)
    mine = reduce_torus(s_rel, side)
    outgoing = mine.astype(jnp.bfloat16).reshape(batch_count, own_cap, out_width)
    plane = lax.axis_index("dp")
    out_rel = jnp.roll(outgoing, -plane, axis=0)
    recv = [out_rel[0]]
    for step in range(1, batch_count):
        perm = [(d, (d + step) % batch_count) for d in range(batch_count)]
        recv.append(lax.ppermute(out_rel[step], "dp", perm))
    incoming = jnp.roll(jnp.stack(recv, axis=0)[::-1], plane + 1, axis=0)
    return incoming.reshape(1, batch_count * own_cap, out_width)


def solution(mesh):
    devices = mesh.devices.reshape(mesh.shape["dp"], -1, 2)
    mesh3 = Mesh(devices, ("dp", "xy", "core"))
    tp = ("xy", "core")
    in_specs = (
        P("dp", tp, None),
        P(),
        P(),
        P(None, None, tp),
        P(None, tp),
        P(tp),
        P(None, tp, None),
        P("dp", None),
        P("dp", None, None),
        P("dp", None, None),
    )
    out_specs = P("dp", tp, None)
    return jax.shard_map(local, mesh=mesh3, in_specs=in_specs, out_specs=out_specs, check_vma=False)
```

```python
import jax
import jax.numpy as jnp
from jax import lax
from jax.sharding import Mesh
from jax.sharding import PartitionSpec as P

HEAD_DIM = 128
IMGS = 3
REG = 5


norm_eps = 1e-06


def layer_norm(row_data, gain_vec, shift_vec):
    values = row_data.astype(jnp.float32)
    center = values - jnp.mean(values, axis=-1, keepdims=True)
    spread = jnp.mean(center * center, axis=-1, keepdims=True)
    return (center * lax.rsqrt(spread + norm_eps) * gain_vec + shift_vec).astype(jnp.bfloat16)


def image_layout(grid_row):
    heights = grid_row[:, 0]
    widths = grid_row[:, 1]
    lengths = REG + heights * widths
    starts = jnp.cumsum(lengths) - lengths
    counts = heights // 2 * (widths // 2)
    merged_end = jnp.cumsum(counts)
    return (heights, widths, starts, merged_end - counts, merged_end)


def pick_rows(onehot, lookup):
    return jnp.sum(onehot * lookup[None, :], axis=1)


def rope_tables(seg_at, position, grid_row):
    heights, widths, starts, first_merged, last_merged = image_layout(grid_row)
    image_ids = jnp.arange(IMGS, dtype=jnp.int32)
    onehot = (seg_at[:, None] == image_ids[None, :]).astype(jnp.int32)
    is_image = jnp.sum(onehot, axis=1) > 0
    in_image = position - pick_rows(onehot, starts) - REG
    is_patch = is_image & (in_image >= 0)
    row_width = jnp.maximum(pick_rows(onehot, widths), 1)
    col_height = jnp.maximum(pick_rows(onehot, heights), 1)
    clipped = jnp.maximum(in_image, 0)
    coord_y = (
        2.0 * ((clipped // row_width).astype(jnp.float32) + 0.5) / col_height.astype(jnp.float32)
        - 1.0
    )
    coord_x = (
        2.0 * ((clipped % row_width).astype(jnp.float32) + 0.5) / row_width.astype(jnp.float32)
        - 1.0
    )
    quarter = HEAD_DIM // 4
    pair_ids = jnp.arange(HEAD_DIM // 2, dtype=jnp.int32)
    omegas = 100.0 ** ((pair_ids % quarter).astype(jnp.float32) / quarter)
    coord_all = jnp.where(pair_ids[None, :] < quarter, coord_y[:, None], coord_x[:, None])
    angles = jnp.where(is_patch[:, None], jnp.pi * omegas[None, :] * coord_all, 0.0)
    return (jnp.cos(angles), jnp.sin(angles))


def rotate(values, cos_rows, sin_rows):
    half_dim = values.shape[-1] // 2
    first_half = values[..., :half_dim]
    second_half = values[..., half_dim:]
    return jnp.concatenate(
        [
            first_half * cos_rows - second_half * sin_rows,
            second_half * cos_rows + first_half * sin_rows,
        ],
        axis=-1,
    )


def merge_sources(grid_row, merged_rows):
    heights, widths, starts, first_merged, last_merged = image_layout(grid_row)
    row_ids = jnp.arange(merged_rows, dtype=jnp.int32)
    onehot = (
        (row_ids[:, None] >= first_merged[None, :]) & (row_ids[:, None] < last_merged[None, :])
    ).astype(jnp.int32)
    is_valid = jnp.sum(onehot, axis=1) > 0
    row_width = pick_rows(onehot, widths)
    half_width = jnp.maximum(row_width // 2, 1)
    in_image = row_ids - pick_rows(onehot, first_merged)
    corner = (
        pick_rows(onehot, starts)
        + REG
        + 2 * (in_image // half_width) * row_width
        + 2 * (in_image % half_width)
    )
    offsets = jnp.stack(
        [jnp.zeros_like(row_width), jnp.ones_like(row_width), row_width, row_width + 1], axis=1
    )
    sources = jnp.where(is_valid[:, None], corner[:, None] + offsets, 0)
    return (sources, is_valid)


def attend(query_rows, query_seg, key_rows, value_rows, key_seg):
    scores = lax.dot_general(
        query_rows, key_rows, (((1,), (1,)), ((), ())), preferred_element_type=jnp.float32
    ) * HEAD_DIM ** (-0.5)
    scores = jnp.where(query_seg[:, None] == key_seg[None, :], scores, -jnp.inf)
    shifted = jnp.exp(scores - jnp.max(scores, axis=1, keepdims=True))
    weights = (shifted / jnp.sum(shifted, axis=1, keepdims=True)).astype(jnp.bfloat16)
    return jnp.dot(weights, value_rows, preferred_element_type=jnp.float32).astype(jnp.bfloat16)


def owner_ranks(owner_row):
    rows = owner_row.shape[0]
    same = owner_row[:, None] == owner_row[None, :]
    earlier = jnp.arange(rows)[None, :] < jnp.arange(rows)[:, None]
    return jnp.sum((same & earlier).astype(jnp.int32), axis=1)


def chip_shift(v, along, step, side):
    perm = []
    for src in range(side * side):
        x, y = src // side, src % side
        if along == 0:
            dst = ((x + step) % side) * side + y
        else:
            dst = x * side + (y + step) % side
        perm.append((src, dst))
    return lax.ppermute(v, "xy", perm)


def ring4(piece, along, side, cut):
    from_left = chip_shift(piece, along, 1, side)
    from_right = chip_shift(piece, along, -1, side)
    size = piece.shape[cut] // 2
    far_a = chip_shift(lax.slice_in_dim(from_left, 0, size, axis=cut), along, 1, side)
    far_b = chip_shift(lax.slice_in_dim(from_right, size, 2 * size, axis=cut), along, -1, side)
    far = jnp.concatenate([far_a, far_b], axis=cut)
    return jnp.stack([piece, from_right, far, from_left], axis=0)


def gather_torus(v, side, cut):
    size = v.shape[cut] // 2
    a = lax.slice_in_dim(v, 0, size, axis=cut)
    b = lax.slice_in_dim(v, size, 2 * size, axis=cut)
    a_l, a_r, a_f = (chip_shift(a, 0, k, side) for k in (1, -1, 2))
    b_l, b_r, b_f = (chip_shift(b, 1, k, side) for k in (1, -1, 2))
    row_x = jnp.stack([a, a_r, a_f, a_l], axis=0)
    col_y = jnp.stack([b, b_r, b_f, b_l], axis=0)
    ra_l, ra_r = chip_shift(row_x, 1, 1, side), chip_shift(row_x, 1, -1, side)
    cb_l, cb_r = chip_shift(col_y, 0, 1, side), chip_shift(col_y, 0, -1, side)
    ra_f = jnp.concatenate(
        [chip_shift(ra_l[:2], 1, 1, side), chip_shift(ra_r[2:], 1, -1, side)], axis=0
    )
    cb_f = jnp.concatenate(
        [chip_shift(cb_l[:2], 0, 1, side), chip_shift(cb_r[2:], 0, -1, side)], axis=0
    )
    first_all = jnp.swapaxes(jnp.stack([row_x, ra_r, ra_f, ra_l], axis=0), 0, 1)
    second_all = jnp.stack([col_y, cb_r, cb_f, cb_l], axis=0)
    return jnp.concatenate([first_all, second_all], axis=cut + 2)


def send_bf16(v, along, step, side):
    return chip_shift(v.astype(jnp.bfloat16), along, step, side).astype(jnp.float32)


def ring_reduce(q, along, side):
    size = q.shape[-1] // 2
    from_left = send_bf16(q[2][..., :size], along, 1, side)
    from_right = send_bf16(q[2][..., size:], along, -1, side)
    to_right = jnp.concatenate([q[1][..., :size] + from_left, q[1][..., size:]], axis=-1)
    to_left = jnp.concatenate([q[3][..., :size], q[3][..., size:] + from_right], axis=-1)
    return q[0] + send_bf16(to_right, along, 1, side) + send_bf16(to_left, along, -1, side)


def direct_reduce(q, along, side):
    return (
        q[0]
        + send_bf16(q[1], along, 1, side)
        + send_bf16(q[3], along, -1, side)
        + send_bf16(q[2], along, 2, side)
    )


def reduce_torus(s_rel, side):
    size = s_rel.shape[-1] // 2
    first = jnp.swapaxes(s_rel[..., :size], 0, 1)
    second = s_rel[..., size:]
    first_sum = direct_reduce(ring_reduce(first, 1, side), 0, side)
    second_sum = direct_reduce(ring_reduce(second, 0, side), 1, side)
    return jnp.concatenate([first_sum, second_sum], axis=-1)


def swap_core(v):
    return lax.ppermute(v, "core", [(0, 1), (1, 0)])


def to_absolute(v, cx, cy):
    return jnp.roll(jnp.roll(v, cx, axis=0), cy, axis=1)


def to_relative(v, cx, cy):
    return jnp.roll(jnp.roll(v, -cx, axis=0), -cy, axis=1)


def local(
    tokens, ln_gain, ln_bias, w_qkv, w_out, layer_scale, w_merge, segment_ids, grid_sizes, owners
):
    chips = lax.axis_size("xy")
    side = 4
    batch_count = lax.axis_size("dp")
    chip = lax.axis_index("xy")
    core = lax.axis_index("core")
    cx = chip // side
    cy = chip % side
    seg_row = segment_ids[0]
    grid_row = grid_sizes[0]
    owner_row = owners[0, :, 0]
    seq_len = seg_row.shape[0]
    block = tokens.shape[1]
    model_width = tokens.shape[2]
    col_width = layer_scale.shape[0]
    half_rows = chips * block
    merged_rows = seq_len // 4
    tensor_count = 2 * chips
    own_cap = 4
    out_width = w_merge.shape[2]

    x_rel = gather_torus(tokens[0], side, 1)
    w_partner = swap_core(w_qkv)
    wo_partner = swap_core(w_out)
    ls_partner = swap_core(layer_scale)

    offs = jnp.arange(side, dtype=jnp.int32)
    chip_of = ((cx + offs)[:, None] % side) * side + (cy + offs)[None, :] % side
    within = jnp.arange(block, dtype=jnp.int32)
    pos_mine = ((2 * chip_of + core)[:, :, None] * block + within).reshape(half_rows)
    pos_other = ((2 * chip_of + 1 - core)[:, :, None] * block + within).reshape(half_rows)
    seg_cores = seg_row.reshape(side, side, 2, block)
    seg_mine = to_relative(seg_cores[:, :, core], cx, cy).reshape(half_rows)
    seg_other = to_relative(seg_cores[:, :, 1 - core], cx, cy).reshape(half_rows)
    cos_t, sin_t = rope_tables(seg_mine, pos_mine, grid_row)

    x_rows = x_rel.reshape(half_rows, model_width)
    normed = layer_norm(x_rows, ln_gain, ln_bias)
    w_both = jnp.stack([w_qkv, w_partner], axis=2)
    qkv_weight = w_both.reshape(model_width, 3 * 2 * HEAD_DIM)
    product = jnp.dot(normed, qkv_weight, preferred_element_type=jnp.float32).reshape(
        half_rows, 3, 2, HEAD_DIM
    )
    cos_rows = cos_t[:, None, :]
    sin_rows = sin_t[:, None, :]
    q_here = rotate(product[:, 0], cos_rows, sin_rows).astype(jnp.bfloat16)
    k_here = rotate(product[:, 1], cos_rows, sin_rows).astype(jnp.bfloat16)
    v_here = product[:, 2].astype(jnp.bfloat16)
    kv_here = jnp.stack([k_here, v_here], axis=1)
    kv_other = swap_core(kv_here)[:, :, ::-1]
    kv_all = jnp.concatenate([kv_here, kv_other], axis=0)
    key_all = kv_all[:, 0]
    value_all = kv_all[:, 1]
    seg_keys = jnp.concatenate([seg_mine, seg_other], axis=0)

    def one_head(h):
        return attend(q_here[:, h], seg_mine, key_all[:, h], value_all[:, h], seg_keys)

    context_rel = jnp.stack([one_head(0), one_head(1)], axis=1).reshape(
        side, side, block, 2 * HEAD_DIM
    )
    context_abs = to_absolute(context_rel, cx, cy).reshape(half_rows, 2 * HEAD_DIM)
    context_g = gather_torus(context_abs, side, 1)
    context = jnp.transpose(context_g, (2, 0, 1, 3)).reshape(half_rows, model_width)
    wo_both = jnp.concatenate([w_out, wo_partner], axis=1).reshape(
        side, side, 2, HEAD_DIM, 2 * col_width
    )
    wo_rel = to_relative(wo_both, cx, cy)
    wo_rel = jnp.where(core == 0, wo_rel, wo_rel[:, :, ::-1])
    wo_rows = wo_rel.reshape(model_width, 2 * col_width)
    mixed = jnp.dot(context, wo_rows, preferred_element_type=jnp.float32)
    group_mine = 2 * chip + core
    group_other = 2 * chip + 1 - core
    x_mine = lax.dynamic_slice_in_dim(x_rel, group_mine * col_width, col_width, 3)
    x_other = lax.dynamic_slice_in_dim(x_rel, group_other * col_width, col_width, 3)
    x_cols = to_absolute(jnp.concatenate([x_mine, x_other], axis=3), cx, cy).reshape(
        half_rows, 2 * col_width
    )
    ls_both = jnp.concatenate([layer_scale, ls_partner], axis=0)
    hidden_here = (x_cols.astype(jnp.float32) + ls_both * mixed).astype(jnp.bfloat16)
    hidden_recv = swap_core(hidden_here[:, col_width:])
    hidden = jnp.concatenate([hidden_here[:, :col_width], hidden_recv], axis=0)

    sources, is_valid = merge_sources(grid_row, merged_rows)
    src_block = sources // block
    src_index = (
        (src_block % 2 != core).astype(jnp.int32) * half_rows
        + (src_block // 2) * block
        + sources % block
    )
    merged = jnp.where(
        is_valid[:, None, None], hidden[src_index], jnp.zeros((), jnp.bfloat16)
    ).reshape(merged_rows, 4 * col_width)
    merge_weight = w_merge.reshape(4 * col_width, out_width)
    ranks = owner_ranks(owner_row)
    owner_dp = owner_row // tensor_count
    owner_t = owner_row % tensor_count
    owner_chip = owner_t // 2
    owner_rel = ((owner_chip // side - cx) % side) * side + (owner_chip % side - cy) % side
    slot_keys = (owner_rel * 2 + owner_t % 2) * (batch_count * own_cap) + owner_dp * own_cap + ranks
    slot_ids = jnp.arange(tensor_count * batch_count * own_cap, dtype=jnp.int32)
    placing = (slot_ids[:, None] == slot_keys[None, :]).astype(jnp.bfloat16)
    by_owner = jnp.dot(placing, merged, preferred_element_type=jnp.float32).astype(jnp.bfloat16)
    group_part = jnp.dot(by_owner, merge_weight, preferred_element_type=jnp.float32).astype(
        jnp.bfloat16
    )
    part16 = group_part.reshape(chips, 2, batch_count * own_cap, out_width)
    part_keep = jnp.where(core == 0, part16[:, 0], part16[:, 1])
    part_send = jnp.where(core == 0, part16[:, 1], part16[:, 0])
    part_chip = part_keep.astype(jnp.float32) + swap_core(part_send).astype(jnp.float32)
    s_rel = part_chip.reshape(side, side, batch_count * own_cap, out_width)
    mine = reduce_torus(s_rel, side)
    outgoing = mine.astype(jnp.bfloat16).reshape(batch_count, own_cap, out_width)
    plane = lax.axis_index("dp")
    out_rel = jnp.roll(outgoing, -plane, axis=0)
    recv = [out_rel[0]]
    for step in range(1, batch_count):
        perm = [(d, (d + step) % batch_count) for d in range(batch_count)]
        recv.append(lax.ppermute(out_rel[step], "dp", perm))
    incoming = jnp.roll(jnp.stack(recv, axis=0)[::-1], plane + 1, axis=0)
    return incoming.reshape(1, batch_count * own_cap, out_width)


def solution(mesh):
    devices = mesh.devices.reshape(mesh.shape["dp"], -1, 2)
    mesh3 = Mesh(devices, ("dp", "xy", "core"))
    tp = ("xy", "core")
    in_specs = (
        P("dp", tp, None),
        P(),
        P(),
        P(None, None, tp),
        P(None, tp),
        P(tp),
        P(None, tp, None),
        P("dp", None),
        P("dp", None, None),
        P("dp", None, None),
    )
    out_specs = P("dp", tp, None)
    return jax.shard_map(local, mesh=mesh3, in_specs=in_specs, out_specs=out_specs, check_vma=False)
```

```python
import jax
import jax.numpy as jnp
from jax import lax
from jax.sharding import Mesh
from jax.sharding import PartitionSpec as P

HEAD_DIM = 128
IMGS = 3
REG = 5


norm_eps = 1e-06


def layer_norm(row_data, gain_vec, shift_vec):
    values = row_data.astype(jnp.float32)
    center = values - jnp.mean(values, axis=-1, keepdims=True)
    spread = jnp.mean(center * center, axis=-1, keepdims=True)
    return (center * lax.rsqrt(spread + norm_eps) * gain_vec + shift_vec).astype(jnp.bfloat16)


def image_layout(grid_row):
    heights = grid_row[:, 0]
    widths = grid_row[:, 1]
    lengths = REG + heights * widths
    starts = jnp.cumsum(lengths) - lengths
    counts = heights // 2 * (widths // 2)
    merged_end = jnp.cumsum(counts)
    return (heights, widths, starts, merged_end - counts, merged_end)


def pick_rows(onehot, lookup):
    return jnp.sum(onehot * lookup[None, :], axis=1)


def rope_tables(seg_at, position, grid_row):
    heights, widths, starts, first_merged, last_merged = image_layout(grid_row)
    image_ids = jnp.arange(IMGS, dtype=jnp.int32)
    onehot = (seg_at[:, None] == image_ids[None, :]).astype(jnp.int32)
    is_image = jnp.sum(onehot, axis=1) > 0
    in_image = position - pick_rows(onehot, starts) - REG
    is_patch = is_image & (in_image >= 0)
    row_width = jnp.maximum(pick_rows(onehot, widths), 1)
    col_height = jnp.maximum(pick_rows(onehot, heights), 1)
    clipped = jnp.maximum(in_image, 0)
    coord_y = (
        2.0 * ((clipped // row_width).astype(jnp.float32) + 0.5) / col_height.astype(jnp.float32)
        - 1.0
    )
    coord_x = (
        2.0 * ((clipped % row_width).astype(jnp.float32) + 0.5) / row_width.astype(jnp.float32)
        - 1.0
    )
    quarter = HEAD_DIM // 4
    pair_ids = jnp.arange(HEAD_DIM // 2, dtype=jnp.int32)
    omegas = 100.0 ** ((pair_ids % quarter).astype(jnp.float32) / quarter)
    coord_all = jnp.where(pair_ids[None, :] < quarter, coord_y[:, None], coord_x[:, None])
    angles = jnp.where(is_patch[:, None], jnp.pi * omegas[None, :] * coord_all, 0.0)
    return (jnp.cos(angles), jnp.sin(angles))


def rotate(values, cos_rows, sin_rows):
    half_dim = values.shape[-1] // 2
    first_half = values[..., :half_dim]
    second_half = values[..., half_dim:]
    return jnp.concatenate(
        [
            first_half * cos_rows - second_half * sin_rows,
            second_half * cos_rows + first_half * sin_rows,
        ],
        axis=-1,
    )


def merge_sources(grid_row, merged_rows):
    heights, widths, starts, first_merged, last_merged = image_layout(grid_row)
    row_ids = jnp.arange(merged_rows, dtype=jnp.int32)
    onehot = (
        (row_ids[:, None] >= first_merged[None, :]) & (row_ids[:, None] < last_merged[None, :])
    ).astype(jnp.int32)
    is_valid = jnp.sum(onehot, axis=1) > 0
    row_width = pick_rows(onehot, widths)
    half_width = jnp.maximum(row_width // 2, 1)
    in_image = row_ids - pick_rows(onehot, first_merged)
    corner = (
        pick_rows(onehot, starts)
        + REG
        + 2 * (in_image // half_width) * row_width
        + 2 * (in_image % half_width)
    )
    offsets = jnp.stack(
        [jnp.zeros_like(row_width), jnp.ones_like(row_width), row_width, row_width + 1], axis=1
    )
    sources = jnp.where(is_valid[:, None], corner[:, None] + offsets, 0)
    return (sources, is_valid)


def attend(query_rows, query_seg, key_rows, value_rows, key_seg):
    scores = lax.dot_general(
        query_rows, key_rows, (((1,), (1,)), ((), ())), preferred_element_type=jnp.float32
    ) * HEAD_DIM ** (-0.5)
    scores = jnp.where(query_seg[:, None] == key_seg[None, :], scores, -jnp.inf)
    shifted = jnp.exp(scores - jnp.max(scores, axis=1, keepdims=True))
    weights = (shifted / jnp.sum(shifted, axis=1, keepdims=True)).astype(jnp.bfloat16)
    return jnp.dot(weights, value_rows, preferred_element_type=jnp.float32).astype(jnp.bfloat16)


def owner_ranks(owner_row):
    rows = owner_row.shape[0]
    same = owner_row[:, None] == owner_row[None, :]
    earlier = jnp.arange(rows)[None, :] < jnp.arange(rows)[:, None]
    return jnp.sum((same & earlier).astype(jnp.int32), axis=1)


def chip_shift(v, along, step, side):
    perm = []
    for src in range(side * side):
        x, y = src // side, src % side
        if along == 0:
            dst = ((x + step) % side) * side + y
        else:
            dst = x * side + (y + step) % side
        perm.append((src, dst))
    return lax.ppermute(v, "xy", perm)


def ring4(piece, along, side, cut):
    from_left = chip_shift(piece, along, 1, side)
    from_right = chip_shift(piece, along, -1, side)
    size = piece.shape[cut] // 2
    far_a = chip_shift(lax.slice_in_dim(from_left, 0, size, axis=cut), along, 1, side)
    far_b = chip_shift(lax.slice_in_dim(from_right, size, 2 * size, axis=cut), along, -1, side)
    far = jnp.concatenate([far_a, far_b], axis=cut)
    return jnp.stack([piece, from_right, far, from_left], axis=0)


def gather_torus(v, side, cut):
    size = v.shape[cut] // 2
    a = lax.slice_in_dim(v, 0, size, axis=cut)
    b = lax.slice_in_dim(v, size, 2 * size, axis=cut)
    a_l, a_r = chip_shift(a, 0, 1, side), chip_shift(a, 0, -1, side)
    b_l, b_r = chip_shift(b, 1, 1, side), chip_shift(b, 1, -1, side)
    part = size // 2
    a_f = jnp.concatenate(
        [
            chip_shift(lax.slice_in_dim(a, 0, part, axis=cut), 0, 2, side),
            chip_shift(lax.slice_in_dim(a, part, size, axis=cut), 0, -2, side),
        ],
        axis=cut,
    )
    b_f = jnp.concatenate(
        [
            chip_shift(lax.slice_in_dim(b, 0, part, axis=cut), 1, 2, side),
            chip_shift(lax.slice_in_dim(b, part, size, axis=cut), 1, -2, side),
        ],
        axis=cut,
    )
    row_x = jnp.stack([a, a_r, a_f, a_l], axis=0)
    col_y = jnp.stack([b, b_r, b_f, b_l], axis=0)
    ra_l, ra_r = chip_shift(row_x, 1, 1, side), chip_shift(row_x, 1, -1, side)
    cb_l, cb_r = chip_shift(col_y, 0, 1, side), chip_shift(col_y, 0, -1, side)
    ra_f = jnp.concatenate(
        [chip_shift(ra_l[:2], 1, 1, side), chip_shift(ra_r[2:], 1, -1, side)], axis=0
    )
    cb_f = jnp.concatenate(
        [chip_shift(cb_l[:2], 0, 1, side), chip_shift(cb_r[2:], 0, -1, side)], axis=0
    )
    first_all = jnp.swapaxes(jnp.stack([row_x, ra_r, ra_f, ra_l], axis=0), 0, 1)
    second_all = jnp.stack([col_y, cb_r, cb_f, cb_l], axis=0)
    return jnp.concatenate([first_all, second_all], axis=cut + 2)


def send_bf16(v, along, step, side):
    return chip_shift(v.astype(jnp.bfloat16), along, step, side).astype(jnp.float32)


def ring_reduce(q, along, side):
    size = q.shape[-1] // 2
    from_left = send_bf16(q[2][..., :size], along, 1, side)
    from_right = send_bf16(q[2][..., size:], along, -1, side)
    to_right = jnp.concatenate([q[1][..., :size] + from_left, q[1][..., size:]], axis=-1)
    to_left = jnp.concatenate([q[3][..., :size], q[3][..., size:] + from_right], axis=-1)
    return q[0] + send_bf16(to_right, along, 1, side) + send_bf16(to_left, along, -1, side)


def direct_reduce(q, along, side):
    return (
        q[0]
        + send_bf16(q[1], along, 1, side)
        + send_bf16(q[3], along, -1, side)
        + send_bf16(q[2], along, 2, side)
    )


def reduce_torus(s_rel, side):
    size = s_rel.shape[-1] // 2
    first = jnp.swapaxes(s_rel[..., :size], 0, 1)
    second = s_rel[..., size:]
    first_sum = direct_reduce(ring_reduce(first, 1, side), 0, side)
    second_sum = direct_reduce(ring_reduce(second, 0, side), 1, side)
    return jnp.concatenate([first_sum, second_sum], axis=-1)


def swap_core(v):
    return lax.ppermute(v, "core", [(0, 1), (1, 0)])


def to_absolute(v, cx, cy):
    return jnp.roll(jnp.roll(v, cx, axis=0), cy, axis=1)


def to_relative(v, cx, cy):
    return jnp.roll(jnp.roll(v, -cx, axis=0), -cy, axis=1)


def local(
    tokens, ln_gain, ln_bias, w_qkv, w_out, layer_scale, w_merge, segment_ids, grid_sizes, owners
):
    chips = lax.axis_size("xy")
    side = 4
    batch_count = lax.axis_size("dp")
    chip = lax.axis_index("xy")
    core = lax.axis_index("core")
    cx = chip // side
    cy = chip % side
    seg_row = segment_ids[0]
    grid_row = grid_sizes[0]
    owner_row = owners[0, :, 0]
    seq_len = seg_row.shape[0]
    block = tokens.shape[1]
    model_width = tokens.shape[2]
    col_width = layer_scale.shape[0]
    half_rows = chips * block
    merged_rows = seq_len // 4
    tensor_count = 2 * chips
    own_cap = 4
    out_width = w_merge.shape[2]

    x_rel = gather_torus(tokens[0], side, 1)
    w_partner = swap_core(w_qkv)
    wo_partner = swap_core(w_out)
    ls_partner = swap_core(layer_scale)

    offs = jnp.arange(side, dtype=jnp.int32)
    chip_of = ((cx + offs)[:, None] % side) * side + (cy + offs)[None, :] % side
    within = jnp.arange(block, dtype=jnp.int32)
    pos_mine = ((2 * chip_of + core)[:, :, None] * block + within).reshape(half_rows)
    pos_other = ((2 * chip_of + 1 - core)[:, :, None] * block + within).reshape(half_rows)
    seg_cores = seg_row.reshape(side, side, 2, block)
    seg_mine = to_relative(seg_cores[:, :, core], cx, cy).reshape(half_rows)
    seg_other = to_relative(seg_cores[:, :, 1 - core], cx, cy).reshape(half_rows)
    cos_t, sin_t = rope_tables(seg_mine, pos_mine, grid_row)

    x_rows = x_rel.reshape(half_rows, model_width)
    normed = layer_norm(x_rows, ln_gain, ln_bias)
    w_both = jnp.stack([w_qkv, w_partner], axis=2)
    qkv_weight = w_both.reshape(model_width, 3 * 2 * HEAD_DIM)
    product = jnp.dot(normed, qkv_weight, preferred_element_type=jnp.float32).reshape(
        half_rows, 3, 2, HEAD_DIM
    )
    cos_rows = cos_t[:, None, :]
    sin_rows = sin_t[:, None, :]
    q_here = rotate(product[:, 0], cos_rows, sin_rows).astype(jnp.bfloat16)
    k_here = rotate(product[:, 1], cos_rows, sin_rows).astype(jnp.bfloat16)
    v_here = product[:, 2].astype(jnp.bfloat16)
    kv_here = jnp.stack([k_here, v_here], axis=1)
    kv_other = swap_core(kv_here)[:, :, ::-1]
    kv_all = jnp.concatenate([kv_here, kv_other], axis=0)
    key_all = kv_all[:, 0]
    value_all = kv_all[:, 1]
    seg_keys = jnp.concatenate([seg_mine, seg_other], axis=0)

    def one_head(h):
        return attend(q_here[:, h], seg_mine, key_all[:, h], value_all[:, h], seg_keys)

    context_rel = jnp.stack([one_head(0), one_head(1)], axis=1).reshape(
        side, side, block, 2 * HEAD_DIM
    )
    context_abs = to_absolute(context_rel, cx, cy).reshape(half_rows, 2 * HEAD_DIM)
    context_g = gather_torus(context_abs, side, 0)
    context = jnp.transpose(context_g, (2, 0, 1, 3)).reshape(half_rows, model_width)
    wo_both = jnp.concatenate([w_out, wo_partner], axis=1).reshape(
        side, side, 2, HEAD_DIM, 2 * col_width
    )
    wo_rel = to_relative(wo_both, cx, cy)
    wo_rel = jnp.where(core == 0, wo_rel, wo_rel[:, :, ::-1])
    wo_rows = wo_rel.reshape(model_width, 2 * col_width)
    mixed = jnp.dot(context, wo_rows, preferred_element_type=jnp.float32)
    group_mine = 2 * chip + core
    group_other = 2 * chip + 1 - core
    x_mine = lax.dynamic_slice_in_dim(x_rel, group_mine * col_width, col_width, 3)
    x_other = lax.dynamic_slice_in_dim(x_rel, group_other * col_width, col_width, 3)
    x_cols = to_absolute(jnp.concatenate([x_mine, x_other], axis=3), cx, cy).reshape(
        half_rows, 2 * col_width
    )
    ls_both = jnp.concatenate([layer_scale, ls_partner], axis=0)
    hidden_here = (x_cols.astype(jnp.float32) + ls_both * mixed).astype(jnp.bfloat16)
    hidden_recv = swap_core(hidden_here[:, col_width:])
    hidden = jnp.concatenate([hidden_here[:, :col_width], hidden_recv], axis=0)

    sources, is_valid = merge_sources(grid_row, merged_rows)
    src_block = sources // block
    src_index = (
        (src_block % 2 != core).astype(jnp.int32) * half_rows
        + (src_block // 2) * block
        + sources % block
    )
    merged = jnp.where(
        is_valid[:, None, None], hidden[src_index], jnp.zeros((), jnp.bfloat16)
    ).reshape(merged_rows, 4 * col_width)
    merge_weight = w_merge.reshape(4 * col_width, out_width)
    ranks = owner_ranks(owner_row)
    owner_dp = owner_row // tensor_count
    owner_t = owner_row % tensor_count
    owner_chip = owner_t // 2
    owner_rel = ((owner_chip // side - cx) % side) * side + (owner_chip % side - cy) % side
    slot_keys = (owner_rel * 2 + owner_t % 2) * (batch_count * own_cap) + owner_dp * own_cap + ranks
    slot_ids = jnp.arange(tensor_count * batch_count * own_cap, dtype=jnp.int32)
    placing = (slot_ids[:, None] == slot_keys[None, :]).astype(jnp.bfloat16)
    by_owner = jnp.dot(placing, merged, preferred_element_type=jnp.float32).astype(jnp.bfloat16)
    group_part = jnp.dot(by_owner, merge_weight, preferred_element_type=jnp.float32).astype(
        jnp.bfloat16
    )
    part16 = group_part.reshape(chips, 2, batch_count * own_cap, out_width)
    part_keep = jnp.where(core == 0, part16[:, 0], part16[:, 1])
    part_send = jnp.where(core == 0, part16[:, 1], part16[:, 0])
    part_chip = part_keep.astype(jnp.float32) + swap_core(part_send).astype(jnp.float32)
    s_rel = part_chip.reshape(side, side, batch_count * own_cap, out_width)
    mine = reduce_torus(s_rel, side)
    outgoing = mine.astype(jnp.bfloat16).reshape(batch_count, own_cap, out_width)
    plane = lax.axis_index("dp")
    out_rel = jnp.roll(outgoing, -plane, axis=0)
    recv = [out_rel[0]]
    for step in range(1, batch_count):
        perm = [(d, (d + step) % batch_count) for d in range(batch_count)]
        recv.append(lax.ppermute(out_rel[step], "dp", perm))
    incoming = jnp.roll(jnp.stack(recv, axis=0)[::-1], plane + 1, axis=0)
    return incoming.reshape(1, batch_count * own_cap, out_width)


def solution(mesh):
    devices = mesh.devices.reshape(mesh.shape["dp"], -1, 2)
    mesh3 = Mesh(devices, ("dp", "xy", "core"))
    tp = ("xy", "core")
    in_specs = (
        P("dp", tp, None),
        P(),
        P(),
        P(None, None, tp),
        P(None, tp),
        P(tp),
        P(None, tp, None),
        P("dp", None),
        P("dp", None, None),
        P("dp", None, None),
    )
    out_specs = P("dp", tp, None)
    return jax.shard_map(local, mesh=mesh3, in_specs=in_specs, out_specs=out_specs, check_vma=False)
```
